128 devices in a mesh: slab: 32 (over z, y, x_lo), px: 2 (over x_hi), py: 2 (over core).
Axes of the slice: x: 4 (x_hi: 2, x_lo: 2; x = x_hi * 2 + x_lo), y: 4, z: 4, core: 2. Of those that a mesh axis runs over, the one named last changes fastest.
Arguments:
- source: float32 [128, 4, 256, 256], P('slab', None, 'px', 'py'), may hold values from -6 to 6
- phase: float32 [128, 256, 256], P('slab', 'px', 'py'), may hold values from 0.3 to 2.8
- attenuation: float32 [128, 256, 256], P('slab', 'px', 'py'), may hold values from 0.00078125 to 0.08
- pml_level: int32 [256, 256], P('px', 'py'), may hold values from 0 to 3
- recv_values: float32 [2, 2, 4, 16384], P('px', 'py', None, 'slab'), may hold values from -8 to 8
- recv_slab: int32 [2, 2, 16384, 1], P('px', 'py', 'slab'), may hold values from 0 to 31; in each aligned block of 512 rows (0 to 511, 512 to 1023, ..., all dimensions but the last counted through in order) at most 64 rows name the same one
- recv_lateral: int32 [2, 2, 16384], P('px', 'py', 'slab'), may hold values from 0 to 16383
- recv_layer: int32 [2, 2, 16384], P('px', 'py', 'slab'), may hold values from 0 to 3
Outputs:
- correction: float32 [128, 4, 256, 256], P('slab', None, 'px', 'py')
The draws below stay inside these ranges and needn't reach their ends.
Inputs may be any that keep to these rules, and one draw needn't show every extreme that they name: `recv_slab`: among the rows of one device, at most 64 receivers name the same slab, a bound that some block reaches of them.
All inputs are finite; a program needn't handle non-finite values.
Results may differ from the reference program's by a relative error of at most 0.000034.
Values sent between devices are 32-bit elements; how exact they have to be, the bound alone decides.
No kernel may reach another device: no remote copies, remote signals or barrier semaphores. Data moves between devices by JAX's collectives and lax.ppermute only.
A program may use at most 128 MiB of HBM per device.

```python
import math
import jax
import jax.numpy as jnp
import numpy as np
from jax import lax

CX = 128
CY = 128
CZ = 4
SHOTS = 2
RECV_DEV = 512
COMP = 4
CAP = 64
RECV = 16384
NX = 256
NY = 256
NZ = 128
N_SLAB = 32
N_PX = 2
N_PY = 2


def place_ends(drawn, rng, smallest, top_value):
    longest = drawn.shape.index(max(drawn.shape))
    spots = []
    for shift in (0, 1):
        where = [jax.random.randint(jax.random.fold_in(rng, axis), (), 0, length) for axis, length in enumerate(drawn.shape)]
        where[longest] = (where[longest] + shift) % drawn.shape[longest]
        spots.append(tuple(where))
    return drawn.at[spots[0]].set(smallest).at[spots[1]].set(top_value)


def block_scale(stream_key, shape, cuts, low, high):
    loudness = 1.0
    for axis_at, blocks in cuts:
        steps = jax.random.uniform(jax.random.fold_in(jax.random.fold_in(stream_key, 6), axis_at), (blocks,), jnp.float32, low / len(cuts), high / len(cuts))
        loudness = loudness * jnp.repeat(jnp.exp(steps), shape[axis_at] // blocks).reshape((-1,) + (1,) * (len(shape) - 1 - axis_at))
    return loudness


def routed_block(rng, own, number, rows, number_of, top, limit, skew):
    ranking = jax.random.permutation(rng, number_of)
    crowded, ordinary = load_shares(number_of, rows * top, limit, skew, True), load_shares(number_of, rows * top, limit, skew, False)
    places = jnp.arange(number_of)

    def named(sizes, rotation):
        used = int((sizes > 0).sum())
        fixed = max(1, used // 4)
        shifted = fixed + (places - fixed + rotation * (used - fixed)) % max(1, number_of - fixed)
        return jnp.zeros((number_of,), jnp.int32).at[ranking[jnp.where(places < fixed, places, shifted)]].set(jnp.asarray(sizes, jnp.int32))

    sizes = jnp.where(number % 4 == 0, named(crowded, number // 4), named(ordinary, number - number // 4 - 1))
    mixed = jax.random.permutation(jax.random.fold_in(own, 3), number_of)
    donor, sink = mixed[0:number_of // 2 * 2:2], mixed[1:number_of // 2 * 2:2]
    room = jnp.minimum(sizes[donor] - 1, limit - sizes[sink]) // 2
    room = jnp.where((donor == ranking[0]) | (sink == ranking[0]) | (sizes[sink] == 0), 0, jnp.maximum(room, 0))
    shifted = jax.random.randint(jax.random.fold_in(own, 4), (number_of // 2,), 0, 1 << 20) % (room + 1)
    sizes = sizes.at[donor].add(-shifted).at[sink].add(shifted)
    labels = jnp.searchsorted(jnp.cumsum(sizes), jnp.arange(rows * top), side="right").astype(jnp.int32)
    listing = labels.reshape(top, rows).T
    listing = listing[jax.random.permutation(jax.random.fold_in(own, 1), rows)]
    rotation = jax.random.randint(jax.random.fold_in(own, 2), (rows, 1), 0, top)
    return jnp.take_along_axis(listing, (jnp.arange(top)[None, :] + rotation) % top, axis=1)


def load_shares(number_of, total, bound, lean, full):
    portions = [(1 << 20) // math.isqrt(grade ** lean) + 1 for grade in range(1, number_of + 1)]
    largest = bound if full else min(bound, max(-(-total // number_of), total * portions[0] // sum(portions)))
    least = 1 if total - largest >= number_of - 1 else 0
    given, spare = [largest] + [least] * (number_of - 1), total - largest - least * (number_of - 1)
    while spare > 0:
        movable = [i for i in range(1, number_of) if given[i] < largest] or [i for i in range(1, number_of) if given[i] < bound]
        mass, left = sum([portions[i] for i in movable]), spare
        for i in movable:
            extra = min(bound - given[i], max(1, left * portions[i] // mass), spare)
            given[i] = given[i] + extra
            spare = spare - extra
    return np.array(given)


def noise(rng, shape, scale, limit, pieces=(), kind=jnp.bfloat16):
    array = jax.random.normal(rng, shape, jnp.float32) * scale
    if len(pieces) > 0:
        array = block_scale(rng, shape, pieces, -0.22, 0.18) * array
    return jnp.clip(array, min=-limit, max=limit).astype(kind)


def setup_inputs(seed: int = 0) -> dict:
    streams_of = jax.random.split(jax.random.key(seed), 9)
    source = noise(streams_of[0], (NZ, COMP, NX, NY), 1.0, 6.0, ((0, 32), (2, 2), (3, 2)), jnp.float32)
    phase = jnp.clip(0.3 + 2.5 * jax.random.uniform(streams_of[1], (NZ, NX, NY), jnp.float32) ** block_scale(streams_of[1], (NZ, NX, NY), ((0, 32), (1, 2), (2, 2)), -0.2, 0.2), 0.3, 2.8)
    attenuation = jnp.clip(jnp.exp(math.log(0.08) - 4.6288867 * jax.random.uniform(streams_of[2], (NZ, NX, NY), jnp.float32) ** block_scale(streams_of[2], (NZ, NX, NY), ((0, 32), (1, 2), (2, 2)), -0.2, 0.2)), 0.00078125, 0.08)
    pml_level = place_ends(jax.random.randint(streams_of[3], (NX, NY), 0, 4), jax.random.fold_in(streams_of[3], 1), 0, 3).astype(jnp.int32)
    recv_values = noise(streams_of[4], (N_PX, N_PY, COMP, RECV), 2.0, 8.0, ((0, 2), (1, 2), (3, 32)), jnp.float32)
    recv_slab_keys = jax.random.split(jax.random.fold_in(streams_of[5], 1), N_PX * N_PY * RECV // RECV_DEV)
    recv_slab_turns = jax.random.permutation(jax.random.fold_in(streams_of[5], 3), N_PX * N_PY * RECV // RECV_DEV)
    recv_slab = jax.vmap(lambda own, number: routed_block(jax.random.fold_in(streams_of[5], 2), own, number, RECV_DEV, N_SLAB, 1, CAP, 2))(recv_slab_keys, recv_slab_turns).reshape((N_PX, N_PY, RECV, 1))
    recv_lateral = place_ends(jax.random.randint(streams_of[6], (N_PX, N_PY, RECV), 0, CX * CY), jax.random.fold_in(streams_of[6], 1), 0, (CX * CY) - 1).astype(jnp.int32)
    recv_layer = place_ends(jax.random.randint(streams_of[7], (N_PX, N_PY, RECV), 0, CZ), jax.random.fold_in(streams_of[7], 1), 0, CZ - 1).astype(jnp.int32)
    return dict(source=source, phase=phase, attenuation=attenuation, pml_level=pml_level, recv_values=recv_values, recv_slab=recv_slab, recv_lateral=recv_lateral, recv_layer=recv_layer)


def march(state, layer):
    real_part, imag_part = state
    rate_real, rate_imag, force_layer = layer
    new_real = rate_real * real_part - rate_imag * imag_part + force_layer[:, 0]
    new_imag = rate_real * imag_part + rate_imag * real_part + force_layer[:, 1]
    return (new_real, new_imag), jnp.stack([new_real, new_imag], axis=1)


def reference(source, phase, attenuation, pml_level, recv_values, recv_slab, recv_lateral, recv_layer):
    damping = attenuation + (0.5 / NZ) * pml_level.astype(jnp.float32)[None, :, :]
    amplitude = jnp.exp(-damping)
    real_mult = amplitude * jnp.cos(phase)
    imag_mult = amplitude * jnp.sin(phase)
    tile_x = jnp.arange(N_PX, dtype=jnp.int32)[:, None, None]
    tile_y = jnp.arange(N_PY, dtype=jnp.int32)[None, :, None]
    depth_index = recv_slab[..., 0] * CZ + recv_layer
    cross_x = jnp.broadcast_to(tile_x * CX + recv_lateral // CY, depth_index.shape)
    cross_y = jnp.broadcast_to(tile_y * CY + recv_lateral % CY, depth_index.shape)
    forcing = source
    for column in range(COMP):
        forcing = forcing.at[depth_index, column, cross_x, cross_y].add(recv_values[:, :, column, :])
    fields = forcing.reshape(NZ, SHOTS, 2, NX, NY)
    zeros = jnp.zeros((SHOTS, NX, NY), jnp.float32)
    final_down, downward = lax.scan(march, (zeros, zeros), (real_mult, imag_mult, fields))
    final_up, upward = lax.scan(march, (zeros, zeros), (real_mult, imag_mult, fields), reverse=True)
    combined = (downward + upward - fields).reshape(NZ, COMP, NX, NY)
    padded = jnp.pad(combined, ((0, 0), (0, 0), (1, 1), (1, 1)))
    neighbours = padded[:, :, 2:, 1:-1] + padded[:, :, :-2, 1:-1] + padded[:, :, 1:-1, 2:] + padded[:, :, 1:-1, :-2]
    return combined - 0.2 * (4.0 * combined - neighbours)
```

```python
import jax
import jax.numpy as jnp
from jax import lax
from jax.sharding import PartitionSpec as P


def from_behind(array, axis, by):
    count = lax.axis_size(axis)
    pairs = [(i, i + by) for i in range(count) if 0 <= i + by < count]
    return lax.ppermute(array, axis, pairs)


def padded_2(block, sides, width):
    for axis, dim in sides:
        count = lax.axis_size(axis)
        forward = [(i, i + 1) for i in range(count - 1)]
        backward = [(target, source) for source, target in forward]
        low = lax.ppermute(
            lax.slice_in_dim(block, block.shape[dim] - width, None, axis=dim), axis, forward
        )
        high = lax.ppermute(lax.slice_in_dim(block, 0, width, axis=dim), axis, backward)
        block = jnp.concatenate([low, block, high], axis=dim)
    return block


def advance(state, layer):
    real_part, imag_part, prod_real, prod_imag = state
    rate_real, rate_imag, force_layer = layer
    new_real = rate_real * real_part - rate_imag * imag_part + force_layer[:, 0]
    new_imag = rate_real * imag_part + rate_imag * real_part + force_layer[:, 1]
    next_real = rate_real * prod_real - rate_imag * prod_imag
    next_imag = rate_real * prod_imag + rate_imag * prod_real
    return (
        (new_real, new_imag, next_real, next_imag),
        (jnp.stack([new_real, new_imag], axis=1), next_real, next_imag),
    )


def shards(source, phase, attenuation, pml_level, recv_values, recv_slab, recv_lateral, recv_layer):
    layers, components, width_x, width_y = source.shape
    shot_count = components // 2
    slab_count = lax.axis_size("slab")
    depth_total = layers * slab_count
    plane_size = width_x * width_y
    rows_here = recv_values.shape[3]
    capacity = rows_here // min(8, slab_count)
    values = recv_values[0, 0]
    target_slab = recv_slab[0, 0, :, 0]
    position = recv_layer[0, 0] * (components * plane_size) + recv_lateral[0, 0]
    one_hot = (target_slab[:, None] == jnp.arange(slab_count, dtype=jnp.int32)[None, :]).astype(
        jnp.int32
    )
    ranking = jnp.sum((jnp.cumsum(one_hot, axis=0) - one_hot) * one_hot, axis=1)
    target_slot = target_slab * capacity + ranking
    send_values = (
        jnp.zeros((components, slab_count * capacity), jnp.float32).at[:, target_slot].set(values)
    )
    send_places = jnp.zeros((slab_count * capacity,), jnp.int32).at[target_slot].set(position)
    got_values, got_places = (
        lax.all_to_all(
            send_values.reshape(components, slab_count, capacity),
            "slab",
            split_axis=1,
            concat_axis=1,
            tiled=True,
        ),
        lax.all_to_all(
            send_places.reshape(1, slab_count, capacity),
            "slab",
            split_axis=1,
            concat_axis=1,
            tiled=True,
        ),
    )
    inject_values = got_values.reshape(components, slab_count * capacity)
    inject_places = got_places.reshape(slab_count * capacity)
    offsets = (jnp.arange(components, dtype=jnp.int32) * plane_size)[:, None]
    flat_index = (inject_places[None, :] + offsets).reshape(-1)
    forcing = source.reshape(-1).at[flat_index].add(inject_values.reshape(-1))
    fields = forcing.reshape(layers, shot_count, 2, width_x, width_y)
    damping = attenuation + 0.5 / depth_total * pml_level.astype(jnp.float32)[None, :, :]
    amplitude = jnp.exp(-damping)
    real_mult = amplitude * jnp.cos(phase)
    imag_mult = amplitude * jnp.sin(phase)
    zeros = jnp.zeros((shot_count, width_x, width_y), jnp.float32)
    ones_plane = jnp.ones((width_x, width_y), jnp.float32)
    zero_plane = jnp.zeros((width_x, width_y), jnp.float32)
    start_state = (zeros, zeros, ones_plane, zero_plane)
    final_down, down_parts = lax.scan(advance, start_state, (real_mult, imag_mult, fields))
    final_up, up_parts = lax.scan(
        advance, start_state, (real_mult, imag_mult, fields), reverse=True
    )
    local_down, down_real, down_imag = down_parts
    local_up, up_real, up_imag = up_parts
    shots_here = shot_count

    def prefix_pair(a_re, a_im, b_re, b_im, sign):
        step = 1
        while step < slab_count:
            final = 2 * step >= slab_count
            parts = [b_re, b_im] if final else [a_re[None], a_im[None], b_re, b_im]
            got = from_behind(jnp.concatenate(parts, axis=0), "slab", sign * step)
            lead = 0 if final else 2
            g_re = got[lead : lead + shots_here]
            g_im = got[lead + shots_here :]
            next_re = a_re * g_re - a_im * g_im + b_re
            next_im = a_re * g_im + a_im * g_re + b_im
            if not final:
                a_re, a_im = a_re * got[0] - a_im * got[1], a_re * got[1] + a_im * got[0]
            b_re, b_im = next_re, next_im
            step *= 2
        got = from_behind(jnp.concatenate([b_re, b_im], axis=0), "slab", sign)
        return got[:shots_here], got[shots_here:]

    enter_real, enter_imag = prefix_pair(
        down_real[-1], down_imag[-1], local_down[-1][:, 0], local_down[-1][:, 1], 1
    )
    below_real, below_imag = prefix_pair(
        up_real[0], up_imag[0], local_up[0][:, 0], local_up[0][:, 1], -1
    )
    full_down_real = (
        local_down[:, :, 0]
        + down_real[:, None] * enter_real[None]
        - down_imag[:, None] * enter_imag[None]
    )
    full_down_imag = (
        local_down[:, :, 1]
        + down_real[:, None] * enter_imag[None]
        + down_imag[:, None] * enter_real[None]
    )
    full_up_real = (
        local_up[:, :, 0]
        + up_real[:, None] * below_real[None]
        - up_imag[:, None] * below_imag[None]
    )
    full_up_imag = (
        local_up[:, :, 1]
        + up_real[:, None] * below_imag[None]
        + up_imag[:, None] * below_real[None]
    )
    downward = jnp.stack([full_down_real, full_down_imag], axis=2)
    upward = jnp.stack([full_up_real, full_up_imag], axis=2)
    combined = (downward + upward - fields).reshape(layers, components, width_x, width_y)
    padded = padded_2(combined, (("px", 2), ("py", 3)), 1)
    neighbours = (
        padded[:, :, 2:, 1:-1]
        + padded[:, :, :-2, 1:-1]
        + padded[:, :, 1:-1, 2:]
        + padded[:, :, 1:-1, :-2]
    )
    return combined - 0.2 * (4.0 * combined - neighbours)


def solution(mesh):
    in_specs = (
        P("slab", None, "px", "py"),
        P("slab", "px", "py"),
        P("slab", "px", "py"),
        P("px", "py"),
        P("px", "py", None, "slab"),
        P("px", "py", "slab", None),
        P("px", "py", "slab"),
        P("px", "py", "slab"),
    )
    out_specs = P("slab", None, "px", "py")
    return jax.shard_map(shards, mesh=mesh, in_specs=in_specs, out_specs=out_specs, check_vma=False)
```

```python
import jax
import jax.numpy as jnp
from jax import lax
from jax.sharding import PartitionSpec as P


def from_behind(array, axis, by):
    count = lax.axis_size(axis)
    pairs = [(i, i + by) for i in range(count) if 0 <= i + by < count]
    return lax.ppermute(array, axis, pairs)


def padded_2(block, sides, width):
    for axis, dim in sides:
        count = lax.axis_size(axis)
        forward = [(i, i + 1) for i in range(count - 1)]
        backward = [(target, source) for source, target in forward]
        low = lax.ppermute(
            lax.slice_in_dim(block, block.shape[dim] - width, None, axis=dim), axis, forward
        )
        high = lax.ppermute(lax.slice_in_dim(block, 0, width, axis=dim), axis, backward)
        block = jnp.concatenate([low, block, high], axis=dim)
    return block


def advance(state, layer):
    real_part, imag_part, prod_real, prod_imag = state
    rate_real, rate_imag, force_layer = layer
    new_real = rate_real * real_part - rate_imag * imag_part + force_layer[:, 0]
    new_imag = rate_real * imag_part + rate_imag * real_part + force_layer[:, 1]
    next_real = rate_real * prod_real - rate_imag * prod_imag
    next_imag = rate_real * prod_imag + rate_imag * prod_real
    return (
        (new_real, new_imag, next_real, next_imag),
        (jnp.stack([new_real, new_imag], axis=1), next_real, next_imag),
    )


def shards(source, phase, attenuation, pml_level, recv_values, recv_slab, recv_lateral, recv_layer):
    layers, components, width_x, width_y = source.shape
    shot_count = components // 2
    slab_count = lax.axis_size("slab")
    depth_total = layers * slab_count
    plane_size = width_x * width_y
    rows_here = recv_values.shape[3]
    capacity = rows_here // min(8, slab_count)
    values = recv_values[0, 0]
    target_slab = recv_slab[0, 0, :, 0]
    position = recv_layer[0, 0] * plane_size + recv_lateral[0, 0]
    one_hot = (target_slab[:, None] == jnp.arange(slab_count, dtype=jnp.int32)[None, :]).astype(
        jnp.int32
    )
    ranking = jnp.sum((jnp.cumsum(one_hot, axis=0) - one_hot) * one_hot, axis=1)
    target_slot = target_slab * capacity + ranking
    rows = jnp.concatenate([values, position.astype(jnp.float32)[None, :]], axis=0)
    send_rows = jnp.zeros((components + 1, slab_count * capacity), jnp.float32).at[:, target_slot].set(rows)
    got_rows = lax.all_to_all(
        send_rows.reshape(components + 1, slab_count, capacity),
        "slab",
        split_axis=1,
        concat_axis=1,
        tiled=True,
    ).reshape(components + 1, slab_count * capacity)
    inject_values = got_rows[:components]
    inject_places = got_rows[components].astype(jnp.int32)
    row_of = inject_places // width_y
    col_of = inject_places % width_y
    pick_rows = (
        row_of[None, :] == jnp.arange(layers * width_x, dtype=jnp.int32)[:, None]
    ).astype(jnp.bfloat16)
    pick_cols = col_of[:, None] == jnp.arange(width_y, dtype=jnp.int32)[None, :]
    high = lax.reduce_precision(inject_values, exponent_bits=8, mantissa_bits=7)
    rest = inject_values - high
    middle = lax.reduce_precision(rest, exponent_bits=8, mantissa_bits=7)
    low = rest - middle
    pieces = jnp.stack([high, middle, low], axis=0)
    spread = jnp.where(pick_cols[None, None, :, :], pieces[:, :, :, None], 0.0)
    spread = jnp.transpose(spread, (2, 0, 1, 3)).reshape(slab_count * capacity, 3 * components * width_y)
    added = jnp.dot(pick_rows, spread.astype(jnp.bfloat16), preferred_element_type=jnp.float32)
    added = added.reshape(layers * width_x, 3, components * width_y)
    added = (added[:, 0] + added[:, 1]) + added[:, 2]
    added = jnp.transpose(added.reshape(layers, width_x, components, width_y), (0, 2, 1, 3))
    forcing = source + added
    fields = forcing.reshape(layers, shot_count, 2, width_x, width_y)
    damping = attenuation + 0.5 / depth_total * pml_level.astype(jnp.float32)[None, :, :]
    amplitude = jnp.exp(-damping)
    real_mult = amplitude * jnp.cos(phase)
    imag_mult = amplitude * jnp.sin(phase)
    zeros = jnp.zeros((shot_count, width_x, width_y), jnp.float32)
    ones_plane = jnp.ones((width_x, width_y), jnp.float32)
    zero_plane = jnp.zeros((width_x, width_y), jnp.float32)
    start_state = (zeros, zeros, ones_plane, zero_plane)
    final_down, down_parts = lax.scan(advance, start_state, (real_mult, imag_mult, fields))
    final_up, up_parts = lax.scan(
        advance, start_state, (real_mult, imag_mult, fields), reverse=True
    )
    local_down, down_real, down_imag = down_parts
    local_up, up_real, up_imag = up_parts
    shots_here = shot_count

    def prefix_pair(a_re, a_im, b_re, b_im, sign):
        step = 1
        while step < slab_count:
            final = 2 * step >= slab_count
            parts = [b_re, b_im] if final else [a_re[None], a_im[None], b_re, b_im]
            got = from_behind(jnp.concatenate(parts, axis=0), "slab", sign * step)
            lead = 0 if final else 2
            g_re = got[lead : lead + shots_here]
            g_im = got[lead + shots_here :]
            next_re = a_re * g_re - a_im * g_im + b_re
            next_im = a_re * g_im + a_im * g_re + b_im
            if not final:
                a_re, a_im = a_re * got[0] - a_im * got[1], a_re * got[1] + a_im * got[0]
            b_re, b_im = next_re, next_im
            step *= 2
        got = from_behind(jnp.concatenate([b_re, b_im], axis=0), "slab", sign)
        return got[:shots_here], got[shots_here:]

    enter_real, enter_imag = prefix_pair(
        down_real[-1], down_imag[-1], local_down[-1][:, 0], local_down[-1][:, 1], 1
    )
    below_real, below_imag = prefix_pair(
        up_real[0], up_imag[0], local_up[0][:, 0], local_up[0][:, 1], -1
    )
    full_down_real = (
        local_down[:, :, 0]
        + down_real[:, None] * enter_real[None]
        - down_imag[:, None] * enter_imag[None]
    )
    full_down_imag = (
        local_down[:, :, 1]
        + down_real[:, None] * enter_imag[None]
        + down_imag[:, None] * enter_real[None]
    )
    full_up_real = (
        local_up[:, :, 0]
        + up_real[:, None] * below_real[None]
        - up_imag[:, None] * below_imag[None]
    )
    full_up_imag = (
        local_up[:, :, 1]
        + up_real[:, None] * below_imag[None]
        + up_imag[:, None] * below_real[None]
    )
    downward = jnp.stack([full_down_real, full_down_imag], axis=2)
    upward = jnp.stack([full_up_real, full_up_imag], axis=2)
    combined = (downward + upward - fields).reshape(layers, components, width_x, width_y)
    padded = padded_2(combined, (("px", 2), ("py", 3)), 1)
    neighbours = (
        padded[:, :, 2:, 1:-1]
        + padded[:, :, :-2, 1:-1]
        + padded[:, :, 1:-1, 2:]
        + padded[:, :, 1:-1, :-2]
    )
    return combined - 0.2 * (4.0 * combined - neighbours)


def solution(mesh):
    in_specs = (
        P("slab", None, "px", "py"),
        P("slab", "px", "py"),
        P("slab", "px", "py"),
        P("px", "py"),
        P("px", "py", None, "slab"),
        P("px", "py", "slab", None),
        P("px", "py", "slab"),
        P("px", "py", "slab"),
    )
    out_specs = P("slab", None, "px", "py")
    return jax.shard_map(shards, mesh=mesh, in_specs=in_specs, out_specs=out_specs, check_vma=False)
```

```python
import jax
import jax.numpy as jnp
from jax import lax
from jax.sharding import PartitionSpec as P


def from_behind(array, axis, by):
    count = lax.axis_size(axis)
    pairs = [(i, i + by) for i in range(count) if 0 <= i + by < count]
    return lax.ppermute(array, axis, pairs)


def complex_times(a_re, a_im, b_re, b_im):
    return a_re * b_re - a_im * b_im, a_re * b_im + a_im * b_re


def inject_receivers(source, recv_values, recv_slab, recv_lateral, recv_layer):
    layers, components, width_x, width_y = source.shape
    slab_count = lax.axis_size("slab")
    plane_size = width_x * width_y
    rows_here = recv_values.shape[3]
    capacity = rows_here // min(8, slab_count)
    values = recv_values[0, 0]
    target_slab = recv_slab[0, 0, :, 0]
    position = recv_layer[0, 0] * plane_size + recv_lateral[0, 0]
    one_hot = (target_slab[:, None] == jnp.arange(slab_count, dtype=jnp.int32)[None, :]).astype(
        jnp.int32
    )
    ranking = jnp.sum((jnp.cumsum(one_hot, axis=0) - one_hot) * one_hot, axis=1)
    target_slot = target_slab * capacity + ranking
    rows = jnp.concatenate([values, position.astype(jnp.float32)[None, :]], axis=0)
    send_rows = (
        jnp.zeros((components + 1, slab_count * capacity), jnp.float32).at[:, target_slot].set(rows)
    )
    got_rows = lax.all_to_all(
        send_rows.reshape(components + 1, slab_count, capacity),
        "slab",
        split_axis=1,
        concat_axis=1,
        tiled=True,
    ).reshape(components + 1, slab_count * capacity)
    inject_values = got_rows[:components]
    inject_places = got_rows[components].astype(jnp.int32)
    row_of = inject_places // width_y
    col_of = inject_places % width_y
    pick_rows = (
        row_of[None, :] == jnp.arange(layers * width_x, dtype=jnp.int32)[:, None]
    ).astype(jnp.bfloat16)
    pick_cols = col_of[:, None] == jnp.arange(width_y, dtype=jnp.int32)[None, :]
    high = lax.reduce_precision(inject_values, exponent_bits=8, mantissa_bits=7)
    rest = inject_values - high
    middle = lax.reduce_precision(rest, exponent_bits=8, mantissa_bits=7)
    low = rest - middle
    pieces = jnp.stack([high, middle, low], axis=0)
    spread = jnp.where(pick_cols[None, None, :, :], pieces[:, :, :, None], 0.0)
    spread = jnp.transpose(spread, (2, 0, 1, 3)).reshape(
        slab_count * capacity, 3 * components * width_y
    )
    added = jnp.dot(pick_rows, spread.astype(jnp.bfloat16), preferred_element_type=jnp.float32)
    added = added.reshape(layers * width_x, 3, components * width_y)
    added = (added[:, 0] + added[:, 1]) + added[:, 2]
    added = jnp.transpose(added.reshape(layers, width_x, components, width_y), (0, 2, 1, 3))
    return source + added


def map_powers(a_re, a_im, sign):
    slab_count = lax.axis_size("slab")
    powers = [(a_re, a_im)]
    step = 1
    while 2 * step < slab_count:
        got = from_behind(jnp.stack([a_re, a_im], axis=0), "slab", sign * step)
        a_re, a_im = complex_times(a_re, a_im, got[0], got[1])
        powers.append((a_re, a_im))
        step *= 2
    return powers


def entering_state(b_re, b_im, powers, sign):
    slab_count = lax.axis_size("slab")
    shots = b_re.shape[0]
    step = 1
    level = 0
    while step < slab_count:
        got = from_behind(jnp.concatenate([b_re, b_im], axis=0), "slab", sign * step)
        a_re, a_im = powers[level]
        t_re, t_im = complex_times(a_re[None], a_im[None], got[:shots], got[shots:])
        b_re, b_im = t_re + b_re, t_im + b_im
        step *= 2
        level += 1
    got = from_behind(jnp.concatenate([b_re, b_im], axis=0), "slab", sign)
    return got[:shots], got[shots:]


def neighbour_sum(block):
    from_low_x = from_behind(block[:, :, -1, :], "px", 1)
    from_high_x = from_behind(block[:, :, 0, :], "px", -1)
    from_low_y = from_behind(block[:, :, :, -1], "py", 1)
    from_high_y = from_behind(block[:, :, :, 0], "py", -1)
    next_x = jnp.concatenate([block[:, :, 1:, :], from_high_x[:, :, None, :]], axis=2)
    prev_x = jnp.concatenate([from_low_x[:, :, None, :], block[:, :, :-1, :]], axis=2)
    next_y = jnp.concatenate([block[:, :, :, 1:], from_high_y[:, :, :, None]], axis=3)
    prev_y = jnp.concatenate([from_low_y[:, :, :, None], block[:, :, :, :-1]], axis=3)
    return next_x + prev_x + next_y + prev_y


def shards(source, phase, attenuation, pml_level, recv_values, recv_slab, recv_lateral, recv_layer):
    layers, components, width_x, width_y = source.shape
    shot_count = components // 2
    slab_count = lax.axis_size("slab")
    depth_total = layers * slab_count

    damping = attenuation + 0.5 / depth_total * pml_level.astype(jnp.float32)[None, :, :]
    amplitude = jnp.exp(-damping)
    rate_re = amplitude * jnp.cos(phase)
    rate_im = amplitude * jnp.sin(phase)

    prod_down = [(rate_re[0], rate_im[0])]
    for k in range(1, layers):
        prod_down.append(complex_times(rate_re[k], rate_im[k], *prod_down[-1]))
    prod_up = [None] * layers
    prod_up[layers - 1] = (rate_re[layers - 1], rate_im[layers - 1])
    for k in range(layers - 2, -1, -1):
        prod_up[k] = complex_times(rate_re[k], rate_im[k], *prod_up[k + 1])
    powers_down = map_powers(*prod_down[-1], 1)
    powers_up = map_powers(*prod_up[0], -1)

    forcing = inject_receivers(source, recv_values, recv_slab, recv_lateral, recv_layer)
    fields = forcing.reshape(layers, shot_count, 2, width_x, width_y)
    f_re = fields[:, :, 0]
    f_im = fields[:, :, 1]

    down = [None] * layers
    state = (f_re[0], f_im[0])
    down[0] = state
    for k in range(1, layers):
        t_re, t_im = complex_times(rate_re[k][None], rate_im[k][None], *state)
        state = (t_re + f_re[k], t_im + f_im[k])
        down[k] = state
    up = [None] * layers
    state = (f_re[layers - 1], f_im[layers - 1])
    up[layers - 1] = state
    for k in range(layers - 2, -1, -1):
        t_re, t_im = complex_times(rate_re[k][None], rate_im[k][None], *state)
        state = (t_re + f_re[k], t_im + f_im[k])
        up[k] = state

    enter_re, enter_im = entering_state(*down[layers - 1], powers_down, 1)
    below_re, below_im = entering_state(*up[0], powers_up, -1)

    combined = []
    for k in range(layers):
        e_re, e_im = complex_times(prod_down[k][0][None], prod_down[k][1][None], enter_re, enter_im)
        u_re, u_im = complex_times(prod_up[k][0][None], prod_up[k][1][None], below_re, below_im)
        c_re = (down[k][0] + e_re) + (up[k][0] + u_re) - f_re[k]
        c_im = (down[k][1] + e_im) + (up[k][1] + u_im) - f_im[k]
        combined.append(jnp.stack([c_re, c_im], axis=1).reshape(components, width_x, width_y))
    combined = jnp.stack(combined, axis=0)
    neighbours = neighbour_sum(combined)
    return combined - 0.2 * (4.0 * combined - neighbours)


def solution(mesh):
    in_specs = (
        P("slab", None, "px", "py"),
        P("slab", "px", "py"),
        P("slab", "px", "py"),
        P("px", "py"),
        P("px", "py", None, "slab"),
        P("px", "py", "slab", None),
        P("px", "py", "slab"),
        P("px", "py", "slab"),
    )
    out_specs = P("slab", None, "px", "py")
    return jax.shard_map(shards, mesh=mesh, in_specs=in_specs, out_specs=out_specs, check_vma=False)
```

```python
import jax
import jax.numpy as jnp
from jax import lax
from jax.sharding import PartitionSpec as P


def from_behind(array, axis, by):
    count = lax.axis_size(axis)
    pairs = [(i, i + by) for i in range(count) if 0 <= i + by < count]
    return lax.ppermute(array, axis, pairs)


def complex_times(a_re, a_im, b_re, b_im):
    return a_re * b_re - a_im * b_im, a_re * b_im + a_im * b_re


def inject_receivers(source, recv_values, recv_slab, recv_lateral, recv_layer):
    layers, components, width_x, width_y = source.shape
    slab_count = lax.axis_size("slab")
    plane_size = width_x * width_y
    rows_here = recv_values.shape[3]
    capacity = rows_here // min(8, slab_count)
    values = recv_values[0, 0]
    target_slab = recv_slab[0, 0, :, 0]
    position = recv_layer[0, 0] * plane_size + recv_lateral[0, 0]
    one_hot = (target_slab[:, None] == jnp.arange(slab_count, dtype=jnp.int32)[None, :]).astype(
        jnp.int32
    )
    ranking = jnp.sum((jnp.cumsum(one_hot, axis=0) - one_hot) * one_hot, axis=1)
    target_slot = target_slab * capacity + ranking
    rows = jnp.concatenate([values, position.astype(jnp.float32)[None, :]], axis=0)
    send_rows = (
        jnp.zeros((components + 1, slab_count * capacity), jnp.float32).at[:, target_slot].set(rows)
    )
    got_rows = lax.all_to_all(
        send_rows.reshape(components + 1, slab_count, capacity),
        "slab",
        split_axis=1,
        concat_axis=1,
        tiled=True,
    ).reshape(components + 1, slab_count * capacity)
    inject_values = got_rows[:components]
    inject_places = got_rows[components].astype(jnp.int32)
    row_of = inject_places // width_y
    col_of = inject_places % width_y
    pick_rows = (
        row_of[None, :] == jnp.arange(layers * width_x, dtype=jnp.int32)[:, None]
    ).astype(jnp.bfloat16)
    pick_cols = col_of[:, None] == jnp.arange(width_y, dtype=jnp.int32)[None, :]
    high = lax.reduce_precision(inject_values, exponent_bits=8, mantissa_bits=7)
    rest = inject_values - high
    middle = lax.reduce_precision(rest, exponent_bits=8, mantissa_bits=7)
    low = rest - middle
    pieces = jnp.stack([high, middle, low], axis=0)
    spread = jnp.where(pick_cols[None, None, :, :], pieces[:, :, :, None], 0.0)
    spread = jnp.transpose(spread, (2, 0, 1, 3)).reshape(
        slab_count * capacity, 3 * components * width_y
    )
    added = jnp.dot(pick_rows, spread.astype(jnp.bfloat16), preferred_element_type=jnp.float32)
    added = added.reshape(layers * width_x, 3, components * width_y)
    added = (added[:, 0] + added[:, 1]) + added[:, 2]
    added = jnp.transpose(added.reshape(layers, width_x, components, width_y), (0, 2, 1, 3))
    return source + added


def exchange(array, step):
    count = lax.axis_size("slab")
    return lax.ppermute(array, "slab", [(i, i ^ step) for i in range(count)])


def block_products(a_re, a_im):
    slab_count = lax.axis_size("slab")
    here = lax.axis_index("slab")
    one = jnp.ones_like(a_re)
    zero = jnp.zeros_like(a_re)
    total = (a_re, a_im)
    below = (one, zero)
    above = (one, zero)
    levels = []
    step = 1
    while 2 * step < slab_count:
        got = exchange(jnp.stack(total, axis=0), step)
        partner = (got[0], got[1])
        levels.append((total, partner, below, above))
        lower = (here & step) == 0
        grown_below = complex_times(*below, *partner)
        grown_above = complex_times(*above, *partner)
        below = (jnp.where(lower, below[0], grown_below[0]), jnp.where(lower, below[1], grown_below[1]))
        above = (jnp.where(lower, grown_above[0], above[0]), jnp.where(lower, grown_above[1], above[1]))
        total = complex_times(*total, *partner)
        step *= 2
    levels.append((None, None, below, above))
    return levels


def entering_states(down_b, up_b, levels):
    slab_count = lax.axis_size("slab")
    here = lax.axis_index("slab")
    shots = down_b[0].shape[0]
    before = (jnp.zeros_like(down_b[0]), jnp.zeros_like(down_b[1]))
    after = (jnp.zeros_like(up_b[0]), jnp.zeros_like(up_b[1]))
    step = 1
    level = 0
    while step < slab_count:
        lower = (here & step) == 0
        total, partner, below, above = levels[level]
        if 2 * step < slab_count:
            got = exchange(jnp.concatenate([*down_b, *up_b], axis=0), step)
            pd = (got[:shots], got[shots : 2 * shots])
            pu = (got[2 * shots : 3 * shots], got[3 * shots :])
            t_re, t_im = total[0][None], total[1][None]
            q_re, q_im = partner[0][None], partner[1][None]
            first = (jnp.where(lower, q_re, t_re), jnp.where(lower, q_im, t_im))
            inner = (jnp.where(lower, down_b[0], pd[0]), jnp.where(lower, down_b[1], pd[1]))
            outer = (jnp.where(lower, pd[0], down_b[0]), jnp.where(lower, pd[1], down_b[1]))
            m_re, m_im = complex_times(*first, *inner)
            new_down = (m_re + outer[0], m_im + outer[1])
            first = (jnp.where(lower, t_re, q_re), jnp.where(lower, t_im, q_im))
            inner = (jnp.where(lower, pu[0], up_b[0]), jnp.where(lower, pu[1], up_b[1]))
            outer = (jnp.where(lower, up_b[0], pu[0]), jnp.where(lower, up_b[1], pu[1]))
            m_re, m_im = complex_times(*first, *inner)
            new_up = (m_re + outer[0], m_im + outer[1])
        else:
            send = jnp.concatenate(
                [jnp.where(lower, down_b[0], up_b[0]), jnp.where(lower, down_b[1], up_b[1])], axis=0
            )
            got = exchange(send, step)
            pd = (got[:shots], got[shots:])
            pu = pd
        g_re, g_im = complex_times(below[0][None], below[1][None], *pd)
        before = (
            jnp.where(lower, before[0], g_re + before[0]),
            jnp.where(lower, before[1], g_im + before[1]),
        )
        g_re, g_im = complex_times(above[0][None], above[1][None], *pu)
        after = (
            jnp.where(lower, g_re + after[0], after[0]),
            jnp.where(lower, g_im + after[1], after[1]),
        )
        if 2 * step < slab_count:
            down_b, up_b = new_down, new_up
        step *= 2
        level += 1
    return before, after


def neighbour_sum(block):
    from_low_x = from_behind(block[:, :, -1, :], "px", 1)
    from_high_x = from_behind(block[:, :, 0, :], "px", -1)
    from_low_y = from_behind(block[:, :, :, -1], "py", 1)
    from_high_y = from_behind(block[:, :, :, 0], "py", -1)
    next_x = jnp.concatenate([block[:, :, 1:, :], from_high_x[:, :, None, :]], axis=2)
    prev_x = jnp.concatenate([from_low_x[:, :, None, :], block[:, :, :-1, :]], axis=2)
    next_y = jnp.concatenate([block[:, :, :, 1:], from_high_y[:, :, :, None]], axis=3)
    prev_y = jnp.concatenate([from_low_y[:, :, :, None], block[:, :, :, :-1]], axis=3)
    return next_x + prev_x + next_y + prev_y


def shards(source, phase, attenuation, pml_level, recv_values, recv_slab, recv_lateral, recv_layer):
    layers, components, width_x, width_y = source.shape
    shot_count = components // 2
    slab_count = lax.axis_size("slab")
    depth_total = layers * slab_count

    damping = attenuation + 0.5 / depth_total * pml_level.astype(jnp.float32)[None, :, :]
    amplitude = jnp.exp(-damping)
    rate_re = amplitude * jnp.cos(phase)
    rate_im = amplitude * jnp.sin(phase)

    prod_down = [(rate_re[0], rate_im[0])]
    for k in range(1, layers):
        prod_down.append(complex_times(rate_re[k], rate_im[k], *prod_down[-1]))
    prod_up = [None] * layers
    prod_up[layers - 1] = (rate_re[layers - 1], rate_im[layers - 1])
    for k in range(layers - 2, -1, -1):
        prod_up[k] = complex_times(rate_re[k], rate_im[k], *prod_up[k + 1])
    levels = block_products(*prod_down[-1])

    forcing = inject_receivers(source, recv_values, recv_slab, recv_lateral, recv_layer)
    fields = forcing.reshape(layers, shot_count, 2, width_x, width_y)
    f_re = fields[:, :, 0]
    f_im = fields[:, :, 1]

    down = [None] * layers
    state = (f_re[0], f_im[0])
    down[0] = state
    for k in range(1, layers):
        t_re, t_im = complex_times(rate_re[k][None], rate_im[k][None], *state)
        state = (t_re + f_re[k], t_im + f_im[k])
        down[k] = state
    up = [None] * layers
    state = (f_re[layers - 1], f_im[layers - 1])
    up[layers - 1] = state
    for k in range(layers - 2, -1, -1):
        t_re, t_im = complex_times(rate_re[k][None], rate_im[k][None], *state)
        state = (t_re + f_re[k], t_im + f_im[k])
        up[k] = state

    (enter_re, enter_im), (below_re, below_im) = entering_states(down[layers - 1], up[0], levels)

    combined = []
    for k in range(layers):
        e_re, e_im = complex_times(prod_down[k][0][None], prod_down[k][1][None], enter_re, enter_im)
        u_re, u_im = complex_times(prod_up[k][0][None], prod_up[k][1][None], below_re, below_im)
        c_re = (down[k][0] + e_re) + (up[k][0] + u_re) - f_re[k]
        c_im = (down[k][1] + e_im) + (up[k][1] + u_im) - f_im[k]
        combined.append(jnp.stack([c_re, c_im], axis=1).reshape(components, width_x, width_y))
    combined = jnp.stack(combined, axis=0)
    neighbours = neighbour_sum(combined)
    return combined - 0.2 * (4.0 * combined - neighbours)


def solution(mesh):
    in_specs = (
        P("slab", None, "px", "py"),
        P("slab", "px", "py"),
        P("slab", "px", "py"),
        P("px", "py"),
        P("px", "py", None, "slab"),
        P("px", "py", "slab", None),
        P("px", "py", "slab"),
        P("px", "py", "slab"),
    )
    out_specs = P("slab", None, "px", "py")
    return jax.shard_map(shards, mesh=mesh, in_specs=in_specs, out_specs=out_specs, check_vma=False)
```

```python
import jax
import jax.numpy as jnp
from jax import lax
from jax.sharding import PartitionSpec as P


def from_behind(array, axis, by):
    count = lax.axis_size(axis)
    pairs = [(i, i + by) for i in range(count) if 0 <= i + by < count]
    return lax.ppermute(array, axis, pairs)


def complex_times(a_re, a_im, b_re, b_im):
    return a_re * b_re - a_im * b_im, a_re * b_im + a_im * b_re


def inject_receivers(source, recv_values, recv_slab, recv_lateral, recv_layer, levels):
    layers, components, width_x, width_y = source.shape
    slab_count = lax.axis_size("slab")
    plane_size = width_x * width_y
    rows_here = recv_values.shape[3]
    capacity = rows_here // min(8, slab_count)
    values = recv_values[0, 0]
    target_slab = recv_slab[0, 0, :, 0]
    position = recv_layer[0, 0] * plane_size + recv_lateral[0, 0]
    one_hot = (target_slab[:, None] == jnp.arange(slab_count, dtype=jnp.int32)[None, :]).astype(
        jnp.int32
    )
    ranking = jnp.sum((jnp.cumsum(one_hot, axis=0) - one_hot) * one_hot, axis=1)
    target_slot = target_slab * capacity + ranking
    rows = jnp.concatenate([values, position.astype(jnp.float32)[None, :]], axis=0)
    send_rows = (
        jnp.zeros((components + 1, slab_count * capacity), jnp.float32).at[:, target_slot].set(rows)
    )
    got_rows = lax.all_to_all(
        send_rows.reshape(components + 1, slab_count, capacity),
        "slab",
        split_axis=1,
        concat_axis=1,
        tiled=True,
    ).reshape(components + 1, slab_count * capacity)
    got_rows, levels = lax.optimization_barrier((got_rows, levels))
    inject_values = got_rows[:components]
    inject_places = got_rows[components].astype(jnp.int32)
    row_of = inject_places // width_y
    col_of = inject_places % width_y
    pick_rows = (
        row_of[None, :] == jnp.arange(layers * width_x, dtype=jnp.int32)[:, None]
    ).astype(jnp.bfloat16)
    pick_cols = col_of[:, None] == jnp.arange(width_y, dtype=jnp.int32)[None, :]
    high = lax.reduce_precision(inject_values, exponent_bits=8, mantissa_bits=7)
    rest = inject_values - high
    middle = lax.reduce_precision(rest, exponent_bits=8, mantissa_bits=7)
    low = rest - middle
    pieces = jnp.stack([high, middle, low], axis=0)
    spread = jnp.where(pick_cols[None, None, :, :], pieces[:, :, :, None], 0.0)
    spread = jnp.transpose(spread, (2, 0, 1, 3)).reshape(
        slab_count * capacity, 3 * components * width_y
    )
    added = jnp.dot(pick_rows, spread.astype(jnp.bfloat16), preferred_element_type=jnp.float32)
    added = added.reshape(layers * width_x, 3, components * width_y)
    added = (added[:, 0] + added[:, 1]) + added[:, 2]
    added = jnp.transpose(added.reshape(layers, width_x, components, width_y), (0, 2, 1, 3))
    return source + added, levels


def exchange(array, step):
    count = lax.axis_size("slab")
    return lax.ppermute(array, "slab", [(i, i ^ step) for i in range(count)])


def block_products(a_re, a_im):
    slab_count = lax.axis_size("slab")
    here = lax.axis_index("slab")
    one = jnp.ones_like(a_re)
    zero = jnp.zeros_like(a_re)
    total = (a_re, a_im)
    below = (one, zero)
    above = (one, zero)
    levels = []
    step = 1
    while 2 * step < slab_count:
        got = exchange(jnp.stack(total, axis=0), step)
        partner = (got[0], got[1])
        levels.append((total, partner, below, above))
        lower = (here & step) == 0
        grown_below = complex_times(*below, *partner)
        grown_above = complex_times(*above, *partner)
        below = (jnp.where(lower, below[0], grown_below[0]), jnp.where(lower, below[1], grown_below[1]))
        above = (jnp.where(lower, grown_above[0], above[0]), jnp.where(lower, grown_above[1], above[1]))
        total = complex_times(*total, *partner)
        step *= 2
    levels.append((None, None, below, above))
    return levels


def entering_states(down_b, up_b, levels):
    slab_count = lax.axis_size("slab")
    here = lax.axis_index("slab")
    shots = down_b[0].shape[0]
    before = (jnp.zeros_like(down_b[0]), jnp.zeros_like(down_b[1]))
    after = (jnp.zeros_like(up_b[0]), jnp.zeros_like(up_b[1]))
    step = 1
    level = 0
    while step < slab_count:
        lower = (here & step) == 0
        total, partner, below, above = levels[level]
        if 2 * step < slab_count:
            got = exchange(jnp.concatenate([*down_b, *up_b], axis=0), step)
            pd = (got[:shots], got[shots : 2 * shots])
            pu = (got[2 * shots : 3 * shots], got[3 * shots :])
            t_re, t_im = total[0][None], total[1][None]
            q_re, q_im = partner[0][None], partner[1][None]
            first = (jnp.where(lower, q_re, t_re), jnp.where(lower, q_im, t_im))
            inner = (jnp.where(lower, down_b[0], pd[0]), jnp.where(lower, down_b[1], pd[1]))
            outer = (jnp.where(lower, pd[0], down_b[0]), jnp.where(lower, pd[1], down_b[1]))
            m_re, m_im = complex_times(*first, *inner)
            new_down = (m_re + outer[0], m_im + outer[1])
            first = (jnp.where(lower, t_re, q_re), jnp.where(lower, t_im, q_im))
            inner = (jnp.where(lower, pu[0], up_b[0]), jnp.where(lower, pu[1], up_b[1]))
            outer = (jnp.where(lower, up_b[0], pu[0]), jnp.where(lower, up_b[1], pu[1]))
            m_re, m_im = complex_times(*first, *inner)
            new_up = (m_re + outer[0], m_im + outer[1])
        else:
            send = jnp.concatenate(
                [jnp.where(lower, down_b[0], up_b[0]), jnp.where(lower, down_b[1], up_b[1])], axis=0
            )
            got = exchange(send, step)
            pd = (got[:shots], got[shots:])
            pu = pd
        g_re, g_im = complex_times(below[0][None], below[1][None], *pd)
        before = (
            jnp.where(lower, before[0], g_re + before[0]),
            jnp.where(lower, before[1], g_im + before[1]),
        )
        g_re, g_im = complex_times(above[0][None], above[1][None], *pu)
        after = (
            jnp.where(lower, g_re + after[0], after[0]),
            jnp.where(lower, g_im + after[1], after[1]),
        )
        if 2 * step < slab_count:
            down_b, up_b = new_down, new_up
        step *= 2
        level += 1
    return before, after


def edge_pair(block, axis, dim):
    count = lax.axis_size(axis)
    last = lax.index_in_dim(block, block.shape[dim] - 1, axis=dim, keepdims=False)
    first = lax.index_in_dim(block, 0, axis=dim, keepdims=False)
    if count == 2:
        here = lax.axis_index(axis)
        got = lax.ppermute(jnp.where(here == 0, last, first), axis, [(0, 1), (1, 0)])
        zero = jnp.zeros_like(got)
        return jnp.where(here == 1, got, zero), jnp.where(here == 0, got, zero)
    return from_behind(last, axis, 1), from_behind(first, axis, -1)


def neighbour_sum(block):
    from_low_x, from_high_x = edge_pair(block, "px", 2)
    from_low_y, from_high_y = edge_pair(block, "py", 3)
    next_x = jnp.concatenate([block[:, :, 1:, :], from_high_x[:, :, None, :]], axis=2)
    prev_x = jnp.concatenate([from_low_x[:, :, None, :], block[:, :, :-1, :]], axis=2)
    next_y = jnp.concatenate([block[:, :, :, 1:], from_high_y[:, :, :, None]], axis=3)
    prev_y = jnp.concatenate([from_low_y[:, :, :, None], block[:, :, :, :-1]], axis=3)
    return next_x + prev_x + next_y + prev_y


def shards(source, phase, attenuation, pml_level, recv_values, recv_slab, recv_lateral, recv_layer):
    layers, components, width_x, width_y = source.shape
    shot_count = components // 2
    slab_count = lax.axis_size("slab")
    depth_total = layers * slab_count

    damping = attenuation + 0.5 / depth_total * pml_level.astype(jnp.float32)[None, :, :]
    amplitude = jnp.exp(-damping)
    rate_re = amplitude * jnp.cos(phase)
    rate_im = amplitude * jnp.sin(phase)

    prod_down = [(rate_re[0], rate_im[0])]
    for k in range(1, layers):
        prod_down.append(complex_times(rate_re[k], rate_im[k], *prod_down[-1]))
    prod_up = [None] * layers
    prod_up[layers - 1] = (rate_re[layers - 1], rate_im[layers - 1])
    for k in range(layers - 2, -1, -1):
        prod_up[k] = complex_times(rate_re[k], rate_im[k], *prod_up[k + 1])
    levels = block_products(*prod_down[-1])

    forcing, levels = inject_receivers(
        source, recv_values, recv_slab, recv_lateral, recv_layer, levels
    )
    fields = forcing.reshape(layers, shot_count, 2, width_x, width_y)
    f_re = fields[:, :, 0]
    f_im = fields[:, :, 1]

    down = [None] * layers
    state = (f_re[0], f_im[0])
    down[0] = state
    for k in range(1, layers):
        t_re, t_im = complex_times(rate_re[k][None], rate_im[k][None], *state)
        state = (t_re + f_re[k], t_im + f_im[k])
        down[k] = state
    up = [None] * layers
    state = (f_re[layers - 1], f_im[layers - 1])
    up[layers - 1] = state
    for k in range(layers - 2, -1, -1):
        t_re, t_im = complex_times(rate_re[k][None], rate_im[k][None], *state)
        state = (t_re + f_re[k], t_im + f_im[k])
        up[k] = state

    (enter_re, enter_im), (below_re, below_im) = entering_states(down[layers - 1], up[0], levels)

    combined = []
    for k in range(layers):
        e_re, e_im = complex_times(prod_down[k][0][None], prod_down[k][1][None], enter_re, enter_im)
        u_re, u_im = complex_times(prod_up[k][0][None], prod_up[k][1][None], below_re, below_im)
        c_re = (down[k][0] + e_re) + (up[k][0] + u_re) - f_re[k]
        c_im = (down[k][1] + e_im) + (up[k][1] + u_im) - f_im[k]
        combined.append(jnp.stack([c_re, c_im], axis=1).reshape(components, width_x, width_y))
    combined = jnp.stack(combined, axis=0)
    neighbours = neighbour_sum(combined)
    return combined - 0.2 * (4.0 * combined - neighbours)


def solution(mesh):
    in_specs = (
        P("slab", None, "px", "py"),
        P("slab", "px", "py"),
        P("slab", "px", "py"),
        P("px", "py"),
        P("px", "py", None, "slab"),
        P("px", "py", "slab", None),
        P("px", "py", "slab"),
        P("px", "py", "slab"),
    )
    out_specs = P("slab", None, "px", "py")
    return jax.shard_map(shards, mesh=mesh, in_specs=in_specs, out_specs=out_specs, check_vma=False)
```

```python
import jax
import jax.numpy as jnp
from jax import lax
from jax.sharding import PartitionSpec as P
from jax.experimental import pallas as pl
from jax.experimental.pallas import tpu as pltpu


def from_behind(array, axis, by):
    count = lax.axis_size(axis)
    pairs = [(i, i + by) for i in range(count) if 0 <= i + by < count]
    return lax.ppermute(array, axis, pairs)


def complex_times(a_re, a_im, b_re, b_im):
    return a_re * b_re - a_im * b_im, a_re * b_im + a_im * b_re


def inject_receivers(source, recv_values, recv_slab, recv_lateral, recv_layer, levels):
    layers, components, width_x, width_y = source.shape
    slab_count = lax.axis_size("slab")
    plane_size = width_x * width_y
    rows_here = recv_values.shape[3]
    capacity = rows_here // min(8, slab_count)
    values = recv_values[0, 0]
    target_slab = recv_slab[0, 0, :, 0]
    position = recv_layer[0, 0] * plane_size + recv_lateral[0, 0]
    one_hot = (target_slab[:, None] == jnp.arange(slab_count, dtype=jnp.int32)[None, :]).astype(
        jnp.int32
    )
    ranking = jnp.sum((jnp.cumsum(one_hot, axis=0) - one_hot) * one_hot, axis=1)
    target_slot = target_slab * capacity + ranking
    rows = jnp.concatenate([values, position.astype(jnp.float32)[None, :]], axis=0)
    send_rows = (
        jnp.zeros((components + 1, slab_count * capacity), jnp.float32).at[:, target_slot].set(rows)
    )
    got_rows = lax.all_to_all(
        send_rows.reshape(components + 1, slab_count, capacity),
        "slab",
        split_axis=1,
        concat_axis=1,
        tiled=True,
    ).reshape(components + 1, slab_count * capacity)
    got_rows, levels = lax.optimization_barrier((got_rows, levels))
    inject_values = got_rows[:components]
    inject_places = got_rows[components].astype(jnp.int32)
    row_of = inject_places // width_y
    col_of = inject_places % width_y
    pick_rows = (
        row_of[None, :] == jnp.arange(layers * width_x, dtype=jnp.int32)[:, None]
    ).astype(jnp.bfloat16)
    pick_cols = col_of[:, None] == jnp.arange(width_y, dtype=jnp.int32)[None, :]
    high = lax.reduce_precision(inject_values, exponent_bits=8, mantissa_bits=7)
    rest = inject_values - high
    middle = lax.reduce_precision(rest, exponent_bits=8, mantissa_bits=7)
    low = rest - middle
    pieces = jnp.stack([high, middle, low], axis=0)
    spread = jnp.where(pick_cols[None, None, :, :], pieces[:, :, :, None], 0.0)
    spread = jnp.transpose(spread, (2, 0, 1, 3)).reshape(
        slab_count * capacity, 3 * components * width_y
    )
    added = jnp.dot(pick_rows, spread.astype(jnp.bfloat16), preferred_element_type=jnp.float32)
    added = added.reshape(layers * width_x, 3, components * width_y)
    added = (added[:, 0] + added[:, 1]) + added[:, 2]
    added = jnp.transpose(added.reshape(layers, width_x, components, width_y), (0, 2, 1, 3))
    return source + added, levels


def exchange(array, step):
    count = lax.axis_size("slab")
    return lax.ppermute(array, "slab", [(i, i ^ step) for i in range(count)])


def block_products(a_re, a_im):
    slab_count = lax.axis_size("slab")
    here = lax.axis_index("slab")
    one = jnp.ones_like(a_re)
    zero = jnp.zeros_like(a_re)
    total = (a_re, a_im)
    below = (one, zero)
    above = (one, zero)
    levels = []
    step = 1
    while 2 * step < slab_count:
        got = exchange(jnp.stack(total, axis=0), step)
        partner = (got[0], got[1])
        levels.append((total, partner, below, above))
        lower = (here & step) == 0
        grown_below = complex_times(*below, *partner)
        grown_above = complex_times(*above, *partner)
        below = (jnp.where(lower, below[0], grown_below[0]), jnp.where(lower, below[1], grown_below[1]))
        above = (jnp.where(lower, grown_above[0], above[0]), jnp.where(lower, grown_above[1], above[1]))
        total = complex_times(*total, *partner)
        step *= 2
    levels.append((None, None, below, above))
    return levels


def entering_states(down_b, up_b, levels):
    slab_count = lax.axis_size("slab")
    here = lax.axis_index("slab")
    shots = down_b[0].shape[0]
    before = (jnp.zeros_like(down_b[0]), jnp.zeros_like(down_b[1]))
    after = (jnp.zeros_like(up_b[0]), jnp.zeros_like(up_b[1]))
    step = 1
    level = 0
    while step < slab_count:
        lower = (here & step) == 0
        total, partner, below, above = levels[level]
        if 2 * step < slab_count:
            got = exchange(jnp.concatenate([*down_b, *up_b], axis=0), step)
            pd = (got[:shots], got[shots : 2 * shots])
            pu = (got[2 * shots : 3 * shots], got[3 * shots :])
            t_re, t_im = total[0][None], total[1][None]
            q_re, q_im = partner[0][None], partner[1][None]
            first = (jnp.where(lower, q_re, t_re), jnp.where(lower, q_im, t_im))
            inner = (jnp.where(lower, down_b[0], pd[0]), jnp.where(lower, down_b[1], pd[1]))
            outer = (jnp.where(lower, pd[0], down_b[0]), jnp.where(lower, pd[1], down_b[1]))
            m_re, m_im = complex_times(*first, *inner)
            new_down = (m_re + outer[0], m_im + outer[1])
            first = (jnp.where(lower, t_re, q_re), jnp.where(lower, t_im, q_im))
            inner = (jnp.where(lower, pu[0], up_b[0]), jnp.where(lower, pu[1], up_b[1]))
            outer = (jnp.where(lower, up_b[0], pu[0]), jnp.where(lower, up_b[1], pu[1]))
            m_re, m_im = complex_times(*first, *inner)
            new_up = (m_re + outer[0], m_im + outer[1])
        else:
            send = jnp.concatenate(
                [jnp.where(lower, down_b[0], up_b[0]), jnp.where(lower, down_b[1], up_b[1])], axis=0
            )
            got = exchange(send, step)
            pd = (got[:shots], got[shots:])
            pu = pd
        g_re, g_im = complex_times(below[0][None], below[1][None], *pd)
        before = (
            jnp.where(lower, before[0], g_re + before[0]),
            jnp.where(lower, before[1], g_im + before[1]),
        )
        g_re, g_im = complex_times(above[0][None], above[1][None], *pu)
        after = (
            jnp.where(lower, g_re + after[0], after[0]),
            jnp.where(lower, g_im + after[1], after[1]),
        )
        if 2 * step < slab_count:
            down_b, up_b = new_down, new_up
        step *= 2
        level += 1
    return before, after


def edge_pair(last, first, axis):
    count = lax.axis_size(axis)
    if count == 2:
        here = lax.axis_index(axis)
        got = lax.ppermute(jnp.where(here == 0, last, first), axis, [(0, 1), (1, 0)])
        zero = jnp.zeros_like(got)
        return jnp.where(here == 1, got, zero), jnp.where(here == 0, got, zero)
    return from_behind(last, axis, 1), from_behind(first, axis, -1)


def sweep_kernel(f_ref, rr_ref, ri_ref, er_ref, ei_ref, br_ref, bi_ref,
                 c_ref, x0_ref, x1_ref, y0_ref, y1_ref):
    layers = f_ref.shape[0]
    shots = er_ref.shape[0]
    downs = []
    for s in range(shots):
        w_re, w_im = er_ref[s], ei_ref[s]
        per_layer = []
        for k in range(layers):
            t_re, t_im = complex_times(rr_ref[k], ri_ref[k], w_re, w_im)
            w_re, w_im = t_re + f_ref[k, 2 * s], t_im + f_ref[k, 2 * s + 1]
            per_layer.append((w_re, w_im))
        downs.append(per_layer)
    for s in range(shots):
        v_re, v_im = br_ref[s], bi_ref[s]
        for k in range(layers - 1, -1, -1):
            t_re, t_im = complex_times(rr_ref[k], ri_ref[k], v_re, v_im)
            f_re, f_im = f_ref[k, 2 * s], f_ref[k, 2 * s + 1]
            v_re, v_im = t_re + f_re, t_im + f_im
            d_re, d_im = downs[s][k]
            for part, plane in ((0, d_re + v_re - f_re), (1, d_im + v_im - f_im)):
                c = 2 * s + part
                c_ref[k, c] = plane
                x0_ref[k, pl.ds(c, 1), :] = plane[0:1, :]
                x1_ref[k, pl.ds(c, 1), :] = plane[-1:, :]
                flipped = jnp.transpose(plane)
                y0_ref[k, pl.ds(c, 1), :] = flipped[0:1, :]
                y1_ref[k, pl.ds(c, 1), :] = flipped[-1:, :]


def stencil_kernel(c_ref, lx_ref, hx_ref, ly_ref, hy_ref, o_ref):
    layers, components, width_x, width_y = c_ref.shape
    rows = lax.broadcasted_iota(jnp.int32, (width_x, width_y), 0)
    cols = lax.broadcasted_iota(jnp.int32, (width_x, width_y), 1)
    for k in range(layers):
        for c in range(components):
            plane = c_ref[k, c]
            low_x = jnp.broadcast_to(lx_ref[k, pl.ds(c, 1), :], (width_x, width_y))
            high_x = jnp.broadcast_to(hx_ref[k, pl.ds(c, 1), :], (width_x, width_y))
            low_y = jnp.transpose(jnp.broadcast_to(ly_ref[k, pl.ds(c, 1), :], (width_y, width_x)))
            high_y = jnp.transpose(jnp.broadcast_to(hy_ref[k, pl.ds(c, 1), :], (width_y, width_x)))
            next_x = jnp.where(rows == width_x - 1, high_x, pltpu.roll(plane, width_x - 1, 0))
            prev_x = jnp.where(rows == 0, low_x, pltpu.roll(plane, 1, 0))
            next_y = jnp.where(cols == width_y - 1, high_y, pltpu.roll(plane, width_y - 1, 1))
            prev_y = jnp.where(cols == 0, low_y, pltpu.roll(plane, 1, 1))
            neighbours = next_x + prev_x + next_y + prev_y
            o_ref[k, c] = plane - 0.2 * (4.0 * plane - neighbours)


def finish(fields, rate_re, rate_im, enter_re, enter_im, below_re, below_im):
    layers, components, width_x, width_y = fields.shape
    edge_x = jax.ShapeDtypeStruct((layers, components, width_y), jnp.float32)
    edge_y = jax.ShapeDtypeStruct((layers, components, width_x), jnp.float32)
    combined, x0, x1, y0, y1 = pl.pallas_call(
        sweep_kernel,
        out_shape=(jax.ShapeDtypeStruct(fields.shape, jnp.float32), edge_x, edge_x, edge_y, edge_y),
    )(fields, rate_re, rate_im, enter_re, enter_im, below_re, below_im)
    from_low_x, from_high_x = edge_pair(x1, x0, "px")
    from_low_y, from_high_y = edge_pair(y1, y0, "py")
    return pl.pallas_call(
        stencil_kernel,
        out_shape=jax.ShapeDtypeStruct(fields.shape, jnp.float32),
    )(combined, from_low_x, from_high_x, from_low_y, from_high_y)


def shards(source, phase, attenuation, pml_level, recv_values, recv_slab, recv_lateral, recv_layer):
    layers, components, width_x, width_y = source.shape
    shot_count = components // 2
    slab_count = lax.axis_size("slab")
    depth_total = layers * slab_count

    damping = attenuation + 0.5 / depth_total * pml_level.astype(jnp.float32)[None, :, :]
    amplitude = jnp.exp(-damping)
    rate_re = amplitude * jnp.cos(phase)
    rate_im = amplitude * jnp.sin(phase)

    prod_down = [(rate_re[0], rate_im[0])]
    for k in range(1, layers):
        prod_down.append(complex_times(rate_re[k], rate_im[k], *prod_down[-1]))
    levels = block_products(*prod_down[-1])

    forcing, levels = inject_receivers(
        source, recv_values, recv_slab, recv_lateral, recv_layer, levels
    )
    fields = forcing.reshape(layers, shot_count, 2, width_x, width_y)
    f_re = fields[:, :, 0]
    f_im = fields[:, :, 1]

    down = [None] * layers
    state = (f_re[0], f_im[0])
    down[0] = state
    for k in range(1, layers):
        t_re, t_im = complex_times(rate_re[k][None], rate_im[k][None], *state)
        state = (t_re + f_re[k], t_im + f_im[k])
        down[k] = state
    up = [None] * layers
    state = (f_re[layers - 1], f_im[layers - 1])
    up[layers - 1] = state
    for k in range(layers - 2, -1, -1):
        t_re, t_im = complex_times(rate_re[k][None], rate_im[k][None], *state)
        state = (t_re + f_re[k], t_im + f_im[k])
        up[k] = state

    (enter_re, enter_im), (below_re, below_im) = entering_states(down[layers - 1], up[0], levels)

    return finish(forcing, rate_re, rate_im, enter_re, enter_im, below_re, below_im)


def solution(mesh):
    in_specs = (
        P("slab", None, "px", "py"),
        P("slab", "px", "py"),
        P("slab", "px", "py"),
        P("px", "py"),
        P("px", "py", None, "slab"),
        P("px", "py", "slab", None),
        P("px", "py", "slab"),
        P("px", "py", "slab"),
    )
    out_specs = P("slab", None, "px", "py")
    return jax.shard_map(shards, mesh=mesh, in_specs=in_specs, out_specs=out_specs, check_vma=False)
```

```python
import jax
import jax.numpy as jnp
from jax import lax
from jax.sharding import PartitionSpec as P
from jax.experimental import pallas as pl
from jax.experimental.pallas import tpu as pltpu


def from_behind(array, axis, by):
    count = lax.axis_size(axis)
    pairs = [(i, i + by) for i in range(count) if 0 <= i + by < count]
    return lax.ppermute(array, axis, pairs)


def complex_times(a_re, a_im, b_re, b_im):
    return a_re * b_re - a_im * b_im, a_re * b_im + a_im * b_re


def exact_pieces(values):
    high = lax.reduce_precision(values, exponent_bits=8, mantissa_bits=7)
    rest = values - high
    middle = lax.reduce_precision(rest, exponent_bits=8, mantissa_bits=7)
    return high, middle, rest - middle


def route_kernel(rows_ref, slab_ref, out_ref):
    rows_here = slab_ref.shape[0]
    slab_count = out_ref.shape[1]
    capacity = out_ref.shape[2]
    slab = slab_ref[...]
    picked = (slab == lax.broadcasted_iota(jnp.int32, (rows_here, slab_count), 1)).astype(jnp.float32)
    earlier = (
        lax.broadcasted_iota(jnp.int32, (rows_here, rows_here), 1)
        < lax.broadcasted_iota(jnp.int32, (rows_here, rows_here), 0)
    ).astype(jnp.bfloat16)
    counts = jnp.dot(earlier, picked.astype(jnp.bfloat16), preferred_element_type=jnp.float32)
    rank = jnp.sum(counts * picked, axis=1, keepdims=True).astype(jnp.int32)
    slot = slab * capacity + rank
    spots = (
        slot == lax.broadcasted_iota(jnp.int32, (rows_here, slab_count * capacity), 1)
    ).astype(jnp.bfloat16)
    rows = rows_ref[...]
    total = None
    for piece in exact_pieces(rows):
        part = jnp.dot(piece.astype(jnp.bfloat16), spots, preferred_element_type=jnp.float32)
        total = part if total is None else total + part
    for s in range(slab_count):
        out_ref[:, s, :] = total[:, s * capacity : (s + 1) * capacity]


def inject_receivers(source, recv_values, recv_slab, recv_lateral, recv_layer, levels):
    layers, components, width_x, width_y = source.shape
    slab_count = lax.axis_size("slab")
    plane_size = width_x * width_y
    rows_here = recv_values.shape[3]
    capacity = rows_here // min(8, slab_count)
    position = recv_layer[0, 0] * plane_size + recv_lateral[0, 0]
    rows = jnp.concatenate([recv_values[0, 0], position.astype(jnp.float32)[None, :]], axis=0)
    send_rows = pl.pallas_call(
        route_kernel,
        out_shape=jax.ShapeDtypeStruct((components + 1, slab_count, capacity), jnp.float32),
    )(rows, recv_slab[0, 0])
    got_rows = lax.all_to_all(
        send_rows,
        "slab",
        split_axis=1,
        concat_axis=1,
        tiled=True,
    ).reshape(components + 1, slab_count * capacity)
    got_rows, levels = lax.optimization_barrier((got_rows, levels))
    inject_values = got_rows[:components]
    inject_places = got_rows[components].astype(jnp.int32)
    row_of = inject_places // width_y
    col_of = inject_places % width_y
    pick_rows = (
        row_of[None, :] == jnp.arange(layers * width_x, dtype=jnp.int32)[:, None]
    ).astype(jnp.bfloat16)
    pick_cols = col_of[:, None] == jnp.arange(width_y, dtype=jnp.int32)[None, :]
    pieces = jnp.stack(exact_pieces(inject_values), axis=0)
    spread = jnp.where(pick_cols[None, None, :, :], pieces[:, :, :, None], 0.0)
    spread = jnp.transpose(spread, (2, 0, 1, 3)).reshape(
        slab_count * capacity, 3 * components * width_y
    )
    added = jnp.dot(pick_rows, spread.astype(jnp.bfloat16), preferred_element_type=jnp.float32)
    added = added.reshape(layers * width_x, 3, components * width_y)
    added = (added[:, 0] + added[:, 1]) + added[:, 2]
    added = jnp.transpose(added.reshape(layers, width_x, components, width_y), (0, 2, 1, 3))
    return source + added, levels


def exchange(array, step):
    count = lax.axis_size("slab")
    return lax.ppermute(array, "slab", [(i, i ^ step) for i in range(count)])


def block_products(a_re, a_im):
    slab_count = lax.axis_size("slab")
    here = lax.axis_index("slab")
    one = jnp.ones_like(a_re)
    zero = jnp.zeros_like(a_re)
    total = (a_re, a_im)
    below = (one, zero)
    above = (one, zero)
    levels = []
    step = 1
    while 2 * step < slab_count:
        got = exchange(jnp.stack(total, axis=0), step)
        partner = (got[0], got[1])
        levels.append((total, partner, below, above))
        lower = (here & step) == 0
        grown_below = complex_times(*below, *partner)
        grown_above = complex_times(*above, *partner)
        below = (jnp.where(lower, below[0], grown_below[0]), jnp.where(lower, below[1], grown_below[1]))
        above = (jnp.where(lower, grown_above[0], above[0]), jnp.where(lower, grown_above[1], above[1]))
        total = complex_times(*total, *partner)
        step *= 2
    levels.append((None, None, below, above))
    return levels


def entering_states(down_b, up_b, levels):
    slab_count = lax.axis_size("slab")
    here = lax.axis_index("slab")
    shots = down_b[0].shape[0]
    before = (jnp.zeros_like(down_b[0]), jnp.zeros_like(down_b[1]))
    after = (jnp.zeros_like(up_b[0]), jnp.zeros_like(up_b[1]))
    step = 1
    level = 0
    while step < slab_count:
        lower = (here & step) == 0
        total, partner, below, above = levels[level]
        if 2 * step < slab_count:
            got = exchange(jnp.concatenate([*down_b, *up_b], axis=0), step)
            pd = (got[:shots], got[shots : 2 * shots])
            pu = (got[2 * shots : 3 * shots], got[3 * shots :])
            t_re, t_im = total[0][None], total[1][None]
            q_re, q_im = partner[0][None], partner[1][None]
            first = (jnp.where(lower, q_re, t_re), jnp.where(lower, q_im, t_im))
            inner = (jnp.where(lower, down_b[0], pd[0]), jnp.where(lower, down_b[1], pd[1]))
            outer = (jnp.where(lower, pd[0], down_b[0]), jnp.where(lower, pd[1], down_b[1]))
            m_re, m_im = complex_times(*first, *inner)
            new_down = (m_re + outer[0], m_im + outer[1])
            first = (jnp.where(lower, t_re, q_re), jnp.where(lower, t_im, q_im))
            inner = (jnp.where(lower, pu[0], up_b[0]), jnp.where(lower, pu[1], up_b[1]))
            outer = (jnp.where(lower, up_b[0], pu[0]), jnp.where(lower, up_b[1], pu[1]))
            m_re, m_im = complex_times(*first, *inner)
            new_up = (m_re + outer[0], m_im + outer[1])
        else:
            send = jnp.concatenate(
                [jnp.where(lower, down_b[0], up_b[0]), jnp.where(lower, down_b[1], up_b[1])], axis=0
            )
            got = exchange(send, step)
            pd = (got[:shots], got[shots:])
            pu = pd
        g_re, g_im = complex_times(below[0][None], below[1][None], *pd)
        before = (
            jnp.where(lower, before[0], g_re + before[0]),
            jnp.where(lower, before[1], g_im + before[1]),
        )
        g_re, g_im = complex_times(above[0][None], above[1][None], *pu)
        after = (
            jnp.where(lower, g_re + after[0], after[0]),
            jnp.where(lower, g_im + after[1], after[1]),
        )
        if 2 * step < slab_count:
            down_b, up_b = new_down, new_up
        step *= 2
        level += 1
    return before, after


def edge_pair(last, first, axis):
    count = lax.axis_size(axis)
    if count == 2:
        here = lax.axis_index(axis)
        got = lax.ppermute(jnp.where(here == 0, last, first), axis, [(0, 1), (1, 0)])
        zero = jnp.zeros_like(got)
        return jnp.where(here == 1, got, zero), jnp.where(here == 0, got, zero)
    return from_behind(last, axis, 1), from_behind(first, axis, -1)


def sweep_kernel(f_ref, rr_ref, ri_ref, er_ref, ei_ref, br_ref, bi_ref,
                 c_ref, x0_ref, x1_ref, y0_ref, y1_ref):
    layers = f_ref.shape[0]
    shots = er_ref.shape[0]
    downs = []
    for s in range(shots):
        w_re, w_im = er_ref[s], ei_ref[s]
        per_layer = []
        for k in range(layers):
            t_re, t_im = complex_times(rr_ref[k], ri_ref[k], w_re, w_im)
            w_re, w_im = t_re + f_ref[k, 2 * s], t_im + f_ref[k, 2 * s + 1]
            per_layer.append((w_re, w_im))
        downs.append(per_layer)
    for s in range(shots):
        v_re, v_im = br_ref[s], bi_ref[s]
        for k in range(layers - 1, -1, -1):
            t_re, t_im = complex_times(rr_ref[k], ri_ref[k], v_re, v_im)
            f_re, f_im = f_ref[k, 2 * s], f_ref[k, 2 * s + 1]
            v_re, v_im = t_re + f_re, t_im + f_im
            d_re, d_im = downs[s][k]
            for part, plane in ((0, d_re + v_re - f_re), (1, d_im + v_im - f_im)):
                c = 2 * s + part
                c_ref[k, c] = plane
                x0_ref[k, pl.ds(c, 1), :] = plane[0:1, :]
                x1_ref[k, pl.ds(c, 1), :] = plane[-1:, :]
                flipped = jnp.transpose(plane)
                y0_ref[k, pl.ds(c, 1), :] = flipped[0:1, :]
                y1_ref[k, pl.ds(c, 1), :] = flipped[-1:, :]


def stencil_kernel(c_ref, lx_ref, hx_ref, ly_ref, hy_ref, o_ref):
    layers, components, width_x, width_y = c_ref.shape
    rows = lax.broadcasted_iota(jnp.int32, (width_x, width_y), 0)
    cols = lax.broadcasted_iota(jnp.int32, (width_x, width_y), 1)
    for k in range(layers):
        for c in range(components):
            plane = c_ref[k, c]
            low_x = jnp.broadcast_to(lx_ref[k, pl.ds(c, 1), :], (width_x, width_y))
            high_x = jnp.broadcast_to(hx_ref[k, pl.ds(c, 1), :], (width_x, width_y))
            low_y = jnp.transpose(jnp.broadcast_to(ly_ref[k, pl.ds(c, 1), :], (width_y, width_x)))
            high_y = jnp.transpose(jnp.broadcast_to(hy_ref[k, pl.ds(c, 1), :], (width_y, width_x)))
            next_x = jnp.where(rows == width_x - 1, high_x, pltpu.roll(plane, width_x - 1, 0))
            prev_x = jnp.where(rows == 0, low_x, pltpu.roll(plane, 1, 0))
            next_y = jnp.where(cols == width_y - 1, high_y, pltpu.roll(plane, width_y - 1, 1))
            prev_y = jnp.where(cols == 0, low_y, pltpu.roll(plane, 1, 1))
            neighbours = next_x + prev_x + next_y + prev_y
            o_ref[k, c] = plane - 0.2 * (4.0 * plane - neighbours)


def finish(fields, rate_re, rate_im, enter_re, enter_im, below_re, below_im):
    layers, components, width_x, width_y = fields.shape
    edge_x = jax.ShapeDtypeStruct((layers, components, width_y), jnp.float32)
    edge_y = jax.ShapeDtypeStruct((layers, components, width_x), jnp.float32)
    combined, x0, x1, y0, y1 = pl.pallas_call(
        sweep_kernel,
        out_shape=(jax.ShapeDtypeStruct(fields.shape, jnp.float32), edge_x, edge_x, edge_y, edge_y),
    )(fields, rate_re, rate_im, enter_re, enter_im, below_re, below_im)
    from_low_x, from_high_x = edge_pair(x1, x0, "px")
    from_low_y, from_high_y = edge_pair(y1, y0, "py")
    return pl.pallas_call(
        stencil_kernel,
        out_shape=jax.ShapeDtypeStruct(fields.shape, jnp.float32),
    )(combined, from_low_x, from_high_x, from_low_y, from_high_y)


def shards(source, phase, attenuation, pml_level, recv_values, recv_slab, recv_lateral, recv_layer):
    layers, components, width_x, width_y = source.shape
    shot_count = components // 2
    slab_count = lax.axis_size("slab")
    depth_total = layers * slab_count

    damping = attenuation + 0.5 / depth_total * pml_level.astype(jnp.float32)[None, :, :]
    amplitude = jnp.exp(-damping)
    rate_re = amplitude * jnp.cos(phase)
    rate_im = amplitude * jnp.sin(phase)

    prod_down = [(rate_re[0], rate_im[0])]
    for k in range(1, layers):
        prod_down.append(complex_times(rate_re[k], rate_im[k], *prod_down[-1]))
    levels = block_products(*prod_down[-1])

    forcing, levels = inject_receivers(
        source, recv_values, recv_slab, recv_lateral, recv_layer, levels
    )
    fields = forcing.reshape(layers, shot_count, 2, width_x, width_y)
    f_re = fields[:, :, 0]
    f_im = fields[:, :, 1]

    down = [None] * layers
    state = (f_re[0], f_im[0])
    down[0] = state
    for k in range(1, layers):
        t_re, t_im = complex_times(rate_re[k][None], rate_im[k][None], *state)
        state = (t_re + f_re[k], t_im + f_im[k])
        down[k] = state
    up = [None] * layers
    state = (f_re[layers - 1], f_im[layers - 1])
    up[layers - 1] = state
    for k in range(layers - 2, -1, -1):
        t_re, t_im = complex_times(rate_re[k][None], rate_im[k][None], *state)
        state = (t_re + f_re[k], t_im + f_im[k])
        up[k] = state

    (enter_re, enter_im), (below_re, below_im) = entering_states(down[layers - 1], up[0], levels)

    return finish(forcing, rate_re, rate_im, enter_re, enter_im, below_re, below_im)


def solution(mesh):
    in_specs = (
        P("slab", None, "px", "py"),
        P("slab", "px", "py"),
        P("slab", "px", "py"),
        P("px", "py"),
        P("px", "py", None, "slab"),
        P("px", "py", "slab", None),
        P("px", "py", "slab"),
        P("px", "py", "slab"),
    )
    out_specs = P("slab", None, "px", "py")
    return jax.shard_map(shards, mesh=mesh, in_specs=in_specs, out_specs=out_specs, check_vma=False)
```

```python
import jax
import jax.numpy as jnp
from jax import lax
from jax.sharding import PartitionSpec as P
from jax.experimental import pallas as pl
from jax.experimental.pallas import tpu as pltpu


def from_behind(array, axis, by):
    count = lax.axis_size(axis)
    pairs = [(i, i + by) for i in range(count) if 0 <= i + by < count]
    return lax.ppermute(array, axis, pairs)


def complex_times(a_re, a_im, b_re, b_im):
    return a_re * b_re - a_im * b_im, a_re * b_im + a_im * b_re


def route_rows(source, recv_values, recv_slab, recv_lateral, recv_layer):
    layers, components, width_x, width_y = source.shape
    slab_count = lax.axis_size("slab")
    plane_size = width_x * width_y
    rows_here = recv_values.shape[3]
    capacity = rows_here // min(8, slab_count)
    values = recv_values[0, 0]
    target_slab = recv_slab[0, 0, :, 0]
    position = recv_layer[0, 0] * plane_size + recv_lateral[0, 0]
    one_hot = (target_slab[:, None] == jnp.arange(slab_count, dtype=jnp.int32)[None, :]).astype(
        jnp.int32
    )
    ranking = jnp.sum((jnp.cumsum(one_hot, axis=0) - one_hot) * one_hot, axis=1)
    target_slot = target_slab * capacity + ranking
    rows = jnp.concatenate([values, position.astype(jnp.float32)[None, :]], axis=0)
    send_rows = (
        jnp.zeros((components + 1, slab_count * capacity), jnp.float32).at[:, target_slot].set(rows)
    )
    return send_rows.reshape(components + 1, slab_count, capacity)


def inject_receivers(source, send_rows):
    layers, components, width_x, width_y = source.shape
    slab_count = lax.axis_size("slab")
    capacity = send_rows.shape[2]
    got_rows = lax.all_to_all(
        send_rows,
        "slab",
        split_axis=1,
        concat_axis=1,
        tiled=True,
    ).reshape(components + 1, slab_count * capacity)
    inject_values = got_rows[:components]
    inject_places = got_rows[components].astype(jnp.int32)
    row_of = inject_places // width_y
    col_of = inject_places % width_y
    pick_rows = (
        row_of[None, :] == jnp.arange(layers * width_x, dtype=jnp.int32)[:, None]
    ).astype(jnp.bfloat16)
    pick_cols = col_of[:, None] == jnp.arange(width_y, dtype=jnp.int32)[None, :]
    high = lax.reduce_precision(inject_values, exponent_bits=8, mantissa_bits=7)
    rest = inject_values - high
    middle = lax.reduce_precision(rest, exponent_bits=8, mantissa_bits=7)
    low = rest - middle
    pieces = jnp.stack([high, middle, low], axis=0)
    spread = jnp.where(pick_cols[None, None, :, :], pieces[:, :, :, None], 0.0)
    spread = jnp.transpose(spread, (2, 0, 1, 3)).reshape(
        slab_count * capacity, 3 * components * width_y
    )
    added = jnp.dot(pick_rows, spread.astype(jnp.bfloat16), preferred_element_type=jnp.float32)
    added = added.reshape(layers * width_x, 3, components * width_y)
    added = (added[:, 0] + added[:, 1]) + added[:, 2]
    added = jnp.transpose(added.reshape(layers, width_x, components, width_y), (0, 2, 1, 3))
    return source + added


def exchange(array, step):
    count = lax.axis_size("slab")
    return lax.ppermute(array, "slab", [(i, i ^ step) for i in range(count)])


def entering_states(down_b, up_b, a_re, a_im):
    slab_count = lax.axis_size("slab")
    here = lax.axis_index("slab")
    shots = down_b[0].shape[0]
    before = (jnp.zeros_like(down_b[0]), jnp.zeros_like(down_b[1]))
    after = (jnp.zeros_like(up_b[0]), jnp.zeros_like(up_b[1]))
    one = jnp.ones_like(a_re)
    zero = jnp.zeros_like(a_re)
    total = (a_re, a_im)
    below = (one, zero)
    above = (one, zero)
    step = 1
    while step < slab_count:
        lower = (here & step) == 0
        if 2 * step < slab_count:
            got = exchange(
                jnp.concatenate([total[0][None], total[1][None], *down_b, *up_b], axis=0), step
            )
            partner = (got[0], got[1])
            got = got[2:]
            pd = (got[:shots], got[shots : 2 * shots])
            pu = (got[2 * shots : 3 * shots], got[3 * shots :])
            t_re, t_im = total[0][None], total[1][None]
            q_re, q_im = partner[0][None], partner[1][None]
            first = (jnp.where(lower, q_re, t_re), jnp.where(lower, q_im, t_im))
            inner = (jnp.where(lower, down_b[0], pd[0]), jnp.where(lower, down_b[1], pd[1]))
            outer = (jnp.where(lower, pd[0], down_b[0]), jnp.where(lower, pd[1], down_b[1]))
            m_re, m_im = complex_times(*first, *inner)
            new_down = (m_re + outer[0], m_im + outer[1])
            first = (jnp.where(lower, t_re, q_re), jnp.where(lower, t_im, q_im))
            inner = (jnp.where(lower, pu[0], up_b[0]), jnp.where(lower, pu[1], up_b[1]))
            outer = (jnp.where(lower, up_b[0], pu[0]), jnp.where(lower, up_b[1], pu[1]))
            m_re, m_im = complex_times(*first, *inner)
            new_up = (m_re + outer[0], m_im + outer[1])
        else:
            send = jnp.concatenate(
                [jnp.where(lower, down_b[0], up_b[0]), jnp.where(lower, down_b[1], up_b[1])], axis=0
            )
            got = exchange(send, step)
            pd = (got[:shots], got[shots:])
            pu = pd
        g_re, g_im = complex_times(below[0][None], below[1][None], *pd)
        before = (
            jnp.where(lower, before[0], g_re + before[0]),
            jnp.where(lower, before[1], g_im + before[1]),
        )
        g_re, g_im = complex_times(above[0][None], above[1][None], *pu)
        after = (
            jnp.where(lower, g_re + after[0], after[0]),
            jnp.where(lower, g_im + after[1], after[1]),
        )
        if 2 * step < slab_count:
            down_b, up_b = new_down, new_up
            grown_below = complex_times(*below, *partner)
            grown_above = complex_times(*above, *partner)
            below = (
                jnp.where(lower, below[0], grown_below[0]),
                jnp.where(lower, below[1], grown_below[1]),
            )
            above = (
                jnp.where(lower, grown_above[0], above[0]),
                jnp.where(lower, grown_above[1], above[1]),
            )
            total = complex_times(*total, *partner)
        step *= 2
    return before, after


def edge_pair(last, first, axis):
    count = lax.axis_size(axis)
    if count == 2:
        here = lax.axis_index(axis)
        got = lax.ppermute(jnp.where(here == 0, last, first), axis, [(0, 1), (1, 0)])
        zero = jnp.zeros_like(got)
        return jnp.where(here == 1, got, zero), jnp.where(here == 0, got, zero)
    return from_behind(last, axis, 1), from_behind(first, axis, -1)


def sweep_kernel(f_ref, rr_ref, ri_ref, er_ref, ei_ref, br_ref, bi_ref,
                 c_ref, x0_ref, x1_ref, y0_ref, y1_ref):
    layers = f_ref.shape[0]
    shots = er_ref.shape[0]
    downs = []
    for s in range(shots):
        w_re, w_im = er_ref[s], ei_ref[s]
        per_layer = []
        for k in range(layers):
            t_re, t_im = complex_times(rr_ref[k], ri_ref[k], w_re, w_im)
            w_re, w_im = t_re + f_ref[k, 2 * s], t_im + f_ref[k, 2 * s + 1]
            per_layer.append((w_re, w_im))
        downs.append(per_layer)
    for s in range(shots):
        v_re, v_im = br_ref[s], bi_ref[s]
        for k in range(layers - 1, -1, -1):
            t_re, t_im = complex_times(rr_ref[k], ri_ref[k], v_re, v_im)
            f_re, f_im = f_ref[k, 2 * s], f_ref[k, 2 * s + 1]
            v_re, v_im = t_re + f_re, t_im + f_im
            d_re, d_im = downs[s][k]
            for part, plane in ((0, d_re + v_re - f_re), (1, d_im + v_im - f_im)):
                c = 2 * s + part
                c_ref[k, c] = plane
                x0_ref[k, pl.ds(c, 1), :] = plane[0:1, :]
                x1_ref[k, pl.ds(c, 1), :] = plane[-1:, :]
                flipped = jnp.transpose(plane)
                y0_ref[k, pl.ds(c, 1), :] = flipped[0:1, :]
                y1_ref[k, pl.ds(c, 1), :] = flipped[-1:, :]


def stencil_kernel(c_ref, lx_ref, hx_ref, ly_ref, hy_ref, o_ref):
    layers, components, width_x, width_y = c_ref.shape
    rows = lax.broadcasted_iota(jnp.int32, (width_x, width_y), 0)
    cols = lax.broadcasted_iota(jnp.int32, (width_x, width_y), 1)
    for k in range(layers):
        for c in range(components):
            plane = c_ref[k, c]
            low_x = jnp.broadcast_to(lx_ref[k, pl.ds(c, 1), :], (width_x, width_y))
            high_x = jnp.broadcast_to(hx_ref[k, pl.ds(c, 1), :], (width_x, width_y))
            low_y = jnp.transpose(jnp.broadcast_to(ly_ref[k, pl.ds(c, 1), :], (width_y, width_x)))
            high_y = jnp.transpose(jnp.broadcast_to(hy_ref[k, pl.ds(c, 1), :], (width_y, width_x)))
            next_x = jnp.where(rows == width_x - 1, high_x, pltpu.roll(plane, width_x - 1, 0))
            prev_x = jnp.where(rows == 0, low_x, pltpu.roll(plane, 1, 0))
            next_y = jnp.where(cols == width_y - 1, high_y, pltpu.roll(plane, width_y - 1, 1))
            prev_y = jnp.where(cols == 0, low_y, pltpu.roll(plane, 1, 1))
            neighbours = next_x + prev_x + next_y + prev_y
            o_ref[k, c] = plane - 0.2 * (4.0 * plane - neighbours)


def finish(fields, rate_re, rate_im, enter_re, enter_im, below_re, below_im):
    layers, components, width_x, width_y = fields.shape
    edge_x = jax.ShapeDtypeStruct((layers, components, width_y), jnp.float32)
    edge_y = jax.ShapeDtypeStruct((layers, components, width_x), jnp.float32)
    combined, x0, x1, y0, y1 = pl.pallas_call(
        sweep_kernel,
        out_shape=(jax.ShapeDtypeStruct(fields.shape, jnp.float32), edge_x, edge_x, edge_y, edge_y),
    )(fields, rate_re, rate_im, enter_re, enter_im, below_re, below_im)
    from_low_x, from_high_x = edge_pair(x1, x0, "px")
    from_low_y, from_high_y = edge_pair(y1, y0, "py")
    return pl.pallas_call(
        stencil_kernel,
        out_shape=jax.ShapeDtypeStruct(fields.shape, jnp.float32),
    )(combined, from_low_x, from_high_x, from_low_y, from_high_y)


def shards(source, phase, attenuation, pml_level, recv_values, recv_slab, recv_lateral, recv_layer):
    layers, components, width_x, width_y = source.shape
    shot_count = components // 2
    slab_count = lax.axis_size("slab")
    depth_total = layers * slab_count

    send_rows = route_rows(source, recv_values, recv_slab, recv_lateral, recv_layer)
    damping = attenuation + 0.5 / depth_total * pml_level.astype(jnp.float32)[None, :, :]
    amplitude = jnp.exp(-damping)
    rate_re = amplitude * jnp.cos(phase)
    rate_im = amplitude * jnp.sin(phase)

    prod_down = [(rate_re[0], rate_im[0])]
    for k in range(1, layers):
        prod_down.append(complex_times(rate_re[k], rate_im[k], *prod_down[-1]))

    forcing = inject_receivers(source, send_rows)
    fields = forcing.reshape(layers, shot_count, 2, width_x, width_y)
    f_re = fields[:, :, 0]
    f_im = fields[:, :, 1]

    down = [None] * layers
    state = (f_re[0], f_im[0])
    down[0] = state
    for k in range(1, layers):
        t_re, t_im = complex_times(rate_re[k][None], rate_im[k][None], *state)
        state = (t_re + f_re[k], t_im + f_im[k])
        down[k] = state
    up = [None] * layers
    state = (f_re[layers - 1], f_im[layers - 1])
    up[layers - 1] = state
    for k in range(layers - 2, -1, -1):
        t_re, t_im = complex_times(rate_re[k][None], rate_im[k][None], *state)
        state = (t_re + f_re[k], t_im + f_im[k])
        up[k] = state

    (enter_re, enter_im), (below_re, below_im) = entering_states(
        down[layers - 1], up[0], *prod_down[-1]
    )

    return finish(forcing, rate_re, rate_im, enter_re, enter_im, below_re, below_im)


def solution(mesh):
    in_specs = (
        P("slab", None, "px", "py"),
        P("slab", "px", "py"),
        P("slab", "px", "py"),
        P("px", "py"),
        P("px", "py", None, "slab"),
        P("px", "py", "slab", None),
        P("px", "py", "slab"),
        P("px", "py", "slab"),
    )
    out_specs = P("slab", None, "px", "py")
    return jax.shard_map(shards, mesh=mesh, in_specs=in_specs, out_specs=out_specs, check_vma=False)
```

```python
import jax
import jax.numpy as jnp
from jax import lax
from jax.sharding import PartitionSpec as P
from jax.experimental import pallas as pl
from jax.experimental.pallas import tpu as pltpu


def from_behind(array, axis, by):
    count = lax.axis_size(axis)
    pairs = [(i, i + by) for i in range(count) if 0 <= i + by < count]
    return lax.ppermute(array, axis, pairs)


def complex_times(a_re, a_im, b_re, b_im):
    return a_re * b_re - a_im * b_im, a_re * b_im + a_im * b_re


def inject_receivers(source, recv_values, recv_slab, recv_lateral, recv_layer, levels):
    layers, components, width_x, width_y = source.shape
    slab_count = lax.axis_size("slab")
    plane_size = width_x * width_y
    rows_here = recv_values.shape[3]
    capacity = rows_here // min(8, slab_count)
    values = recv_values[0, 0]
    target_slab = recv_slab[0, 0, :, 0]
    position = recv_layer[0, 0] * plane_size + recv_lateral[0, 0]
    one_hot = (target_slab[:, None] == jnp.arange(slab_count, dtype=jnp.int32)[None, :]).astype(
        jnp.int32
    )
    ranking = jnp.sum((jnp.cumsum(one_hot, axis=0) - one_hot) * one_hot, axis=1)
    target_slot = target_slab * capacity + ranking
    rows = jnp.concatenate([values, position.astype(jnp.float32)[None, :]], axis=0)
    send_rows = (
        jnp.zeros((components + 1, slab_count * capacity), jnp.float32).at[:, target_slot].set(rows)
    )
    got_rows = lax.all_to_all(
        send_rows.reshape(components + 1, slab_count, capacity),
        "slab",
        split_axis=1,
        concat_axis=1,
        tiled=True,
    ).reshape(components + 1, slab_count * capacity)
    got_rows, levels = lax.optimization_barrier((got_rows, levels))
    inject_values = got_rows[:components]
    inject_places = got_rows[components].astype(jnp.int32)
    row_of = inject_places // width_y
    col_of = inject_places % width_y
    pick_rows = (
        row_of[None, :] == jnp.arange(layers * width_x, dtype=jnp.int32)[:, None]
    ).astype(jnp.bfloat16)
    pick_cols = col_of[:, None] == jnp.arange(width_y, dtype=jnp.int32)[None, :]
    high = lax.reduce_precision(inject_values, exponent_bits=8, mantissa_bits=7)
    rest = inject_values - high
    middle = lax.reduce_precision(rest, exponent_bits=8, mantissa_bits=7)
    low = rest - middle
    pieces = jnp.stack([high, middle, low], axis=0)
    spread = jnp.where(pick_cols[None, None, :, :], pieces[:, :, :, None], 0.0)
    spread = jnp.transpose(spread, (2, 0, 1, 3)).reshape(
        slab_count * capacity, 3 * components * width_y
    )
    added = jnp.dot(pick_rows, spread.astype(jnp.bfloat16), preferred_element_type=jnp.float32)
    added = added.reshape(layers * width_x, 3, components * width_y)
    added = (added[:, 0] + added[:, 1]) + added[:, 2]
    added = jnp.transpose(added.reshape(layers, width_x, components, width_y), (0, 2, 1, 3))
    return source + added, levels


def exchange(array, step):
    count = lax.axis_size("slab")
    return lax.ppermute(array, "slab", [(i, i ^ step) for i in range(count)])


def block_products(a_re, a_im):
    slab_count = lax.axis_size("slab")
    here = lax.axis_index("slab")
    one = jnp.ones_like(a_re)
    zero = jnp.zeros_like(a_re)
    total = (a_re, a_im)
    below = (one, zero)
    above = (one, zero)
    levels = []
    step = 1
    while 2 * step < slab_count:
        got = exchange(jnp.stack(total, axis=0), step)
        partner = (got[0], got[1])
        levels.append((total, partner, below, above))
        lower = (here & step) == 0
        grown_below = complex_times(*below, *partner)
        grown_above = complex_times(*above, *partner)
        below = (jnp.where(lower, below[0], grown_below[0]), jnp.where(lower, below[1], grown_below[1]))
        above = (jnp.where(lower, grown_above[0], above[0]), jnp.where(lower, grown_above[1], above[1]))
        total = complex_times(*total, *partner)
        step *= 2
    levels.append((None, None, below, above))
    return levels


def entering_states(down_b, up_b, levels, defer_last=False):
    slab_count = lax.axis_size("slab")
    here = lax.axis_index("slab")
    shots = down_b[0].shape[0]
    before = (jnp.zeros_like(down_b[0]), jnp.zeros_like(down_b[1]))
    after = (jnp.zeros_like(up_b[0]), jnp.zeros_like(up_b[1]))
    step = 1
    level = 0
    while step < slab_count:
        lower = (here & step) == 0
        total, partner, below, above = levels[level]
        if 2 * step < slab_count:
            got = exchange(jnp.concatenate([*down_b, *up_b], axis=0), step)
            pd = (got[:shots], got[shots : 2 * shots])
            pu = (got[2 * shots : 3 * shots], got[3 * shots :])
            t_re, t_im = total[0][None], total[1][None]
            q_re, q_im = partner[0][None], partner[1][None]
            first = (jnp.where(lower, q_re, t_re), jnp.where(lower, q_im, t_im))
            inner = (jnp.where(lower, down_b[0], pd[0]), jnp.where(lower, down_b[1], pd[1]))
            outer = (jnp.where(lower, pd[0], down_b[0]), jnp.where(lower, pd[1], down_b[1]))
            m_re, m_im = complex_times(*first, *inner)
            new_down = (m_re + outer[0], m_im + outer[1])
            first = (jnp.where(lower, t_re, q_re), jnp.where(lower, t_im, q_im))
            inner = (jnp.where(lower, pu[0], up_b[0]), jnp.where(lower, pu[1], up_b[1]))
            outer = (jnp.where(lower, up_b[0], pu[0]), jnp.where(lower, up_b[1], pu[1]))
            m_re, m_im = complex_times(*first, *inner)
            new_up = (m_re + outer[0], m_im + outer[1])
        else:
            send = jnp.concatenate(
                [jnp.where(lower, down_b[0], up_b[0]), jnp.where(lower, down_b[1], up_b[1])], axis=0
            )
            got = exchange(send, step)
            if defer_last:
                return before, after, got, below, above, lower
            pd = (got[:shots], got[shots:])
            pu = pd
        g_re, g_im = complex_times(below[0][None], below[1][None], *pd)
        before = (
            jnp.where(lower, before[0], g_re + before[0]),
            jnp.where(lower, before[1], g_im + before[1]),
        )
        g_re, g_im = complex_times(above[0][None], above[1][None], *pu)
        after = (
            jnp.where(lower, g_re + after[0], after[0]),
            jnp.where(lower, g_im + after[1], after[1]),
        )
        if 2 * step < slab_count:
            down_b, up_b = new_down, new_up
        step *= 2
        level += 1
    if defer_last:
        return before, after, None, None, None, None
    return before, after


def edge_pair(last, first, axis):
    count = lax.axis_size(axis)
    if count == 2:
        here = lax.axis_index(axis)
        got = lax.ppermute(jnp.where(here == 0, last, first), axis, [(0, 1), (1, 0)])
        zero = jnp.zeros_like(got)
        return jnp.where(here == 1, got, zero), jnp.where(here == 0, got, zero)
    return from_behind(last, axis, 1), from_behind(first, axis, -1)


def sweep_kernel(f_ref, rr_ref, ri_ref, er_ref, ei_ref, br_ref, bi_ref,
                 c_ref, x0_ref, x1_ref, y0_ref, y1_ref):
    layers = f_ref.shape[0]
    shots = er_ref.shape[0]
    downs = []
    for s in range(shots):
        w_re, w_im = er_ref[s], ei_ref[s]
        per_layer = []
        for k in range(layers):
            t_re, t_im = complex_times(rr_ref[k], ri_ref[k], w_re, w_im)
            w_re, w_im = t_re + f_ref[k, 2 * s], t_im + f_ref[k, 2 * s + 1]
            per_layer.append((w_re, w_im))
        downs.append(per_layer)
    for s in range(shots):
        v_re, v_im = br_ref[s], bi_ref[s]
        for k in range(layers - 1, -1, -1):
            t_re, t_im = complex_times(rr_ref[k], ri_ref[k], v_re, v_im)
            f_re, f_im = f_ref[k, 2 * s], f_ref[k, 2 * s + 1]
            v_re, v_im = t_re + f_re, t_im + f_im
            d_re, d_im = downs[s][k]
            for part, plane in ((0, d_re + v_re - f_re), (1, d_im + v_im - f_im)):
                c = 2 * s + part
                c_ref[k, c] = plane
                x0_ref[k, pl.ds(c, 1), :] = plane[0:1, :]
                x1_ref[k, pl.ds(c, 1), :] = plane[-1:, :]
                flipped = jnp.transpose(plane)
                y0_ref[k, pl.ds(c, 1), :] = flipped[0:1, :]
                y1_ref[k, pl.ds(c, 1), :] = flipped[-1:, :]


def stencil_kernel(c_ref, lx_ref, hx_ref, ly_ref, hy_ref, o_ref):
    layers, components, width_x, width_y = c_ref.shape
    rows = lax.broadcasted_iota(jnp.int32, (width_x, width_y), 0)
    cols = lax.broadcasted_iota(jnp.int32, (width_x, width_y), 1)
    for k in range(layers):
        for c in range(components):
            plane = c_ref[k, c]
            low_x = jnp.broadcast_to(lx_ref[k, pl.ds(c, 1), :], (width_x, width_y))
            high_x = jnp.broadcast_to(hx_ref[k, pl.ds(c, 1), :], (width_x, width_y))
            low_y = jnp.transpose(jnp.broadcast_to(ly_ref[k, pl.ds(c, 1), :], (width_y, width_x)))
            high_y = jnp.transpose(jnp.broadcast_to(hy_ref[k, pl.ds(c, 1), :], (width_y, width_x)))
            next_x = jnp.where(rows == width_x - 1, high_x, pltpu.roll(plane, width_x - 1, 0))
            prev_x = jnp.where(rows == 0, low_x, pltpu.roll(plane, 1, 0))
            next_y = jnp.where(cols == width_y - 1, high_y, pltpu.roll(plane, width_y - 1, 1))
            prev_y = jnp.where(cols == 0, low_y, pltpu.roll(plane, 1, 1))
            neighbours = next_x + prev_x + next_y + prev_y
            o_ref[k, c] = plane - 0.2 * (4.0 * plane - neighbours)


def finish(fields, rate_re, rate_im, enter_re, enter_im, below_re, below_im):
    layers, components, width_x, width_y = fields.shape
    edge_x = jax.ShapeDtypeStruct((layers, components, width_y), jnp.float32)
    edge_y = jax.ShapeDtypeStruct((layers, components, width_x), jnp.float32)
    combined, x0, x1, y0, y1 = pl.pallas_call(
        sweep_kernel,
        out_shape=(jax.ShapeDtypeStruct(fields.shape, jnp.float32), edge_x, edge_x, edge_y, edge_y),
    )(fields, rate_re, rate_im, enter_re, enter_im, below_re, below_im)
    from_low_x, from_high_x = edge_pair(x1, x0, "px")
    from_low_y, from_high_y = edge_pair(y1, y0, "py")
    return pl.pallas_call(
        stencil_kernel,
        out_shape=jax.ShapeDtypeStruct(fields.shape, jnp.float32),
    )(combined, from_low_x, from_high_x, from_low_y, from_high_y)


def last_sweep_kernel(flag_ref, f_ref, rr_ref, ri_ref, br_ref, bi_ref, ar_ref, ai_ref,
                      lr_ref, li_ref, hr_ref, hi_ref, got_ref, c_ref, sx_ref, sy_ref):
    layers = f_ref.shape[0]
    shots = br_ref.shape[0]
    lower = flag_ref[0] == 1
    first_x = flag_ref[1] == 0
    first_y = flag_ref[2] == 0
    for s in range(shots):
        p_re, p_im = got_ref[s], got_ref[shots + s]
        g_re, g_im = complex_times(lr_ref[...], li_ref[...], p_re, p_im)
        w_re = jnp.where(lower, br_ref[s], g_re + br_ref[s])
        w_im = jnp.where(lower, bi_ref[s], g_im + bi_ref[s])
        g_re, g_im = complex_times(hr_ref[...], hi_ref[...], p_re, p_im)
        v_re = jnp.where(lower, g_re + ar_ref[s], ar_ref[s])
        v_im = jnp.where(lower, g_im + ai_ref[s], ai_ref[s])
        downs = []
        for k in range(layers):
            t_re, t_im = complex_times(rr_ref[k], ri_ref[k], w_re, w_im)
            w_re, w_im = t_re + f_ref[k, 2 * s], t_im + f_ref[k, 2 * s + 1]
            downs.append((w_re, w_im))
        for k in range(layers - 1, -1, -1):
            t_re, t_im = complex_times(rr_ref[k], ri_ref[k], v_re, v_im)
            f_re, f_im = f_ref[k, 2 * s], f_ref[k, 2 * s + 1]
            v_re, v_im = t_re + f_re, t_im + f_im
            d_re, d_im = downs[k]
            for part, plane in ((0, d_re + v_re - f_re), (1, d_im + v_im - f_im)):
                c = 2 * s + part
                c_ref[k, c] = plane
                sx_ref[k, pl.ds(c, 1), :] = jnp.where(first_x, plane[-1:, :], plane[0:1, :])
                flipped = jnp.transpose(plane)
                sy_ref[k, pl.ds(c, 1), :] = jnp.where(first_y, flipped[-1:, :], flipped[0:1, :])


def paired_stencil_kernel(flag_ref, c_ref, gx_ref, gy_ref, o_ref):
    layers, components, width_x, width_y = c_ref.shape
    rows = lax.broadcasted_iota(jnp.int32, (width_x, width_y), 0)
    cols = lax.broadcasted_iota(jnp.int32, (width_x, width_y), 1)
    first_x = flag_ref[1] == 0
    first_y = flag_ref[2] == 0
    for k in range(layers):
        for c in range(components):
            plane = c_ref[k, c]
            edge_x = gx_ref[k, pl.ds(c, 1), :]
            edge_y = gy_ref[k, pl.ds(c, 1), :]
            none_x = jnp.zeros_like(edge_x)
            none_y = jnp.zeros_like(edge_y)
            low_x = jnp.broadcast_to(jnp.where(first_x, none_x, edge_x), (width_x, width_y))
            high_x = jnp.broadcast_to(jnp.where(first_x, edge_x, none_x), (width_x, width_y))
            low_y = jnp.transpose(
                jnp.broadcast_to(jnp.where(first_y, none_y, edge_y), (width_y, width_x))
            )
            high_y = jnp.transpose(
                jnp.broadcast_to(jnp.where(first_y, edge_y, none_y), (width_y, width_x))
            )
            next_x = jnp.where(rows == width_x - 1, high_x, pltpu.roll(plane, width_x - 1, 0))
            prev_x = jnp.where(rows == 0, low_x, pltpu.roll(plane, 1, 0))
            next_y = jnp.where(cols == width_y - 1, high_y, pltpu.roll(plane, width_y - 1, 1))
            prev_y = jnp.where(cols == 0, low_y, pltpu.roll(plane, 1, 1))
            neighbours = next_x + prev_x + next_y + prev_y
            o_ref[k, c] = plane - 0.2 * (4.0 * plane - neighbours)


def finish_paired(fields, rate_re, rate_im, before, after, got, below, above, lower):
    layers, components, width_x, width_y = fields.shape
    flags = jnp.stack(
        [lower.astype(jnp.int32), lax.axis_index("px"), lax.axis_index("py")]
    ).astype(jnp.int32)
    smem = pl.BlockSpec(memory_space=pltpu.SMEM)
    vmem = pl.BlockSpec(memory_space=pltpu.VMEM)
    edge_x = jax.ShapeDtypeStruct((layers, components, width_y), jnp.float32)
    edge_y = jax.ShapeDtypeStruct((layers, components, width_x), jnp.float32)
    combined, send_x, send_y = pl.pallas_call(
        last_sweep_kernel,
        in_specs=[smem] + [vmem] * 12,
        out_specs=(vmem, vmem, vmem),
        out_shape=(jax.ShapeDtypeStruct(fields.shape, jnp.float32), edge_x, edge_y),
    )(flags, fields, rate_re, rate_im, *before, *after, *below, *above, got)
    got_x = lax.ppermute(send_x, "px", [(0, 1), (1, 0)])
    got_y = lax.ppermute(send_y, "py", [(0, 1), (1, 0)])
    return pl.pallas_call(
        paired_stencil_kernel,
        in_specs=[smem, vmem, vmem, vmem],
        out_specs=vmem,
        out_shape=jax.ShapeDtypeStruct(fields.shape, jnp.float32),
    )(flags, combined, got_x, got_y)


def shards(source, phase, attenuation, pml_level, recv_values, recv_slab, recv_lateral, recv_layer):
    layers, components, width_x, width_y = source.shape
    shot_count = components // 2
    slab_count = lax.axis_size("slab")
    depth_total = layers * slab_count

    damping = attenuation + 0.5 / depth_total * pml_level.astype(jnp.float32)[None, :, :]
    amplitude = jnp.exp(-damping)
    rate_re = amplitude * jnp.cos(phase)
    rate_im = amplitude * jnp.sin(phase)

    prod_down = [(rate_re[0], rate_im[0])]
    for k in range(1, layers):
        prod_down.append(complex_times(rate_re[k], rate_im[k], *prod_down[-1]))
    levels = block_products(*prod_down[-1])

    forcing, levels = inject_receivers(
        source, recv_values, recv_slab, recv_lateral, recv_layer, levels
    )
    fields = forcing.reshape(layers, shot_count, 2, width_x, width_y)
    f_re = fields[:, :, 0]
    f_im = fields[:, :, 1]

    down = [None] * layers
    state = (f_re[0], f_im[0])
    down[0] = state
    for k in range(1, layers):
        t_re, t_im = complex_times(rate_re[k][None], rate_im[k][None], *state)
        state = (t_re + f_re[k], t_im + f_im[k])
        down[k] = state
    up = [None] * layers
    state = (f_re[layers - 1], f_im[layers - 1])
    up[layers - 1] = state
    for k in range(layers - 2, -1, -1):
        t_re, t_im = complex_times(rate_re[k][None], rate_im[k][None], *state)
        state = (t_re + f_re[k], t_im + f_im[k])
        up[k] = state

    if lax.axis_size("px") == 2 and lax.axis_size("py") == 2 and slab_count > 1:
        parts = entering_states(down[layers - 1], up[0], levels, defer_last=True)
        return finish_paired(forcing, rate_re, rate_im, *parts)
    (enter_re, enter_im), (below_re, below_im) = entering_states(down[layers - 1], up[0], levels)

    return finish(forcing, rate_re, rate_im, enter_re, enter_im, below_re, below_im)


def solution(mesh):
    in_specs = (
        P("slab", None, "px", "py"),
        P("slab", "px", "py"),
        P("slab", "px", "py"),
        P("px", "py"),
        P("px", "py", None, "slab"),
        P("px", "py", "slab", None),
        P("px", "py", "slab"),
        P("px", "py", "slab"),
    )
    out_specs = P("slab", None, "px", "py")
    return jax.shard_map(shards, mesh=mesh, in_specs=in_specs, out_specs=out_specs, check_vma=False)
```

```python
import jax
import jax.numpy as jnp
from jax import lax
from jax.sharding import PartitionSpec as P
from jax.experimental import pallas as pl
from jax.experimental.pallas import tpu as pltpu


def from_behind(array, axis, by):
    count = lax.axis_size(axis)
    pairs = [(i, i + by) for i in range(count) if 0 <= i + by < count]
    return lax.ppermute(array, axis, pairs)


def complex_times(a_re, a_im, b_re, b_im):
    return a_re * b_re - a_im * b_im, a_re * b_im + a_im * b_re


def inject_receivers(source, recv_values, recv_slab, recv_lateral, recv_layer, levels):
    layers, components, width_x, width_y = source.shape
    slab_count = lax.axis_size("slab")
    plane_size = width_x * width_y
    rows_here = recv_values.shape[3]
    capacity = rows_here // min(8, slab_count)
    values = recv_values[0, 0]
    target_slab = recv_slab[0, 0, :, 0]
    position = recv_layer[0, 0] * plane_size + recv_lateral[0, 0]
    order = jnp.arange(rows_here, dtype=jnp.int32)
    same_before = (target_slab[:, None] == target_slab[None, :]) & (order[None, :] < order[:, None])
    ranking = jnp.sum(same_before.astype(jnp.int32), axis=1)
    target_slot = target_slab * capacity + ranking
    rows = jnp.concatenate([values, position.astype(jnp.float32)[None, :]], axis=0)
    send_rows = (
        jnp.zeros((components + 1, slab_count * capacity), jnp.float32).at[:, target_slot].set(rows)
    )
    got_rows = lax.all_to_all(send_rows, "slab", split_axis=1, concat_axis=1, tiled=True)
    inject_values = got_rows[:components]
    inject_places = got_rows[components].astype(jnp.int32)
    row_of = inject_places // width_y
    col_of = inject_places % width_y
    pick_rows = (
        row_of[None, :] == jnp.arange(layers * width_x, dtype=jnp.int32)[:, None]
    ).astype(jnp.bfloat16)
    pick_cols = col_of[:, None] == jnp.arange(width_y, dtype=jnp.int32)[None, :]
    high = lax.reduce_precision(inject_values, exponent_bits=8, mantissa_bits=7)
    rest = inject_values - high
    middle = lax.reduce_precision(rest, exponent_bits=8, mantissa_bits=7)
    low = rest - middle
    pieces = jnp.stack([high, middle, low], axis=0)
    spread = jnp.where(pick_cols[None, None, :, :], pieces[:, :, :, None], 0.0)
    spread = jnp.transpose(spread, (2, 0, 1, 3)).reshape(
        slab_count * capacity, 3 * components * width_y
    )
    added = jnp.dot(pick_rows, spread.astype(jnp.bfloat16), preferred_element_type=jnp.float32)
    added = added.reshape(layers * width_x, 3, components * width_y)
    added = (added[:, 0] + added[:, 1]) + added[:, 2]
    added = jnp.transpose(added.reshape(layers, width_x, components, width_y), (0, 2, 1, 3))
    return source + added, levels


def exchange(array, step):
    count = lax.axis_size("slab")
    return lax.ppermute(array, "slab", [(i, i ^ step) for i in range(count)])


def block_products(a_re, a_im):
    slab_count = lax.axis_size("slab")
    here = lax.axis_index("slab")
    one = jnp.ones_like(a_re)
    zero = jnp.zeros_like(a_re)
    total = (a_re, a_im)
    below = (one, zero)
    above = (one, zero)
    levels = []
    step = 1
    while 2 * step < slab_count:
        got = exchange(jnp.stack(total, axis=0), step)
        partner = (got[0], got[1])
        levels.append((total, partner, below, above))
        lower = (here & step) == 0
        grown_below = complex_times(*below, *partner)
        grown_above = complex_times(*above, *partner)
        below = (jnp.where(lower, below[0], grown_below[0]), jnp.where(lower, below[1], grown_below[1]))
        above = (jnp.where(lower, grown_above[0], above[0]), jnp.where(lower, grown_above[1], above[1]))
        total = complex_times(*total, *partner)
        step *= 2
    levels.append((None, None, below, above))
    return levels


def entering_states(down_b, up_b, levels, defer_last=False):
    slab_count = lax.axis_size("slab")
    here = lax.axis_index("slab")
    shots = down_b[0].shape[0]
    before = (jnp.zeros_like(down_b[0]), jnp.zeros_like(down_b[1]))
    after = (jnp.zeros_like(up_b[0]), jnp.zeros_like(up_b[1]))
    step = 1
    level = 0
    while step < slab_count:
        lower = (here & step) == 0
        total, partner, below, above = levels[level]
        if 2 * step < slab_count:
            got = exchange(jnp.concatenate([*down_b, *up_b], axis=0), step)
            pd = (got[:shots], got[shots : 2 * shots])
            pu = (got[2 * shots : 3 * shots], got[3 * shots :])
            t_re, t_im = total[0][None], total[1][None]
            q_re, q_im = partner[0][None], partner[1][None]
            first = (jnp.where(lower, q_re, t_re), jnp.where(lower, q_im, t_im))
            inner = (jnp.where(lower, down_b[0], pd[0]), jnp.where(lower, down_b[1], pd[1]))
            outer = (jnp.where(lower, pd[0], down_b[0]), jnp.where(lower, pd[1], down_b[1]))
            m_re, m_im = complex_times(*first, *inner)
            new_down = (m_re + outer[0], m_im + outer[1])
            first = (jnp.where(lower, t_re, q_re), jnp.where(lower, t_im, q_im))
            inner = (jnp.where(lower, pu[0], up_b[0]), jnp.where(lower, pu[1], up_b[1]))
            outer = (jnp.where(lower, up_b[0], pu[0]), jnp.where(lower, up_b[1], pu[1]))
            m_re, m_im = complex_times(*first, *inner)
            new_up = (m_re + outer[0], m_im + outer[1])
        else:
            send = jnp.concatenate(
                [jnp.where(lower, down_b[0], up_b[0]), jnp.where(lower, down_b[1], up_b[1])], axis=0
            )
            got = exchange(send, step)
            if defer_last:
                return before, after, got, below, above, lower
            pd = (got[:shots], got[shots:])
            pu = pd
        g_re, g_im = complex_times(below[0][None], below[1][None], *pd)
        before = (
            jnp.where(lower, before[0], g_re + before[0]),
            jnp.where(lower, before[1], g_im + before[1]),
        )
        g_re, g_im = complex_times(above[0][None], above[1][None], *pu)
        after = (
            jnp.where(lower, g_re + after[0], after[0]),
            jnp.where(lower, g_im + after[1], after[1]),
        )
        if 2 * step < slab_count:
            down_b, up_b = new_down, new_up
        step *= 2
        level += 1
    if defer_last:
        return before, after, None, None, None, None
    return before, after


def edge_pair(last, first, axis):
    count = lax.axis_size(axis)
    if count == 2:
        here = lax.axis_index(axis)
        got = lax.ppermute(jnp.where(here == 0, last, first), axis, [(0, 1), (1, 0)])
        zero = jnp.zeros_like(got)
        return jnp.where(here == 1, got, zero), jnp.where(here == 0, got, zero)
    return from_behind(last, axis, 1), from_behind(first, axis, -1)


def sweep_kernel(f_ref, rr_ref, ri_ref, er_ref, ei_ref, br_ref, bi_ref,
                 c_ref, x0_ref, x1_ref, y0_ref, y1_ref):
    layers = f_ref.shape[0]
    shots = er_ref.shape[0]
    downs = []
    for s in range(shots):
        w_re, w_im = er_ref[s], ei_ref[s]
        per_layer = []
        for k in range(layers):
            t_re, t_im = complex_times(rr_ref[k], ri_ref[k], w_re, w_im)
            w_re, w_im = t_re + f_ref[k, 2 * s], t_im + f_ref[k, 2 * s + 1]
            per_layer.append((w_re, w_im))
        downs.append(per_layer)
    for s in range(shots):
        v_re, v_im = br_ref[s], bi_ref[s]
        for k in range(layers - 1, -1, -1):
            t_re, t_im = complex_times(rr_ref[k], ri_ref[k], v_re, v_im)
            f_re, f_im = f_ref[k, 2 * s], f_ref[k, 2 * s + 1]
            v_re, v_im = t_re + f_re, t_im + f_im
            d_re, d_im = downs[s][k]
            for part, plane in ((0, d_re + v_re - f_re), (1, d_im + v_im - f_im)):
                c = 2 * s + part
                c_ref[k, c] = plane
                x0_ref[k, pl.ds(c, 1), :] = plane[0:1, :]
                x1_ref[k, pl.ds(c, 1), :] = plane[-1:, :]
                flipped = jnp.transpose(plane)
                y0_ref[k, pl.ds(c, 1), :] = flipped[0:1, :]
                y1_ref[k, pl.ds(c, 1), :] = flipped[-1:, :]


def stencil_kernel(c_ref, lx_ref, hx_ref, ly_ref, hy_ref, o_ref):
    layers, components, width_x, width_y = c_ref.shape
    rows = lax.broadcasted_iota(jnp.int32, (width_x, width_y), 0)
    cols = lax.broadcasted_iota(jnp.int32, (width_x, width_y), 1)
    for k in range(layers):
        for c in range(components):
            plane = c_ref[k, c]
            low_x = jnp.broadcast_to(lx_ref[k, pl.ds(c, 1), :], (width_x, width_y))
            high_x = jnp.broadcast_to(hx_ref[k, pl.ds(c, 1), :], (width_x, width_y))
            low_y = jnp.transpose(jnp.broadcast_to(ly_ref[k, pl.ds(c, 1), :], (width_y, width_x)))
            high_y = jnp.transpose(jnp.broadcast_to(hy_ref[k, pl.ds(c, 1), :], (width_y, width_x)))
            next_x = jnp.where(rows == width_x - 1, high_x, pltpu.roll(plane, width_x - 1, 0))
            prev_x = jnp.where(rows == 0, low_x, pltpu.roll(plane, 1, 0))
            next_y = jnp.where(cols == width_y - 1, high_y, pltpu.roll(plane, width_y - 1, 1))
            prev_y = jnp.where(cols == 0, low_y, pltpu.roll(plane, 1, 1))
            neighbours = next_x + prev_x + next_y + prev_y
            o_ref[k, c] = plane - 0.2 * (4.0 * plane - neighbours)


def finish(fields, rate_re, rate_im, enter_re, enter_im, below_re, below_im):
    layers, components, width_x, width_y = fields.shape
    edge_x = jax.ShapeDtypeStruct((layers, components, width_y), jnp.float32)
    edge_y = jax.ShapeDtypeStruct((layers, components, width_x), jnp.float32)
    combined, x0, x1, y0, y1 = pl.pallas_call(
        sweep_kernel,
        out_shape=(jax.ShapeDtypeStruct(fields.shape, jnp.float32), edge_x, edge_x, edge_y, edge_y),
    )(fields, rate_re, rate_im, enter_re, enter_im, below_re, below_im)
    from_low_x, from_high_x = edge_pair(x1, x0, "px")
    from_low_y, from_high_y = edge_pair(y1, y0, "py")
    return pl.pallas_call(
        stencil_kernel,
        out_shape=jax.ShapeDtypeStruct(fields.shape, jnp.float32),
    )(combined, from_low_x, from_high_x, from_low_y, from_high_y)


def last_sweep_kernel(flag_ref, f_ref, rr_ref, ri_ref, br_ref, bi_ref, ar_ref, ai_ref,
                      lr_ref, li_ref, hr_ref, hi_ref, got_ref, c_ref, sx_ref, sy_ref):
    layers = f_ref.shape[0]
    shots = br_ref.shape[0]
    lower = flag_ref[0] == 1
    first_x = flag_ref[1] == 0
    first_y = flag_ref[2] == 0
    for s in range(shots):
        p_re, p_im = got_ref[s], got_ref[shots + s]
        g_re, g_im = complex_times(lr_ref[...], li_ref[...], p_re, p_im)
        w_re = jnp.where(lower, br_ref[s], g_re + br_ref[s])
        w_im = jnp.where(lower, bi_ref[s], g_im + bi_ref[s])
        g_re, g_im = complex_times(hr_ref[...], hi_ref[...], p_re, p_im)
        v_re = jnp.where(lower, g_re + ar_ref[s], ar_ref[s])
        v_im = jnp.where(lower, g_im + ai_ref[s], ai_ref[s])
        downs = []
        for k in range(layers):
            t_re, t_im = complex_times(rr_ref[k], ri_ref[k], w_re, w_im)
            w_re, w_im = t_re + f_ref[k, 2 * s], t_im + f_ref[k, 2 * s + 1]
            downs.append((w_re, w_im))
        for k in range(layers - 1, -1, -1):
            t_re, t_im = complex_times(rr_ref[k], ri_ref[k], v_re, v_im)
            f_re, f_im = f_ref[k, 2 * s], f_ref[k, 2 * s + 1]
            v_re, v_im = t_re + f_re, t_im + f_im
            d_re, d_im = downs[k]
            for part, plane in ((0, d_re + v_re - f_re), (1, d_im + v_im - f_im)):
                c = 2 * s + part
                c_ref[k, c] = plane
                sx_ref[k, pl.ds(c, 1), :] = jnp.where(first_x, plane[-1:, :], plane[0:1, :])
                flipped = jnp.transpose(plane)
                sy_ref[k, pl.ds(c, 1), :] = jnp.where(first_y, flipped[-1:, :], flipped[0:1, :])


def paired_stencil_kernel(flag_ref, c_ref, gx_ref, gy_ref, o_ref):
    layers, components, width_x, width_y = c_ref.shape
    rows = lax.broadcasted_iota(jnp.int32, (width_x, width_y), 0)
    cols = lax.broadcasted_iota(jnp.int32, (width_x, width_y), 1)
    first_x = flag_ref[1] == 0
    first_y = flag_ref[2] == 0
    for k in range(layers):
        for c in range(components):
            plane = c_ref[k, c]
            edge_x = gx_ref[k, pl.ds(c, 1), :]
            edge_y = gy_ref[k, pl.ds(c, 1), :]
            none_x = jnp.zeros_like(edge_x)
            none_y = jnp.zeros_like(edge_y)
            low_x = jnp.broadcast_to(jnp.where(first_x, none_x, edge_x), (width_x, width_y))
            high_x = jnp.broadcast_to(jnp.where(first_x, edge_x, none_x), (width_x, width_y))
            low_y = jnp.transpose(
                jnp.broadcast_to(jnp.where(first_y, none_y, edge_y), (width_y, width_x))
            )
            high_y = jnp.transpose(
                jnp.broadcast_to(jnp.where(first_y, edge_y, none_y), (width_y, width_x))
            )
            next_x = jnp.where(rows == width_x - 1, high_x, pltpu.roll(plane, width_x - 1, 0))
            prev_x = jnp.where(rows == 0, low_x, pltpu.roll(plane, 1, 0))
            next_y = jnp.where(cols == width_y - 1, high_y, pltpu.roll(plane, width_y - 1, 1))
            prev_y = jnp.where(cols == 0, low_y, pltpu.roll(plane, 1, 1))
            neighbours = next_x + prev_x + next_y + prev_y
            o_ref[k, c] = plane - 0.2 * (4.0 * plane - neighbours)


def finish_paired(fields, rate_re, rate_im, before, after, got, below, above, lower):
    layers, components, width_x, width_y = fields.shape
    flags = jnp.stack(
        [lower.astype(jnp.int32), lax.axis_index("px"), lax.axis_index("py")]
    ).astype(jnp.int32)
    smem = pl.BlockSpec(memory_space=pltpu.SMEM)
    vmem = pl.BlockSpec(memory_space=pltpu.VMEM)
    edge_x = jax.ShapeDtypeStruct((layers, components, width_y), jnp.float32)
    edge_y = jax.ShapeDtypeStruct((layers, components, width_x), jnp.float32)
    combined, send_x, send_y = pl.pallas_call(
        last_sweep_kernel,
        in_specs=[smem] + [vmem] * 12,
        out_specs=(vmem, vmem, vmem),
        out_shape=(jax.ShapeDtypeStruct(fields.shape, jnp.float32), edge_x, edge_y),
    )(flags, fields, rate_re, rate_im, *before, *after, *below, *above, got)
    got_x = lax.ppermute(send_x, "px", [(0, 1), (1, 0)])
    got_y = lax.ppermute(send_y, "py", [(0, 1), (1, 0)])
    return pl.pallas_call(
        paired_stencil_kernel,
        in_specs=[smem, vmem, vmem, vmem],
        out_specs=vmem,
        out_shape=jax.ShapeDtypeStruct(fields.shape, jnp.float32),
    )(flags, combined, got_x, got_y)


def shards(source, phase, attenuation, pml_level, recv_values, recv_slab, recv_lateral, recv_layer):
    layers, components, width_x, width_y = source.shape
    shot_count = components // 2
    slab_count = lax.axis_size("slab")
    depth_total = layers * slab_count

    damping = attenuation + 0.5 / depth_total * pml_level.astype(jnp.float32)[None, :, :]
    amplitude = jnp.exp(-damping)
    rate_re = amplitude * jnp.cos(phase)
    rate_im = amplitude * jnp.sin(phase)

    prod_down = [(rate_re[0], rate_im[0])]
    for k in range(1, layers):
        prod_down.append(complex_times(rate_re[k], rate_im[k], *prod_down[-1]))
    levels = block_products(*prod_down[-1])

    forcing, levels = inject_receivers(
        source, recv_values, recv_slab, recv_lateral, recv_layer, levels
    )
    fields = forcing.reshape(layers, shot_count, 2, width_x, width_y)
    f_re = fields[:, :, 0]
    f_im = fields[:, :, 1]

    down = [None] * layers
    state = (f_re[0], f_im[0])
    down[0] = state
    for k in range(1, layers):
        t_re, t_im = complex_times(rate_re[k][None], rate_im[k][None], *state)
        state = (t_re + f_re[k], t_im + f_im[k])
        down[k] = state
    up = [None] * layers
    state = (f_re[layers - 1], f_im[layers - 1])
    up[layers - 1] = state
    for k in range(layers - 2, -1, -1):
        t_re, t_im = complex_times(rate_re[k][None], rate_im[k][None], *state)
        state = (t_re + f_re[k], t_im + f_im[k])
        up[k] = state

    if lax.axis_size("px") == 2 and lax.axis_size("py") == 2 and slab_count > 1:
        parts = entering_states(down[layers - 1], up[0], levels, defer_last=True)
        return finish_paired(forcing, rate_re, rate_im, *parts)
    (enter_re, enter_im), (below_re, below_im) = entering_states(down[layers - 1], up[0], levels)

    return finish(forcing, rate_re, rate_im, enter_re, enter_im, below_re, below_im)


def solution(mesh):
    in_specs = (
        P("slab", None, "px", "py"),
        P("slab", "px", "py"),
        P("slab", "px", "py"),
        P("px", "py"),
        P("px", "py", None, "slab"),
        P("px", "py", "slab", None),
        P("px", "py", "slab"),
        P("px", "py", "slab"),
    )
    out_specs = P("slab", None, "px", "py")
    return jax.shard_map(shards, mesh=mesh, in_specs=in_specs, out_specs=out_specs, check_vma=False)
```

```python
import jax
import jax.numpy as jnp
from jax import lax
from jax.sharding import PartitionSpec as P
from jax.experimental import pallas as pl
from jax.experimental.pallas import tpu as pltpu


def from_behind(array, axis, by):
    count = lax.axis_size(axis)
    pairs = [(i, i + by) for i in range(count) if 0 <= i + by < count]
    return lax.ppermute(array, axis, pairs)


def complex_times(a_re, a_im, b_re, b_im):
    return a_re * b_re - a_im * b_im, a_re * b_im + a_im * b_re


def inject_receivers(source, recv_values, recv_slab, recv_lateral, recv_layer, levels):
    layers, components, width_x, width_y = source.shape
    slab_count = lax.axis_size("slab")
    plane_size = width_x * width_y
    rows_here = recv_values.shape[3]
    capacity = rows_here // min(8, slab_count)
    values = recv_values[0, 0]
    target_slab = recv_slab[0, 0, :, 0]
    position = recv_layer[0, 0] * plane_size + recv_lateral[0, 0]
    order = jnp.arange(rows_here, dtype=jnp.int32)
    same_before = (target_slab[:, None] == target_slab[None, :]) & (order[None, :] < order[:, None])
    ranking = jnp.sum(same_before.astype(jnp.int32), axis=1)
    target_slot = target_slab * capacity + ranking
    rows = jnp.concatenate([values, position.astype(jnp.float32)[None, :]], axis=0)
    send_rows = (
        jnp.zeros((components + 1, slab_count * capacity), jnp.float32).at[:, target_slot].set(rows)
    )
    got_rows = lax.all_to_all(send_rows, "slab", split_axis=1, concat_axis=1, tiled=True)
    inject_values = got_rows[:components]
    inject_places = got_rows[components].astype(jnp.int32)
    row_of = inject_places // width_y
    col_of = inject_places % width_y
    pick_rows = (
        row_of[None, :] == jnp.arange(layers * width_x, dtype=jnp.int32)[:, None]
    ).astype(jnp.bfloat16)
    pick_cols = col_of[:, None] == jnp.arange(width_y, dtype=jnp.int32)[None, :]
    high = lax.reduce_precision(inject_values, exponent_bits=8, mantissa_bits=7)
    pieces = jnp.stack([high, inject_values - high], axis=0)
    spread = jnp.where(pick_cols[None, None, :, :], pieces[:, :, :, None], 0.0)
    spread = jnp.transpose(spread, (2, 0, 1, 3)).reshape(
        slab_count * capacity, 2 * components * width_y
    )
    added = jnp.dot(pick_rows, spread.astype(jnp.bfloat16), preferred_element_type=jnp.float32)
    added = added.reshape(layers * width_x, 2, components * width_y)
    added = added[:, 0] + added[:, 1]
    added = jnp.transpose(added.reshape(layers, width_x, components, width_y), (0, 2, 1, 3))
    return source + added, levels


def exchange(array, step):
    count = lax.axis_size("slab")
    return lax.ppermute(array, "slab", [(i, i ^ step) for i in range(count)])


def block_products(a_re, a_im):
    slab_count = lax.axis_size("slab")
    here = lax.axis_index("slab")
    one = jnp.ones_like(a_re)
    zero = jnp.zeros_like(a_re)
    total = (a_re, a_im)
    below = (one, zero)
    above = (one, zero)
    levels = []
    step = 1
    while 2 * step < slab_count:
        got = exchange(jnp.stack(total, axis=0), step)
        partner = (got[0], got[1])
        levels.append((total, partner, below, above))
        lower = (here & step) == 0
        grown_below = complex_times(*below, *partner)
        grown_above = complex_times(*above, *partner)
        below = (jnp.where(lower, below[0], grown_below[0]), jnp.where(lower, below[1], grown_below[1]))
        above = (jnp.where(lower, grown_above[0], above[0]), jnp.where(lower, grown_above[1], above[1]))
        total = complex_times(*total, *partner)
        step *= 2
    levels.append((None, None, below, above))
    return levels


def entering_states(down_b, up_b, levels, defer_last=False):
    slab_count = lax.axis_size("slab")
    here = lax.axis_index("slab")
    shots = down_b[0].shape[0]
    before = (jnp.zeros_like(down_b[0]), jnp.zeros_like(down_b[1]))
    after = (jnp.zeros_like(up_b[0]), jnp.zeros_like(up_b[1]))
    step = 1
    level = 0
    while step < slab_count:
        lower = (here & step) == 0
        total, partner, below, above = levels[level]
        if 2 * step < slab_count:
            got = exchange(jnp.concatenate([*down_b, *up_b], axis=0), step)
            pd = (got[:shots], got[shots : 2 * shots])
            pu = (got[2 * shots : 3 * shots], got[3 * shots :])
            t_re, t_im = total[0][None], total[1][None]
            q_re, q_im = partner[0][None], partner[1][None]
            first = (jnp.where(lower, q_re, t_re), jnp.where(lower, q_im, t_im))
            inner = (jnp.where(lower, down_b[0], pd[0]), jnp.where(lower, down_b[1], pd[1]))
            outer = (jnp.where(lower, pd[0], down_b[0]), jnp.where(lower, pd[1], down_b[1]))
            m_re, m_im = complex_times(*first, *inner)
            new_down = (m_re + outer[0], m_im + outer[1])
            first = (jnp.where(lower, t_re, q_re), jnp.where(lower, t_im, q_im))
            inner = (jnp.where(lower, pu[0], up_b[0]), jnp.where(lower, pu[1], up_b[1]))
            outer = (jnp.where(lower, up_b[0], pu[0]), jnp.where(lower, up_b[1], pu[1]))
            m_re, m_im = complex_times(*first, *inner)
            new_up = (m_re + outer[0], m_im + outer[1])
        else:
            send = jnp.concatenate(
                [jnp.where(lower, down_b[0], up_b[0]), jnp.where(lower, down_b[1], up_b[1])], axis=0
            )
            got = exchange(send, step)
            if defer_last:
                return before, after, got, below, above, lower
            pd = (got[:shots], got[shots:])
            pu = pd
        g_re, g_im = complex_times(below[0][None], below[1][None], *pd)
        before = (
            jnp.where(lower, before[0], g_re + before[0]),
            jnp.where(lower, before[1], g_im + before[1]),
        )
        g_re, g_im = complex_times(above[0][None], above[1][None], *pu)
        after = (
            jnp.where(lower, g_re + after[0], after[0]),
            jnp.where(lower, g_im + after[1], after[1]),
        )
        if 2 * step < slab_count:
            down_b, up_b = new_down, new_up
        step *= 2
        level += 1
    if defer_last:
        return before, after, None, None, None, None
    return before, after


def edge_pair(last, first, axis):
    count = lax.axis_size(axis)
    if count == 2:
        here = lax.axis_index(axis)
        got = lax.ppermute(jnp.where(here == 0, last, first), axis, [(0, 1), (1, 0)])
        zero = jnp.zeros_like(got)
        return jnp.where(here == 1, got, zero), jnp.where(here == 0, got, zero)
    return from_behind(last, axis, 1), from_behind(first, axis, -1)


def sweep_kernel(f_ref, rr_ref, ri_ref, er_ref, ei_ref, br_ref, bi_ref,
                 c_ref, x0_ref, x1_ref, y0_ref, y1_ref):
    layers = f_ref.shape[0]
    shots = er_ref.shape[0]
    downs = []
    for s in range(shots):
        w_re, w_im = er_ref[s], ei_ref[s]
        per_layer = []
        for k in range(layers):
            t_re, t_im = complex_times(rr_ref[k], ri_ref[k], w_re, w_im)
            w_re, w_im = t_re + f_ref[k, 2 * s], t_im + f_ref[k, 2 * s + 1]
            per_layer.append((w_re, w_im))
        downs.append(per_layer)
    for s in range(shots):
        v_re, v_im = br_ref[s], bi_ref[s]
        for k in range(layers - 1, -1, -1):
            t_re, t_im = complex_times(rr_ref[k], ri_ref[k], v_re, v_im)
            f_re, f_im = f_ref[k, 2 * s], f_ref[k, 2 * s + 1]
            v_re, v_im = t_re + f_re, t_im + f_im
            d_re, d_im = downs[s][k]
            for part, plane in ((0, d_re + v_re - f_re), (1, d_im + v_im - f_im)):
                c = 2 * s + part
                c_ref[k, c] = plane
                x0_ref[k, pl.ds(c, 1), :] = plane[0:1, :]
                x1_ref[k, pl.ds(c, 1), :] = plane[-1:, :]
                flipped = jnp.transpose(plane)
                y0_ref[k, pl.ds(c, 1), :] = flipped[0:1, :]
                y1_ref[k, pl.ds(c, 1), :] = flipped[-1:, :]


def stencil_kernel(c_ref, lx_ref, hx_ref, ly_ref, hy_ref, o_ref):
    layers, components, width_x, width_y = c_ref.shape
    rows = lax.broadcasted_iota(jnp.int32, (width_x, width_y), 0)
    cols = lax.broadcasted_iota(jnp.int32, (width_x, width_y), 1)
    for k in range(layers):
        for c in range(components):
            plane = c_ref[k, c]
            low_x = jnp.broadcast_to(lx_ref[k, pl.ds(c, 1), :], (width_x, width_y))
            high_x = jnp.broadcast_to(hx_ref[k, pl.ds(c, 1), :], (width_x, width_y))
            low_y = jnp.transpose(jnp.broadcast_to(ly_ref[k, pl.ds(c, 1), :], (width_y, width_x)))
            high_y = jnp.transpose(jnp.broadcast_to(hy_ref[k, pl.ds(c, 1), :], (width_y, width_x)))
            next_x = jnp.where(rows == width_x - 1, high_x, pltpu.roll(plane, width_x - 1, 0))
            prev_x = jnp.where(rows == 0, low_x, pltpu.roll(plane, 1, 0))
            next_y = jnp.where(cols == width_y - 1, high_y, pltpu.roll(plane, width_y - 1, 1))
            prev_y = jnp.where(cols == 0, low_y, pltpu.roll(plane, 1, 1))
            neighbours = next_x + prev_x + next_y + prev_y
            o_ref[k, c] = plane - 0.2 * (4.0 * plane - neighbours)


def finish(fields, rate_re, rate_im, enter_re, enter_im, below_re, below_im):
    layers, components, width_x, width_y = fields.shape
    edge_x = jax.ShapeDtypeStruct((layers, components, width_y), jnp.float32)
    edge_y = jax.ShapeDtypeStruct((layers, components, width_x), jnp.float32)
    combined, x0, x1, y0, y1 = pl.pallas_call(
        sweep_kernel,
        out_shape=(jax.ShapeDtypeStruct(fields.shape, jnp.float32), edge_x, edge_x, edge_y, edge_y),
    )(fields, rate_re, rate_im, enter_re, enter_im, below_re, below_im)
    from_low_x, from_high_x = edge_pair(x1, x0, "px")
    from_low_y, from_high_y = edge_pair(y1, y0, "py")
    return pl.pallas_call(
        stencil_kernel,
        out_shape=jax.ShapeDtypeStruct(fields.shape, jnp.float32),
    )(combined, from_low_x, from_high_x, from_low_y, from_high_y)


def last_sweep_kernel(flag_ref, f_ref, rr_ref, ri_ref, br_ref, bi_ref, ar_ref, ai_ref,
                      lr_ref, li_ref, hr_ref, hi_ref, got_ref, c_ref, sx_ref, sy_ref):
    layers = f_ref.shape[0]
    shots = br_ref.shape[0]
    lower = flag_ref[0] == 1
    first_x = flag_ref[1] == 0
    first_y = flag_ref[2] == 0
    for s in range(shots):
        p_re, p_im = got_ref[s], got_ref[shots + s]
        g_re, g_im = complex_times(lr_ref[...], li_ref[...], p_re, p_im)
        w_re = jnp.where(lower, br_ref[s], g_re + br_ref[s])
        w_im = jnp.where(lower, bi_ref[s], g_im + bi_ref[s])
        g_re, g_im = complex_times(hr_ref[...], hi_ref[...], p_re, p_im)
        v_re = jnp.where(lower, g_re + ar_ref[s], ar_ref[s])
        v_im = jnp.where(lower, g_im + ai_ref[s], ai_ref[s])
        downs = []
        for k in range(layers):
            t_re, t_im = complex_times(rr_ref[k], ri_ref[k], w_re, w_im)
            w_re, w_im = t_re + f_ref[k, 2 * s], t_im + f_ref[k, 2 * s + 1]
            downs.append((w_re, w_im))
        for k in range(layers - 1, -1, -1):
            t_re, t_im = complex_times(rr_ref[k], ri_ref[k], v_re, v_im)
            f_re, f_im = f_ref[k, 2 * s], f_ref[k, 2 * s + 1]
            v_re, v_im = t_re + f_re, t_im + f_im
            d_re, d_im = downs[k]
            for part, plane in ((0, d_re + v_re - f_re), (1, d_im + v_im - f_im)):
                c = 2 * s + part
                c_ref[k, c] = plane
                sx_ref[k, pl.ds(c, 1), :] = jnp.where(first_x, plane[-1:, :], plane[0:1, :])
                flipped = jnp.transpose(plane)
                sy_ref[k, pl.ds(c, 1), :] = jnp.where(first_y, flipped[-1:, :], flipped[0:1, :])


def paired_stencil_kernel(flag_ref, c_ref, gx_ref, gy_ref, o_ref):
    layers, components, width_x, width_y = c_ref.shape
    rows = lax.broadcasted_iota(jnp.int32, (width_x, width_y), 0)
    cols = lax.broadcasted_iota(jnp.int32, (width_x, width_y), 1)
    side_rows = lax.broadcasted_iota(jnp.int32, (width_y, width_x), 0)
    first_x = flag_ref[1] == 0
    first_y = flag_ref[2] == 0
    for k in range(layers):
        for c in range(components):
            plane = c_ref[k, c]
            edge_x = gx_ref[k, pl.ds(c, 1), :]
            edge_y = jnp.broadcast_to(gy_ref[k, pl.ds(c, 1), :], (width_y, width_x))
            none_x = jnp.zeros_like(edge_x)
            low_x = jnp.broadcast_to(jnp.where(first_x, none_x, edge_x), (width_x, width_y))
            high_x = jnp.broadcast_to(jnp.where(first_x, edge_x, none_x), (width_x, width_y))
            side = jnp.where(side_rows == jnp.where(first_y, width_y - 1, 0), edge_y, 0.0)
            next_x = jnp.where(rows == width_x - 1, high_x, pltpu.roll(plane, width_x - 1, 0))
            prev_x = jnp.where(rows == 0, low_x, pltpu.roll(plane, 1, 0))
            next_y = jnp.where(cols == width_y - 1, 0.0, pltpu.roll(plane, width_y - 1, 1))
            prev_y = jnp.where(cols == 0, 0.0, pltpu.roll(plane, 1, 1))
            neighbours = next_x + prev_x + next_y + prev_y + jnp.transpose(side)
            o_ref[k, c] = plane - 0.2 * (4.0 * plane - neighbours)


def finish_paired(fields, rate_re, rate_im, before, after, got, below, above, lower):
    layers, components, width_x, width_y = fields.shape
    flags = jnp.stack(
        [lower.astype(jnp.int32), lax.axis_index("px"), lax.axis_index("py")]
    ).astype(jnp.int32)
    smem = pl.BlockSpec(memory_space=pltpu.SMEM)
    vmem = pl.BlockSpec(memory_space=pltpu.VMEM)
    edge_x = jax.ShapeDtypeStruct((layers, components, width_y), jnp.float32)
    edge_y = jax.ShapeDtypeStruct((layers, components, width_x), jnp.float32)
    combined, send_x, send_y = pl.pallas_call(
        last_sweep_kernel,
        in_specs=[smem] + [vmem] * 12,
        out_specs=(vmem, vmem, vmem),
        out_shape=(jax.ShapeDtypeStruct(fields.shape, jnp.float32), edge_x, edge_y),
    )(flags, fields, rate_re, rate_im, *before, *after, *below, *above, got)
    got_x = lax.ppermute(send_x, "px", [(0, 1), (1, 0)])
    got_y = lax.ppermute(send_y, "py", [(0, 1), (1, 0)])
    return pl.pallas_call(
        paired_stencil_kernel,
        in_specs=[smem, vmem, vmem, vmem],
        out_specs=vmem,
        out_shape=jax.ShapeDtypeStruct(fields.shape, jnp.float32),
    )(flags, combined, got_x, got_y)


def shards(source, phase, attenuation, pml_level, recv_values, recv_slab, recv_lateral, recv_layer):
    layers, components, width_x, width_y = source.shape
    shot_count = components // 2
    slab_count = lax.axis_size("slab")
    depth_total = layers * slab_count

    damping = attenuation + 0.5 / depth_total * pml_level.astype(jnp.float32)[None, :, :]
    amplitude = jnp.exp(-damping)
    rate_re = amplitude * jnp.cos(phase)
    rate_im = amplitude * jnp.sin(phase)

    prod_down = [(rate_re[0], rate_im[0])]
    for k in range(1, layers):
        prod_down.append(complex_times(rate_re[k], rate_im[k], *prod_down[-1]))
    levels = block_products(*prod_down[-1])

    forcing, levels = inject_receivers(
        source, recv_values, recv_slab, recv_lateral, recv_layer, levels
    )
    fields = forcing.reshape(layers, shot_count, 2, width_x, width_y)
    f_re = fields[:, :, 0]
    f_im = fields[:, :, 1]

    down = [None] * layers
    state = (f_re[0], f_im[0])
    down[0] = state
    for k in range(1, layers):
        t_re, t_im = complex_times(rate_re[k][None], rate_im[k][None], *state)
        state = (t_re + f_re[k], t_im + f_im[k])
        down[k] = state
    up = [None] * layers
    state = (f_re[layers - 1], f_im[layers - 1])
    up[layers - 1] = state
    for k in range(layers - 2, -1, -1):
        t_re, t_im = complex_times(rate_re[k][None], rate_im[k][None], *state)
        state = (t_re + f_re[k], t_im + f_im[k])
        up[k] = state

    if lax.axis_size("px") == 2 and lax.axis_size("py") == 2 and slab_count > 1:
        parts = entering_states(down[layers - 1], up[0], levels, defer_last=True)
        return finish_paired(forcing, rate_re, rate_im, *parts)
    (enter_re, enter_im), (below_re, below_im) = entering_states(down[layers - 1], up[0], levels)

    return finish(forcing, rate_re, rate_im, enter_re, enter_im, below_re, below_im)


def solution(mesh):
    in_specs = (
        P("slab", None, "px", "py"),
        P("slab", "px", "py"),
        P("slab", "px", "py"),
        P("px", "py"),
        P("px", "py", None, "slab"),
        P("px", "py", "slab", None),
        P("px", "py", "slab"),
        P("px", "py", "slab"),
    )
    out_specs = P("slab", None, "px", "py")
    return jax.shard_map(shards, mesh=mesh, in_specs=in_specs, out_specs=out_specs, check_vma=False)
```

```python
import jax
import jax.numpy as jnp
from jax import lax
from jax.sharding import PartitionSpec as P
from jax.experimental import pallas as pl
from jax.experimental.pallas import tpu as pltpu


def from_behind(array, axis, by):
    count = lax.axis_size(axis)
    pairs = [(i, i + by) for i in range(count) if 0 <= i + by < count]
    return lax.ppermute(array, axis, pairs)


def complex_times(a_re, a_im, b_re, b_im):
    return a_re * b_re - a_im * b_im, a_re * b_im + a_im * b_re


def inject_receivers(source, recv_values, recv_slab, recv_lateral, recv_layer, levels):
    layers, components, width_x, width_y = source.shape
    slab_count = lax.axis_size("slab")
    plane_size = width_x * width_y
    rows_here = recv_values.shape[3]
    capacity = rows_here // min(8, slab_count)
    values = recv_values[0, 0]
    target_slab = recv_slab[0, 0, :, 0]
    position = recv_layer[0, 0] * plane_size + recv_lateral[0, 0]
    order = jnp.arange(rows_here, dtype=jnp.int32)
    same_before = (target_slab[:, None] == target_slab[None, :]) & (order[None, :] < order[:, None])
    ranking = jnp.sum(same_before.astype(jnp.int32), axis=1)
    target_slot = target_slab * capacity + ranking
    rows = jnp.concatenate([values, position.astype(jnp.float32)[None, :]], axis=0)
    send_rows = (
        jnp.zeros((components + 1, slab_count * capacity), jnp.float32).at[:, target_slot].set(rows)
    )
    got_rows = lax.all_to_all(send_rows, "slab", split_axis=1, concat_axis=1, tiled=True)
    inject_values = got_rows[:components]
    inject_places = got_rows[components].astype(jnp.int32)
    row_of = inject_places // width_y
    col_of = inject_places % width_y
    pick_rows = (
        row_of[None, :] == jnp.arange(layers * width_x, dtype=jnp.int32)[:, None]
    ).astype(jnp.bfloat16)
    pick_cols = col_of[:, None] == jnp.arange(width_y, dtype=jnp.int32)[None, :]
    high = lax.reduce_precision(inject_values, exponent_bits=8, mantissa_bits=7)
    pieces = jnp.stack([high, inject_values - high], axis=0)
    spread = jnp.where(pick_cols[None, None, :, :], pieces[:, :, :, None], 0.0)
    spread = jnp.transpose(spread, (2, 0, 1, 3)).reshape(
        slab_count * capacity, 2 * components * width_y
    )
    added = jnp.dot(pick_rows, spread.astype(jnp.bfloat16), preferred_element_type=jnp.float32)
    added = added.reshape(layers * width_x, 2, components * width_y)
    added = added[:, 0] + added[:, 1]
    added = jnp.transpose(added.reshape(layers, width_x, components, width_y), (0, 2, 1, 3))
    return source + added, levels


def exchange(array, step):
    count = lax.axis_size("slab")
    return lax.ppermute(array, "slab", [(i, i ^ step) for i in range(count)])


def block_products(a_re, a_im):
    slab_count = lax.axis_size("slab")
    here = lax.axis_index("slab")
    one = jnp.ones_like(a_re)
    zero = jnp.zeros_like(a_re)
    total = (a_re, a_im)
    below = (one, zero)
    above = (one, zero)
    levels = []
    step = 1
    while 2 * step < slab_count:
        got = exchange(jnp.stack(total, axis=0), step)
        partner = (got[0], got[1])
        levels.append((total, partner, below, above))
        lower = (here & step) == 0
        grown_below = complex_times(*below, *partner)
        grown_above = complex_times(*above, *partner)
        below = (jnp.where(lower, below[0], grown_below[0]), jnp.where(lower, below[1], grown_below[1]))
        above = (jnp.where(lower, grown_above[0], above[0]), jnp.where(lower, grown_above[1], above[1]))
        total = complex_times(*total, *partner)
        step *= 2
    levels.append((None, None, below, above))
    return levels


def entering_states(down_b, up_b, levels, defer_last=False):
    slab_count = lax.axis_size("slab")
    here = lax.axis_index("slab")
    shots = down_b[0].shape[0]
    before = (jnp.zeros_like(down_b[0]), jnp.zeros_like(down_b[1]))
    after = (jnp.zeros_like(up_b[0]), jnp.zeros_like(up_b[1]))
    step = 1
    level = 0
    while step < slab_count:
        lower = (here & step) == 0
        total, partner, below, above = levels[level]
        if 2 * step < slab_count:
            got = exchange(jnp.concatenate([*down_b, *up_b], axis=0), step)
            pd = (got[:shots], got[shots : 2 * shots])
            pu = (got[2 * shots : 3 * shots], got[3 * shots :])
            t_re, t_im = total[0][None], total[1][None]
            q_re, q_im = partner[0][None], partner[1][None]
            first = (jnp.where(lower, q_re, t_re), jnp.where(lower, q_im, t_im))
            inner = (jnp.where(lower, down_b[0], pd[0]), jnp.where(lower, down_b[1], pd[1]))
            outer = (jnp.where(lower, pd[0], down_b[0]), jnp.where(lower, pd[1], down_b[1]))
            m_re, m_im = complex_times(*first, *inner)
            new_down = (m_re + outer[0], m_im + outer[1])
            first = (jnp.where(lower, t_re, q_re), jnp.where(lower, t_im, q_im))
            inner = (jnp.where(lower, pu[0], up_b[0]), jnp.where(lower, pu[1], up_b[1]))
            outer = (jnp.where(lower, up_b[0], pu[0]), jnp.where(lower, up_b[1], pu[1]))
            m_re, m_im = complex_times(*first, *inner)
            new_up = (m_re + outer[0], m_im + outer[1])
        else:
            send = jnp.concatenate(
                [jnp.where(lower, down_b[0], up_b[0]), jnp.where(lower, down_b[1], up_b[1])], axis=0
            )
            got = exchange(send, step)
            if defer_last:
                return before, after, got, below, above, lower
            pd = (got[:shots], got[shots:])
            pu = pd
        g_re, g_im = complex_times(below[0][None], below[1][None], *pd)
        before = (
            jnp.where(lower, before[0], g_re + before[0]),
            jnp.where(lower, before[1], g_im + before[1]),
        )
        g_re, g_im = complex_times(above[0][None], above[1][None], *pu)
        after = (
            jnp.where(lower, g_re + after[0], after[0]),
            jnp.where(lower, g_im + after[1], after[1]),
        )
        if 2 * step < slab_count:
            down_b, up_b = new_down, new_up
        step *= 2
        level += 1
    if defer_last:
        return before, after, None, None, None, None
    return before, after


def edge_pair(last, first, axis):
    count = lax.axis_size(axis)
    if count == 2:
        here = lax.axis_index(axis)
        got = lax.ppermute(jnp.where(here == 0, last, first), axis, [(0, 1), (1, 0)])
        zero = jnp.zeros_like(got)
        return jnp.where(here == 1, got, zero), jnp.where(here == 0, got, zero)
    return from_behind(last, axis, 1), from_behind(first, axis, -1)


def sweep_kernel(f_ref, rr_ref, ri_ref, er_ref, ei_ref, br_ref, bi_ref,
                 c_ref, x0_ref, x1_ref, y0_ref, y1_ref):
    layers = f_ref.shape[0]
    shots = er_ref.shape[0]
    downs = []
    for s in range(shots):
        w_re, w_im = er_ref[s], ei_ref[s]
        per_layer = []
        for k in range(layers):
            t_re, t_im = complex_times(rr_ref[k], ri_ref[k], w_re, w_im)
            w_re, w_im = t_re + f_ref[k, 2 * s], t_im + f_ref[k, 2 * s + 1]
            per_layer.append((w_re, w_im))
        downs.append(per_layer)
    for s in range(shots):
        v_re, v_im = br_ref[s], bi_ref[s]
        for k in range(layers - 1, -1, -1):
            t_re, t_im = complex_times(rr_ref[k], ri_ref[k], v_re, v_im)
            f_re, f_im = f_ref[k, 2 * s], f_ref[k, 2 * s + 1]
            v_re, v_im = t_re + f_re, t_im + f_im
            d_re, d_im = downs[s][k]
            for part, plane in ((0, d_re + v_re - f_re), (1, d_im + v_im - f_im)):
                c = 2 * s + part
                c_ref[k, c] = plane
                x0_ref[k, pl.ds(c, 1), :] = plane[0:1, :]
                x1_ref[k, pl.ds(c, 1), :] = plane[-1:, :]
                flipped = jnp.transpose(plane)
                y0_ref[k, pl.ds(c, 1), :] = flipped[0:1, :]
                y1_ref[k, pl.ds(c, 1), :] = flipped[-1:, :]


def stencil_kernel(c_ref, lx_ref, hx_ref, ly_ref, hy_ref, o_ref):
    layers, components, width_x, width_y = c_ref.shape
    rows = lax.broadcasted_iota(jnp.int32, (width_x, width_y), 0)
    cols = lax.broadcasted_iota(jnp.int32, (width_x, width_y), 1)
    for k in range(layers):
        for c in range(components):
            plane = c_ref[k, c]
            low_x = jnp.broadcast_to(lx_ref[k, pl.ds(c, 1), :], (width_x, width_y))
            high_x = jnp.broadcast_to(hx_ref[k, pl.ds(c, 1), :], (width_x, width_y))
            low_y = jnp.transpose(jnp.broadcast_to(ly_ref[k, pl.ds(c, 1), :], (width_y, width_x)))
            high_y = jnp.transpose(jnp.broadcast_to(hy_ref[k, pl.ds(c, 1), :], (width_y, width_x)))
            next_x = jnp.where(rows == width_x - 1, high_x, pltpu.roll(plane, width_x - 1, 0))
            prev_x = jnp.where(rows == 0, low_x, pltpu.roll(plane, 1, 0))
            next_y = jnp.where(cols == width_y - 1, high_y, pltpu.roll(plane, width_y - 1, 1))
            prev_y = jnp.where(cols == 0, low_y, pltpu.roll(plane, 1, 1))
            neighbours = next_x + prev_x + next_y + prev_y
            o_ref[k, c] = plane - 0.2 * (4.0 * plane - neighbours)


def finish(fields, rate_re, rate_im, enter_re, enter_im, below_re, below_im):
    layers, components, width_x, width_y = fields.shape
    edge_x = jax.ShapeDtypeStruct((layers, components, width_y), jnp.float32)
    edge_y = jax.ShapeDtypeStruct((layers, components, width_x), jnp.float32)
    combined, x0, x1, y0, y1 = pl.pallas_call(
        sweep_kernel,
        out_shape=(jax.ShapeDtypeStruct(fields.shape, jnp.float32), edge_x, edge_x, edge_y, edge_y),
    )(fields, rate_re, rate_im, enter_re, enter_im, below_re, below_im)
    from_low_x, from_high_x = edge_pair(x1, x0, "px")
    from_low_y, from_high_y = edge_pair(y1, y0, "py")
    return pl.pallas_call(
        stencil_kernel,
        out_shape=jax.ShapeDtypeStruct(fields.shape, jnp.float32),
    )(combined, from_low_x, from_high_x, from_low_y, from_high_y)


def swept_values(flag_ref, f_ref, rr_ref, ri_ref, br_ref, bi_ref, ar_ref, ai_ref,
                 lr_ref, li_ref, hr_ref, hi_ref, got_ref, cut, emit):
    layers = f_ref.shape[0]
    shots = br_ref.shape[0]
    lower = flag_ref[0] == 1
    for s in range(shots):
        p_re, p_im = cut(got_ref, s), cut(got_ref, shots + s)
        g_re, g_im = complex_times(cut(lr_ref), cut(li_ref), p_re, p_im)
        w_re = jnp.where(lower, cut(br_ref, s), g_re + cut(br_ref, s))
        w_im = jnp.where(lower, cut(bi_ref, s), g_im + cut(bi_ref, s))
        g_re, g_im = complex_times(cut(hr_ref), cut(hi_ref), p_re, p_im)
        v_re = jnp.where(lower, g_re + cut(ar_ref, s), cut(ar_ref, s))
        v_im = jnp.where(lower, g_im + cut(ai_ref, s), cut(ai_ref, s))
        downs = []
        for k in range(layers):
            t_re, t_im = complex_times(cut(rr_ref, k), cut(ri_ref, k), w_re, w_im)
            w_re, w_im = t_re + cut(f_ref, k, 2 * s), t_im + cut(f_ref, k, 2 * s + 1)
            downs.append((w_re, w_im))
        for k in range(layers - 1, -1, -1):
            t_re, t_im = complex_times(cut(rr_ref, k), cut(ri_ref, k), v_re, v_im)
            f_re, f_im = cut(f_ref, k, 2 * s), cut(f_ref, k, 2 * s + 1)
            v_re, v_im = t_re + f_re, t_im + f_im
            d_re, d_im = downs[k]
            emit(k, 2 * s, d_re + v_re - f_re)
            emit(k, 2 * s + 1, d_im + v_im - f_im)


def edge_kernel(*refs):
    ins, (sx_ref, sy_ref, side_ref) = refs[:13], refs[13:]
    flag_ref = ins[0]
    components = sx_ref.shape[1]
    first_x = flag_ref[1] == 0
    first_y = flag_ref[2] == 0
    found = {}

    def keep(name):
        def emit(k, c, value):
            found[(name, k, c)] = value
        return emit

    for name, part in (("x0", (pl.ds(0, 1), slice(None))), ("x1", (pl.ds(-1 % 128, 1), slice(None))),
                       ("y0", (slice(None), pl.ds(0, 1))), ("y1", (slice(None), pl.ds(-1 % 128, 1)))):
        def cut(ref, *lead, part=part):
            return ref[tuple(lead) + part]
        swept_values(*ins, cut, keep(name))
    side_ref[...] = jnp.zeros_like(side_ref)
    layers = sx_ref.shape[0]
    for k in range(layers):
        for c in range(components):
            sx_ref[k, pl.ds(c, 1), :] = jnp.where(first_x, found[("x1", k, c)], found[("x0", k, c)])
            j = k * components + c
            side_ref[:, pl.ds(j, 1)] = jnp.where(first_y, found[("y1", k, c)], found[("y0", k, c)])
    flipped = jnp.transpose(side_ref[...])
    for k in range(layers):
        for c in range(components):
            j = k * components + c
            sy_ref[k, pl.ds(c, 1), :] = flipped[j : j + 1, :]


def main_kernel(*refs):
    ins, o_ref = refs[:13], refs[13]
    width_x, width_y = o_ref.shape[2], o_ref.shape[3]
    rows = lax.broadcasted_iota(jnp.int32, (width_x, width_y), 0)
    cols = lax.broadcasted_iota(jnp.int32, (width_x, width_y), 1)

    def cut(ref, *lead):
        return ref[tuple(lead)]

    def emit(k, c, plane):
        next_x = jnp.where(rows == width_x - 1, 0.0, pltpu.roll(plane, width_x - 1, 0))
        prev_x = jnp.where(rows == 0, 0.0, pltpu.roll(plane, 1, 0))
        next_y = jnp.where(cols == width_y - 1, 0.0, pltpu.roll(plane, width_y - 1, 1))
        prev_y = jnp.where(cols == 0, 0.0, pltpu.roll(plane, 1, 1))
        neighbours = next_x + prev_x + next_y + prev_y
        o_ref[k, c] = plane - 0.2 * (4.0 * plane - neighbours)

    swept_values(*ins, cut, emit)


def fix_kernel(flag_ref, base_ref, gx_ref, gy_ref, o_ref):
    layers, components, width_x, width_y = base_ref.shape
    rows = lax.broadcasted_iota(jnp.int32, (width_x, width_y), 0)
    side_rows = lax.broadcasted_iota(jnp.int32, (width_y, width_x), 0)
    first_x = flag_ref[1] == 0
    first_y = flag_ref[2] == 0
    for k in range(layers):
        for c in range(components):
            edge_x = jnp.broadcast_to(gx_ref[k, pl.ds(c, 1), :], (width_x, width_y))
            edge_y = jnp.broadcast_to(gy_ref[k, pl.ds(c, 1), :], (width_y, width_x))
            across = jnp.where(rows == jnp.where(first_x, width_x - 1, 0), edge_x, 0.0)
            side = jnp.where(side_rows == jnp.where(first_y, width_y - 1, 0), edge_y, 0.0)
            o_ref[k, c] = base_ref[k, c] + 0.2 * (across + jnp.transpose(side))


def finish_paired(fields, rate_re, rate_im, before, after, got, below, above, lower):
    layers, components, width_x, width_y = fields.shape
    flags = jnp.stack(
        [lower.astype(jnp.int32), lax.axis_index("px"), lax.axis_index("py")]
    ).astype(jnp.int32)
    smem = pl.BlockSpec(memory_space=pltpu.SMEM)
    vmem = pl.BlockSpec(memory_space=pltpu.VMEM)
    operands = (flags, fields, rate_re, rate_im, *before, *after, *below, *above, got)
    edge_x = jax.ShapeDtypeStruct((layers, components, width_y), jnp.float32)
    edge_y = jax.ShapeDtypeStruct((layers, components, width_x), jnp.float32)
    send_x, send_y = pl.pallas_call(
        edge_kernel,
        in_specs=[smem] + [vmem] * 12,
        out_specs=(vmem, vmem),
        out_shape=(edge_x, edge_y),
        scratch_shapes=[pltpu.VMEM((width_x, width_y), jnp.float32)],
    )(*operands)
    got_x = lax.ppermute(send_x, "px", [(0, 1), (1, 0)])
    got_y = lax.ppermute(send_y, "py", [(0, 1), (1, 0)])
    base = pl.pallas_call(
        main_kernel,
        in_specs=[smem] + [vmem] * 12,
        out_specs=vmem,
        out_shape=jax.ShapeDtypeStruct(fields.shape, jnp.float32),
    )(*operands)
    return pl.pallas_call(
        fix_kernel,
        in_specs=[smem, vmem, vmem, vmem],
        out_specs=vmem,
        out_shape=jax.ShapeDtypeStruct(fields.shape, jnp.float32),
        input_output_aliases={1: 0},
    )(flags, base, got_x, got_y)


def shards(source, phase, attenuation, pml_level, recv_values, recv_slab, recv_lateral, recv_layer):
    layers, components, width_x, width_y = source.shape
    shot_count = components // 2
    slab_count = lax.axis_size("slab")
    depth_total = layers * slab_count

    damping = attenuation + 0.5 / depth_total * pml_level.astype(jnp.float32)[None, :, :]
    amplitude = jnp.exp(-damping)
    rate_re = amplitude * jnp.cos(phase)
    rate_im = amplitude * jnp.sin(phase)

    prod_down = [(rate_re[0], rate_im[0])]
    for k in range(1, layers):
        prod_down.append(complex_times(rate_re[k], rate_im[k], *prod_down[-1]))
    levels = block_products(*prod_down[-1])

    forcing, levels = inject_receivers(
        source, recv_values, recv_slab, recv_lateral, recv_layer, levels
    )
    fields = forcing.reshape(layers, shot_count, 2, width_x, width_y)
    f_re = fields[:, :, 0]
    f_im = fields[:, :, 1]

    down = [None] * layers
    state = (f_re[0], f_im[0])
    down[0] = state
    for k in range(1, layers):
        t_re, t_im = complex_times(rate_re[k][None], rate_im[k][None], *state)
        state = (t_re + f_re[k], t_im + f_im[k])
        down[k] = state
    up = [None] * layers
    state = (f_re[layers - 1], f_im[layers - 1])
    up[layers - 1] = state
    for k in range(layers - 2, -1, -1):
        t_re, t_im = complex_times(rate_re[k][None], rate_im[k][None], *state)
        state = (t_re + f_re[k], t_im + f_im[k])
        up[k] = state

    if lax.axis_size("px") == 2 and lax.axis_size("py") == 2 and slab_count > 1:
        parts = entering_states(down[layers - 1], up[0], levels, defer_last=True)
        return finish_paired(forcing, rate_re, rate_im, *parts)
    (enter_re, enter_im), (below_re, below_im) = entering_states(down[layers - 1], up[0], levels)

    return finish(forcing, rate_re, rate_im, enter_re, enter_im, below_re, below_im)


def solution(mesh):
    in_specs = (
        P("slab", None, "px", "py"),
        P("slab", "px", "py"),
        P("slab", "px", "py"),
        P("px", "py"),
        P("px", "py", None, "slab"),
        P("px", "py", "slab", None),
        P("px", "py", "slab"),
        P("px", "py", "slab"),
    )
    out_specs = P("slab", None, "px", "py")
    return jax.shard_map(shards, mesh=mesh, in_specs=in_specs, out_specs=out_specs, check_vma=False)
```

```python
import jax
import jax.numpy as jnp
from jax import lax
from jax.sharding import PartitionSpec as P
from jax.experimental import pallas as pl
from jax.experimental.pallas import tpu as pltpu


def from_behind(array, axis, by):
    count = lax.axis_size(axis)
    pairs = [(i, i + by) for i in range(count) if 0 <= i + by < count]
    return lax.ppermute(array, axis, pairs)


def complex_times(a_re, a_im, b_re, b_im):
    return a_re * b_re - a_im * b_im, a_re * b_im + a_im * b_re


def inject_receivers(source, recv_values, recv_slab, recv_lateral, recv_layer, levels):
    layers, components, width_x, width_y = source.shape
    slab_count = lax.axis_size("slab")
    plane_size = width_x * width_y
    rows_here = recv_values.shape[3]
    capacity = rows_here // min(8, slab_count)
    values = recv_values[0, 0]
    target_slab = recv_slab[0, 0, :, 0]
    position = recv_layer[0, 0] * plane_size + recv_lateral[0, 0]
    order = jnp.arange(rows_here, dtype=jnp.int32)
    same_before = (target_slab[:, None] == target_slab[None, :]) & (order[None, :] < order[:, None])
    ranking = jnp.sum(same_before.astype(jnp.int32), axis=1)
    target_slot = target_slab * capacity + ranking
    rows = jnp.concatenate([values, position.astype(jnp.float32)[None, :]], axis=0)
    send_rows = (
        jnp.zeros((components + 1, slab_count * capacity), jnp.float32).at[:, target_slot].set(rows)
    )
    got_rows = lax.all_to_all(send_rows, "slab", split_axis=1, concat_axis=1, tiled=True)
    inject_values = got_rows[:components]
    inject_places = got_rows[components].astype(jnp.int32)
    row_of = inject_places // width_y
    col_of = inject_places % width_y
    pick_rows = (
        row_of[None, :] == jnp.arange(layers * width_x, dtype=jnp.int32)[:, None]
    ).astype(jnp.bfloat16)
    pick_cols = col_of[:, None] == jnp.arange(width_y, dtype=jnp.int32)[None, :]
    high = lax.reduce_precision(inject_values, exponent_bits=8, mantissa_bits=7)
    pieces = jnp.stack([high, inject_values - high], axis=0)
    spread = jnp.where(pick_cols[None, None, :, :], pieces[:, :, :, None], 0.0)
    spread = jnp.transpose(spread, (2, 0, 1, 3)).reshape(
        slab_count * capacity, 2 * components * width_y
    )
    added = jnp.dot(pick_rows, spread.astype(jnp.bfloat16), preferred_element_type=jnp.float32)
    added = added.reshape(layers * width_x, 2, components * width_y)
    added = added[:, 0] + added[:, 1]
    added = jnp.transpose(added.reshape(layers, width_x, components, width_y), (0, 2, 1, 3))
    return source + added, levels


def exchange(array, step):
    count = lax.axis_size("slab")
    return lax.ppermute(array, "slab", [(i, i ^ step) for i in range(count)])


def block_products(a_re, a_im):
    slab_count = lax.axis_size("slab")
    here = lax.axis_index("slab")
    one = jnp.ones_like(a_re)
    zero = jnp.zeros_like(a_re)
    total = (a_re, a_im)
    below = (one, zero)
    above = (one, zero)
    levels = []
    step = 1
    while 2 * step < slab_count:
        got = exchange(jnp.stack(total, axis=0), step)
        partner = (got[0], got[1])
        levels.append((total, partner, below, above))
        lower = (here & step) == 0
        grown_below = complex_times(*below, *partner)
        grown_above = complex_times(*above, *partner)
        below = (jnp.where(lower, below[0], grown_below[0]), jnp.where(lower, below[1], grown_below[1]))
        above = (jnp.where(lower, grown_above[0], above[0]), jnp.where(lower, grown_above[1], above[1]))
        total = complex_times(*total, *partner)
        step *= 2
    levels.append((None, None, below, above))
    return levels


def entering_states(down_b, up_b, levels, defer_last=False):
    slab_count = lax.axis_size("slab")
    here = lax.axis_index("slab")
    shots = down_b[0].shape[0]
    before = (jnp.zeros_like(down_b[0]), jnp.zeros_like(down_b[1]))
    after = (jnp.zeros_like(up_b[0]), jnp.zeros_like(up_b[1]))
    step = 1
    level = 0
    while step < slab_count:
        lower = (here & step) == 0
        total, partner, below, above = levels[level]
        if 2 * step < slab_count:
            got = exchange(jnp.concatenate([*down_b, *up_b], axis=0), step)
            pd = (got[:shots], got[shots : 2 * shots])
            pu = (got[2 * shots : 3 * shots], got[3 * shots :])
            t_re, t_im = total[0][None], total[1][None]
            q_re, q_im = partner[0][None], partner[1][None]
            first = (jnp.where(lower, q_re, t_re), jnp.where(lower, q_im, t_im))
            inner = (jnp.where(lower, down_b[0], pd[0]), jnp.where(lower, down_b[1], pd[1]))
            outer = (jnp.where(lower, pd[0], down_b[0]), jnp.where(lower, pd[1], down_b[1]))
            m_re, m_im = complex_times(*first, *inner)
            new_down = (m_re + outer[0], m_im + outer[1])
            first = (jnp.where(lower, t_re, q_re), jnp.where(lower, t_im, q_im))
            inner = (jnp.where(lower, pu[0], up_b[0]), jnp.where(lower, pu[1], up_b[1]))
            outer = (jnp.where(lower, up_b[0], pu[0]), jnp.where(lower, up_b[1], pu[1]))
            m_re, m_im = complex_times(*first, *inner)
            new_up = (m_re + outer[0], m_im + outer[1])
        else:
            send = jnp.concatenate(
                [jnp.where(lower, down_b[0], up_b[0]), jnp.where(lower, down_b[1], up_b[1])], axis=0
            )
            got = exchange(send, step)
            if defer_last:
                return before, after, got, below, above, lower
            pd = (got[:shots], got[shots:])
            pu = pd
        g_re, g_im = complex_times(below[0][None], below[1][None], *pd)
        before = (
            jnp.where(lower, before[0], g_re + before[0]),
            jnp.where(lower, before[1], g_im + before[1]),
        )
        g_re, g_im = complex_times(above[0][None], above[1][None], *pu)
        after = (
            jnp.where(lower, g_re + after[0], after[0]),
            jnp.where(lower, g_im + after[1], after[1]),
        )
        if 2 * step < slab_count:
            down_b, up_b = new_down, new_up
        step *= 2
        level += 1
    if defer_last:
        return before, after, None, None, None, None
    return before, after


def edge_pair(last, first, axis):
    count = lax.axis_size(axis)
    if count == 2:
        here = lax.axis_index(axis)
        got = lax.ppermute(jnp.where(here == 0, last, first), axis, [(0, 1), (1, 0)])
        zero = jnp.zeros_like(got)
        return jnp.where(here == 1, got, zero), jnp.where(here == 0, got, zero)
    return from_behind(last, axis, 1), from_behind(first, axis, -1)


def sweep_kernel(f_ref, rr_ref, ri_ref, er_ref, ei_ref, br_ref, bi_ref,
                 c_ref, x0_ref, x1_ref, y0_ref, y1_ref):
    layers = f_ref.shape[0]
    shots = er_ref.shape[0]
    downs = []
    for s in range(shots):
        w_re, w_im = er_ref[s], ei_ref[s]
        per_layer = []
        for k in range(layers):
            t_re, t_im = complex_times(rr_ref[k], ri_ref[k], w_re, w_im)
            w_re, w_im = t_re + f_ref[k, 2 * s], t_im + f_ref[k, 2 * s + 1]
            per_layer.append((w_re, w_im))
        downs.append(per_layer)
    for s in range(shots):
        v_re, v_im = br_ref[s], bi_ref[s]
        for k in range(layers - 1, -1, -1):
            t_re, t_im = complex_times(rr_ref[k], ri_ref[k], v_re, v_im)
            f_re, f_im = f_ref[k, 2 * s], f_ref[k, 2 * s + 1]
            v_re, v_im = t_re + f_re, t_im + f_im
            d_re, d_im = downs[s][k]
            for part, plane in ((0, d_re + v_re - f_re), (1, d_im + v_im - f_im)):
                c = 2 * s + part
                c_ref[k, c] = plane
                x0_ref[k, pl.ds(c, 1), :] = plane[0:1, :]
                x1_ref[k, pl.ds(c, 1), :] = plane[-1:, :]
                flipped = jnp.transpose(plane)
                y0_ref[k, pl.ds(c, 1), :] = flipped[0:1, :]
                y1_ref[k, pl.ds(c, 1), :] = flipped[-1:, :]


def stencil_kernel(c_ref, lx_ref, hx_ref, ly_ref, hy_ref, o_ref):
    layers, components, width_x, width_y = c_ref.shape
    rows = lax.broadcasted_iota(jnp.int32, (width_x, width_y), 0)
    cols = lax.broadcasted_iota(jnp.int32, (width_x, width_y), 1)
    for k in range(layers):
        for c in range(components):
            plane = c_ref[k, c]
            low_x = jnp.broadcast_to(lx_ref[k, pl.ds(c, 1), :], (width_x, width_y))
            high_x = jnp.broadcast_to(hx_ref[k, pl.ds(c, 1), :], (width_x, width_y))
            low_y = jnp.transpose(jnp.broadcast_to(ly_ref[k, pl.ds(c, 1), :], (width_y, width_x)))
            high_y = jnp.transpose(jnp.broadcast_to(hy_ref[k, pl.ds(c, 1), :], (width_y, width_x)))
            next_x = jnp.where(rows == width_x - 1, high_x, pltpu.roll(plane, width_x - 1, 0))
            prev_x = jnp.where(rows == 0, low_x, pltpu.roll(plane, 1, 0))
            next_y = jnp.where(cols == width_y - 1, high_y, pltpu.roll(plane, width_y - 1, 1))
            prev_y = jnp.where(cols == 0, low_y, pltpu.roll(plane, 1, 1))
            neighbours = next_x + prev_x + next_y + prev_y
            o_ref[k, c] = plane - 0.2 * (4.0 * plane - neighbours)


def finish(fields, rate_re, rate_im, enter_re, enter_im, below_re, below_im):
    layers, components, width_x, width_y = fields.shape
    edge_x = jax.ShapeDtypeStruct((layers, components, width_y), jnp.float32)
    edge_y = jax.ShapeDtypeStruct((layers, components, width_x), jnp.float32)
    combined, x0, x1, y0, y1 = pl.pallas_call(
        sweep_kernel,
        out_shape=(jax.ShapeDtypeStruct(fields.shape, jnp.float32), edge_x, edge_x, edge_y, edge_y),
    )(fields, rate_re, rate_im, enter_re, enter_im, below_re, below_im)
    from_low_x, from_high_x = edge_pair(x1, x0, "px")
    from_low_y, from_high_y = edge_pair(y1, y0, "py")
    return pl.pallas_call(
        stencil_kernel,
        out_shape=jax.ShapeDtypeStruct(fields.shape, jnp.float32),
    )(combined, from_low_x, from_high_x, from_low_y, from_high_y)


def last_sweep_kernel(flag_ref, f_ref, rr_ref, ri_ref, br_ref, bi_ref, ar_ref, ai_ref,
                      lr_ref, li_ref, hr_ref, hi_ref, got_ref, c_ref, sx_ref, sy_ref):
    layers = f_ref.shape[0]
    shots = br_ref.shape[0]
    lower = flag_ref[0] == 1
    first_x = flag_ref[1] == 0
    first_y = flag_ref[2] == 0
    for s in range(shots):
        p_re, p_im = got_ref[s], got_ref[shots + s]
        g_re, g_im = complex_times(lr_ref[...], li_ref[...], p_re, p_im)
        w_re = jnp.where(lower, br_ref[s], g_re + br_ref[s])
        w_im = jnp.where(lower, bi_ref[s], g_im + bi_ref[s])
        g_re, g_im = complex_times(hr_ref[...], hi_ref[...], p_re, p_im)
        v_re = jnp.where(lower, g_re + ar_ref[s], ar_ref[s])
        v_im = jnp.where(lower, g_im + ai_ref[s], ai_ref[s])
        downs = []
        for k in range(layers):
            t_re, t_im = complex_times(rr_ref[k], ri_ref[k], w_re, w_im)
            w_re, w_im = t_re + f_ref[k, 2 * s], t_im + f_ref[k, 2 * s + 1]
            downs.append((w_re, w_im))
        for k in range(layers - 1, -1, -1):
            t_re, t_im = complex_times(rr_ref[k], ri_ref[k], v_re, v_im)
            f_re, f_im = f_ref[k, 2 * s], f_ref[k, 2 * s + 1]
            v_re, v_im = t_re + f_re, t_im + f_im
            d_re, d_im = downs[k]
            for part, plane in ((0, d_re + v_re - f_re), (1, d_im + v_im - f_im)):
                c = 2 * s + part
                c_ref[k, c] = plane
                sx_ref[k, pl.ds(c, 1), :] = jnp.where(first_x, plane[-1:, :], plane[0:1, :])
                j = k * c_ref.shape[1] + c
                sy_ref[:, pl.ds(j, 1)] = jnp.where(first_y, plane[:, -1:], plane[:, 0:1])


def paired_stencil_kernel(flag_ref, c_ref, gx_ref, gy_ref, o_ref):
    layers, components, width_x, width_y = c_ref.shape
    rows = lax.broadcasted_iota(jnp.int32, (width_x, width_y), 0)
    cols = lax.broadcasted_iota(jnp.int32, (width_x, width_y), 1)
    first_x = flag_ref[1] == 0
    first_y = flag_ref[2] == 0
    for k in range(layers):
        for c in range(components):
            plane = c_ref[k, c]
            edge_x = gx_ref[k, pl.ds(c, 1), :]
            edge_y = gy_ref[:, pl.ds(k * components + c, 1)]
            none_x = jnp.zeros_like(edge_x)
            none_y = jnp.zeros_like(edge_y)
            low_x = jnp.broadcast_to(jnp.where(first_x, none_x, edge_x), (width_x, width_y))
            high_x = jnp.broadcast_to(jnp.where(first_x, edge_x, none_x), (width_x, width_y))
            low_y = jnp.broadcast_to(jnp.where(first_y, none_y, edge_y), (width_x, width_y))
            high_y = jnp.broadcast_to(jnp.where(first_y, edge_y, none_y), (width_x, width_y))
            next_x = jnp.where(rows == width_x - 1, high_x, pltpu.roll(plane, width_x - 1, 0))
            prev_x = jnp.where(rows == 0, low_x, pltpu.roll(plane, 1, 0))
            next_y = jnp.where(cols == width_y - 1, high_y, pltpu.roll(plane, width_y - 1, 1))
            prev_y = jnp.where(cols == 0, low_y, pltpu.roll(plane, 1, 1))
            neighbours = next_x + prev_x + next_y + prev_y
            o_ref[k, c] = plane - 0.2 * (4.0 * plane - neighbours)


def finish_paired(fields, rate_re, rate_im, before, after, got, below, above, lower):
    layers, components, width_x, width_y = fields.shape
    flags = jnp.stack(
        [lower.astype(jnp.int32), lax.axis_index("px"), lax.axis_index("py")]
    ).astype(jnp.int32)
    smem = pl.BlockSpec(memory_space=pltpu.SMEM)
    vmem = pl.BlockSpec(memory_space=pltpu.VMEM)
    edge_x = jax.ShapeDtypeStruct((layers, components, width_y), jnp.float32)
    edge_y = jax.ShapeDtypeStruct((width_x, layers * components), jnp.float32)
    combined, send_x, send_y = pl.pallas_call(
        last_sweep_kernel,
        in_specs=[smem] + [vmem] * 12,
        out_specs=(vmem, vmem, vmem),
        out_shape=(jax.ShapeDtypeStruct(fields.shape, jnp.float32), edge_x, edge_y),
    )(flags, fields, rate_re, rate_im, *before, *after, *below, *above, got)
    got_x = lax.ppermute(send_x, "px", [(0, 1), (1, 0)])
    got_y = lax.ppermute(send_y, "py", [(0, 1), (1, 0)])
    return pl.pallas_call(
        paired_stencil_kernel,
        in_specs=[smem, vmem, vmem, vmem],
        out_specs=vmem,
        out_shape=jax.ShapeDtypeStruct(fields.shape, jnp.float32),
    )(flags, combined, got_x, got_y)


def shards(source, phase, attenuation, pml_level, recv_values, recv_slab, recv_lateral, recv_layer):
    layers, components, width_x, width_y = source.shape
    shot_count = components // 2
    slab_count = lax.axis_size("slab")
    depth_total = layers * slab_count

    damping = attenuation + 0.5 / depth_total * pml_level.astype(jnp.float32)[None, :, :]
    amplitude = jnp.exp(-damping)
    rate_re = amplitude * jnp.cos(phase)
    rate_im = amplitude * jnp.sin(phase)

    prod_down = [(rate_re[0], rate_im[0])]
    for k in range(1, layers):
        prod_down.append(complex_times(rate_re[k], rate_im[k], *prod_down[-1]))
    levels = block_products(*prod_down[-1])

    forcing, levels = inject_receivers(
        source, recv_values, recv_slab, recv_lateral, recv_layer, levels
    )
    fields = forcing.reshape(layers, shot_count, 2, width_x, width_y)
    f_re = fields[:, :, 0]
    f_im = fields[:, :, 1]

    down = [None] * layers
    state = (f_re[0], f_im[0])
    down[0] = state
    for k in range(1, layers):
        t_re, t_im = complex_times(rate_re[k][None], rate_im[k][None], *state)
        state = (t_re + f_re[k], t_im + f_im[k])
        down[k] = state
    up = [None] * layers
    state = (f_re[layers - 1], f_im[layers - 1])
    up[layers - 1] = state
    for k in range(layers - 2, -1, -1):
        t_re, t_im = complex_times(rate_re[k][None], rate_im[k][None], *state)
        state = (t_re + f_re[k], t_im + f_im[k])
        up[k] = state

    if lax.axis_size("px") == 2 and lax.axis_size("py") == 2 and slab_count > 1:
        parts = entering_states(down[layers - 1], up[0], levels, defer_last=True)
        return finish_paired(forcing, rate_re, rate_im, *parts)
    (enter_re, enter_im), (below_re, below_im) = entering_states(down[layers - 1], up[0], levels)

    return finish(forcing, rate_re, rate_im, enter_re, enter_im, below_re, below_im)


def solution(mesh):
    in_specs = (
        P("slab", None, "px", "py"),
        P("slab", "px", "py"),
        P("slab", "px", "py"),
        P("px", "py"),
        P("px", "py", None, "slab"),
        P("px", "py", "slab", None),
        P("px", "py", "slab"),
        P("px", "py", "slab"),
    )
    out_specs = P("slab", None, "px", "py")
    return jax.shard_map(shards, mesh=mesh, in_specs=in_specs, out_specs=out_specs, check_vma=False)
```

```python
import jax
import jax.numpy as jnp
from jax import lax
from jax.sharding import PartitionSpec as P
from jax.experimental import pallas as pl
from jax.experimental.pallas import tpu as pltpu


def from_behind(array, axis, by):
    count = lax.axis_size(axis)
    pairs = [(i, i + by) for i in range(count) if 0 <= i + by < count]
    return lax.ppermute(array, axis, pairs)


def complex_times(a_re, a_im, b_re, b_im):
    return a_re * b_re - a_im * b_im, a_re * b_im + a_im * b_re


def inject_receivers(source, recv_values, recv_slab, recv_lateral, recv_layer, levels):
    layers, components, width_x, width_y = source.shape
    slab_count = lax.axis_size("slab")
    plane_size = width_x * width_y
    rows_here = recv_values.shape[3]
    capacity = rows_here // min(8, slab_count)
    values = recv_values[0, 0]
    target_slab = recv_slab[0, 0, :, 0]
    position = recv_layer[0, 0] * plane_size + recv_lateral[0, 0]
    order = jnp.arange(rows_here, dtype=jnp.int32)
    same_before = (target_slab[:, None] == target_slab[None, :]) & (order[None, :] < order[:, None])
    ranking = jnp.sum(same_before.astype(jnp.int32), axis=1)
    target_slot = target_slab * capacity + ranking
    rows = jnp.concatenate([values, position.astype(jnp.float32)[None, :]], axis=0)
    high = lax.reduce_precision(rows, exponent_bits=8, mantissa_bits=7)
    rest = rows - high
    middle = lax.reduce_precision(rest, exponent_bits=8, mantissa_bits=7)
    parts = jnp.stack([high, middle, rest - middle], axis=0).astype(jnp.bfloat16)
    spots = (
        target_slot[:, None] == jnp.arange(slab_count * capacity, dtype=jnp.int32)[None, :]
    ).astype(jnp.bfloat16)
    placed = jnp.dot(
        parts.reshape(3 * (components + 1), rows_here), spots, preferred_element_type=jnp.float32
    ).reshape(3, components + 1, slab_count * capacity)
    send_rows = (placed[0] + placed[1]) + placed[2]
    got_rows = lax.all_to_all(send_rows, "slab", split_axis=1, concat_axis=1, tiled=True)
    inject_values = got_rows[:components]
    inject_places = got_rows[components].astype(jnp.int32)
    row_of = inject_places // width_y
    col_of = inject_places % width_y
    pick_rows = (
        row_of[None, :] == jnp.arange(layers * width_x, dtype=jnp.int32)[:, None]
    ).astype(jnp.bfloat16)
    pick_cols = col_of[:, None] == jnp.arange(width_y, dtype=jnp.int32)[None, :]
    high = lax.reduce_precision(inject_values, exponent_bits=8, mantissa_bits=7)
    pieces = jnp.stack([high, inject_values - high], axis=0)
    spread = jnp.where(pick_cols[None, None, :, :], pieces[:, :, :, None], 0.0)
    spread = jnp.transpose(spread, (2, 0, 1, 3)).reshape(
        slab_count * capacity, 2 * components * width_y
    )
    added = jnp.dot(pick_rows, spread.astype(jnp.bfloat16), preferred_element_type=jnp.float32)
    added = added.reshape(layers * width_x, 2, components * width_y)
    added = added[:, 0] + added[:, 1]
    added = jnp.transpose(added.reshape(layers, width_x, components, width_y), (0, 2, 1, 3))
    return source + added, levels


def exchange(array, step):
    count = lax.axis_size("slab")
    return lax.ppermute(array, "slab", [(i, i ^ step) for i in range(count)])


def block_products(a_re, a_im):
    slab_count = lax.axis_size("slab")
    here = lax.axis_index("slab")
    one = jnp.ones_like(a_re)
    zero = jnp.zeros_like(a_re)
    total = (a_re, a_im)
    below = (one, zero)
    above = (one, zero)
    levels = []
    step = 1
    while 2 * step < slab_count:
        got = exchange(jnp.stack(total, axis=0), step)
        partner = (got[0], got[1])
        levels.append((total, partner, below, above))
        lower = (here & step) == 0
        grown_below = complex_times(*below, *partner)
        grown_above = complex_times(*above, *partner)
        below = (jnp.where(lower, below[0], grown_below[0]), jnp.where(lower, below[1], grown_below[1]))
        above = (jnp.where(lower, grown_above[0], above[0]), jnp.where(lower, grown_above[1], above[1]))
        total = complex_times(*total, *partner)
        step *= 2
    levels.append((None, None, below, above))
    return levels


def entering_states(down_b, up_b, levels, defer_last=False):
    slab_count = lax.axis_size("slab")
    here = lax.axis_index("slab")
    shots = down_b[0].shape[0]
    before = (jnp.zeros_like(down_b[0]), jnp.zeros_like(down_b[1]))
    after = (jnp.zeros_like(up_b[0]), jnp.zeros_like(up_b[1]))
    step = 1
    level = 0
    while step < slab_count:
        lower = (here & step) == 0
        total, partner, below, above = levels[level]
        if 2 * step < slab_count:
            got = exchange(jnp.concatenate([*down_b, *up_b], axis=0), step)
            pd = (got[:shots], got[shots : 2 * shots])
            pu = (got[2 * shots : 3 * shots], got[3 * shots :])
            t_re, t_im = total[0][None], total[1][None]
            q_re, q_im = partner[0][None], partner[1][None]
            first = (jnp.where(lower, q_re, t_re), jnp.where(lower, q_im, t_im))
            inner = (jnp.where(lower, down_b[0], pd[0]), jnp.where(lower, down_b[1], pd[1]))
            outer = (jnp.where(lower, pd[0], down_b[0]), jnp.where(lower, pd[1], down_b[1]))
            m_re, m_im = complex_times(*first, *inner)
            new_down = (m_re + outer[0], m_im + outer[1])
            first = (jnp.where(lower, t_re, q_re), jnp.where(lower, t_im, q_im))
            inner = (jnp.where(lower, pu[0], up_b[0]), jnp.where(lower, pu[1], up_b[1]))
            outer = (jnp.where(lower, up_b[0], pu[0]), jnp.where(lower, up_b[1], pu[1]))
            m_re, m_im = complex_times(*first, *inner)
            new_up = (m_re + outer[0], m_im + outer[1])
        else:
            send = jnp.concatenate(
                [jnp.where(lower, down_b[0], up_b[0]), jnp.where(lower, down_b[1], up_b[1])], axis=0
            )
            got = exchange(send, step)
            if defer_last:
                return before, after, got, below, above, lower
            pd = (got[:shots], got[shots:])
            pu = pd
        g_re, g_im = complex_times(below[0][None], below[1][None], *pd)
        before = (
            jnp.where(lower, before[0], g_re + before[0]),
            jnp.where(lower, before[1], g_im + before[1]),
        )
        g_re, g_im = complex_times(above[0][None], above[1][None], *pu)
        after = (
            jnp.where(lower, g_re + after[0], after[0]),
            jnp.where(lower, g_im + after[1], after[1]),
        )
        if 2 * step < slab_count:
            down_b, up_b = new_down, new_up
        step *= 2
        level += 1
    if defer_last:
        return before, after, None, None, None, None
    return before, after


def edge_pair(last, first, axis):
    count = lax.axis_size(axis)
    if count == 2:
        here = lax.axis_index(axis)
        got = lax.ppermute(jnp.where(here == 0, last, first), axis, [(0, 1), (1, 0)])
        zero = jnp.zeros_like(got)
        return jnp.where(here == 1, got, zero), jnp.where(here == 0, got, zero)
    return from_behind(last, axis, 1), from_behind(first, axis, -1)


def sweep_kernel(f_ref, rr_ref, ri_ref, er_ref, ei_ref, br_ref, bi_ref,
                 c_ref, x0_ref, x1_ref, y0_ref, y1_ref):
    layers = f_ref.shape[0]
    shots = er_ref.shape[0]
    downs = []
    for s in range(shots):
        w_re, w_im = er_ref[s], ei_ref[s]
        per_layer = []
        for k in range(layers):
            t_re, t_im = complex_times(rr_ref[k], ri_ref[k], w_re, w_im)
            w_re, w_im = t_re + f_ref[k, 2 * s], t_im + f_ref[k, 2 * s + 1]
            per_layer.append((w_re, w_im))
        downs.append(per_layer)
    for s in range(shots):
        v_re, v_im = br_ref[s], bi_ref[s]
        for k in range(layers - 1, -1, -1):
            t_re, t_im = complex_times(rr_ref[k], ri_ref[k], v_re, v_im)
            f_re, f_im = f_ref[k, 2 * s], f_ref[k, 2 * s + 1]
            v_re, v_im = t_re + f_re, t_im + f_im
            d_re, d_im = downs[s][k]
            for part, plane in ((0, d_re + v_re - f_re), (1, d_im + v_im - f_im)):
                c = 2 * s + part
                c_ref[k, c] = plane
                x0_ref[k, pl.ds(c, 1), :] = plane[0:1, :]
                x1_ref[k, pl.ds(c, 1), :] = plane[-1:, :]
                flipped = jnp.transpose(plane)
                y0_ref[k, pl.ds(c, 1), :] = flipped[0:1, :]
                y1_ref[k, pl.ds(c, 1), :] = flipped[-1:, :]


def stencil_kernel(c_ref, lx_ref, hx_ref, ly_ref, hy_ref, o_ref):
    layers, components, width_x, width_y = c_ref.shape
    rows = lax.broadcasted_iota(jnp.int32, (width_x, width_y), 0)
    cols = lax.broadcasted_iota(jnp.int32, (width_x, width_y), 1)
    for k in range(layers):
        for c in range(components):
            plane = c_ref[k, c]
            low_x = jnp.broadcast_to(lx_ref[k, pl.ds(c, 1), :], (width_x, width_y))
            high_x = jnp.broadcast_to(hx_ref[k, pl.ds(c, 1), :], (width_x, width_y))
            low_y = jnp.transpose(jnp.broadcast_to(ly_ref[k, pl.ds(c, 1), :], (width_y, width_x)))
            high_y = jnp.transpose(jnp.broadcast_to(hy_ref[k, pl.ds(c, 1), :], (width_y, width_x)))
            next_x = jnp.where(rows == width_x - 1, high_x, pltpu.roll(plane, width_x - 1, 0))
            prev_x = jnp.where(rows == 0, low_x, pltpu.roll(plane, 1, 0))
            next_y = jnp.where(cols == width_y - 1, high_y, pltpu.roll(plane, width_y - 1, 1))
            prev_y = jnp.where(cols == 0, low_y, pltpu.roll(plane, 1, 1))
            neighbours = next_x + prev_x + next_y + prev_y
            o_ref[k, c] = plane - 0.2 * (4.0 * plane - neighbours)


def finish(fields, rate_re, rate_im, enter_re, enter_im, below_re, below_im):
    layers, components, width_x, width_y = fields.shape
    edge_x = jax.ShapeDtypeStruct((layers, components, width_y), jnp.float32)
    edge_y = jax.ShapeDtypeStruct((layers, components, width_x), jnp.float32)
    combined, x0, x1, y0, y1 = pl.pallas_call(
        sweep_kernel,
        out_shape=(jax.ShapeDtypeStruct(fields.shape, jnp.float32), edge_x, edge_x, edge_y, edge_y),
    )(fields, rate_re, rate_im, enter_re, enter_im, below_re, below_im)
    from_low_x, from_high_x = edge_pair(x1, x0, "px")
    from_low_y, from_high_y = edge_pair(y1, y0, "py")
    return pl.pallas_call(
        stencil_kernel,
        out_shape=jax.ShapeDtypeStruct(fields.shape, jnp.float32),
    )(combined, from_low_x, from_high_x, from_low_y, from_high_y)


def last_sweep_kernel(flag_ref, f_ref, rr_ref, ri_ref, br_ref, bi_ref, ar_ref, ai_ref,
                      lr_ref, li_ref, hr_ref, hi_ref, got_ref, c_ref, sx_ref, sy_ref):
    layers = f_ref.shape[0]
    shots = br_ref.shape[0]
    lower = flag_ref[0] == 1
    first_x = flag_ref[1] == 0
    first_y = flag_ref[2] == 0
    for s in range(shots):
        p_re, p_im = got_ref[s], got_ref[shots + s]
        g_re, g_im = complex_times(lr_ref[...], li_ref[...], p_re, p_im)
        w_re = jnp.where(lower, br_ref[s], g_re + br_ref[s])
        w_im = jnp.where(lower, bi_ref[s], g_im + bi_ref[s])
        g_re, g_im = complex_times(hr_ref[...], hi_ref[...], p_re, p_im)
        v_re = jnp.where(lower, g_re + ar_ref[s], ar_ref[s])
        v_im = jnp.where(lower, g_im + ai_ref[s], ai_ref[s])
        downs = []
        for k in range(layers):
            t_re, t_im = complex_times(rr_ref[k], ri_ref[k], w_re, w_im)
            w_re, w_im = t_re + f_ref[k, 2 * s], t_im + f_ref[k, 2 * s + 1]
            downs.append((w_re, w_im))
        for k in range(layers - 1, -1, -1):
            t_re, t_im = complex_times(rr_ref[k], ri_ref[k], v_re, v_im)
            f_re, f_im = f_ref[k, 2 * s], f_ref[k, 2 * s + 1]
            v_re, v_im = t_re + f_re, t_im + f_im
            d_re, d_im = downs[k]
            for part, plane in ((0, d_re + v_re - f_re), (1, d_im + v_im - f_im)):
                c = 2 * s + part
                c_ref[k, c] = plane
                sx_ref[k, pl.ds(c, 1), :] = jnp.where(first_x, plane[-1:, :], plane[0:1, :])
                flipped = jnp.transpose(plane)
                sy_ref[k, pl.ds(c, 1), :] = jnp.where(first_y, flipped[-1:, :], flipped[0:1, :])


def paired_stencil_kernel(flag_ref, c_ref, gx_ref, gy_ref, o_ref):
    layers, components, width_x, width_y = c_ref.shape
    rows = lax.broadcasted_iota(jnp.int32, (width_x, width_y), 0)
    cols = lax.broadcasted_iota(jnp.int32, (width_x, width_y), 1)
    side_rows = lax.broadcasted_iota(jnp.int32, (width_y, width_x), 0)
    first_x = flag_ref[1] == 0
    first_y = flag_ref[2] == 0
    for k in range(layers):
        for c in range(components):
            plane = c_ref[k, c]
            edge_x = gx_ref[k, pl.ds(c, 1), :]
            edge_y = jnp.broadcast_to(gy_ref[k, pl.ds(c, 1), :], (width_y, width_x))
            none_x = jnp.zeros_like(edge_x)
            low_x = jnp.broadcast_to(jnp.where(first_x, none_x, edge_x), (width_x, width_y))
            high_x = jnp.broadcast_to(jnp.where(first_x, edge_x, none_x), (width_x, width_y))
            side = jnp.where(side_rows == jnp.where(first_y, width_y - 1, 0), edge_y, 0.0)
            next_x = jnp.where(rows == width_x - 1, high_x, pltpu.roll(plane, width_x - 1, 0))
            prev_x = jnp.where(rows == 0, low_x, pltpu.roll(plane, 1, 0))
            next_y = jnp.where(cols == width_y - 1, 0.0, pltpu.roll(plane, width_y - 1, 1))
            prev_y = jnp.where(cols == 0, 0.0, pltpu.roll(plane, 1, 1))
            neighbours = next_x + prev_x + next_y + prev_y + jnp.transpose(side)
            o_ref[k, c] = plane - 0.2 * (4.0 * plane - neighbours)


def finish_paired(fields, rate_re, rate_im, before, after, got, below, above, lower):
    layers, components, width_x, width_y = fields.shape
    flags = jnp.stack(
        [lower.astype(jnp.int32), lax.axis_index("px"), lax.axis_index("py")]
    ).astype(jnp.int32)
    smem = pl.BlockSpec(memory_space=pltpu.SMEM)
    vmem = pl.BlockSpec(memory_space=pltpu.VMEM)
    edge_x = jax.ShapeDtypeStruct((layers, components, width_y), jnp.float32)
    edge_y = jax.ShapeDtypeStruct((layers, components, width_x), jnp.float32)
    combined, send_x, send_y = pl.pallas_call(
        last_sweep_kernel,
        in_specs=[smem] + [vmem] * 12,
        out_specs=(vmem, vmem, vmem),
        out_shape=(jax.ShapeDtypeStruct(fields.shape, jnp.float32), edge_x, edge_y),
    )(flags, fields, rate_re, rate_im, *before, *after, *below, *above, got)
    got_x = lax.ppermute(send_x, "px", [(0, 1), (1, 0)])
    got_y = lax.ppermute(send_y, "py", [(0, 1), (1, 0)])
    return pl.pallas_call(
        paired_stencil_kernel,
        in_specs=[smem, vmem, vmem, vmem],
        out_specs=vmem,
        out_shape=jax.ShapeDtypeStruct(fields.shape, jnp.float32),
    )(flags, combined, got_x, got_y)


def shards(source, phase, attenuation, pml_level, recv_values, recv_slab, recv_lateral, recv_layer):
    layers, components, width_x, width_y = source.shape
    shot_count = components // 2
    slab_count = lax.axis_size("slab")
    depth_total = layers * slab_count

    damping = attenuation + 0.5 / depth_total * pml_level.astype(jnp.float32)[None, :, :]
    amplitude = jnp.exp(-damping)
    rate_re = amplitude * jnp.cos(phase)
    rate_im = amplitude * jnp.sin(phase)

    prod_down = [(rate_re[0], rate_im[0])]
    for k in range(1, layers):
        prod_down.append(complex_times(rate_re[k], rate_im[k], *prod_down[-1]))
    levels = block_products(*prod_down[-1])

    forcing, levels = inject_receivers(
        source, recv_values, recv_slab, recv_lateral, recv_layer, levels
    )
    fields = forcing.reshape(layers, shot_count, 2, width_x, width_y)
    f_re = fields[:, :, 0]
    f_im = fields[:, :, 1]

    down = [None] * layers
    state = (f_re[0], f_im[0])
    down[0] = state
    for k in range(1, layers):
        t_re, t_im = complex_times(rate_re[k][None], rate_im[k][None], *state)
        state = (t_re + f_re[k], t_im + f_im[k])
        down[k] = state
    up = [None] * layers
    state = (f_re[layers - 1], f_im[layers - 1])
    up[layers - 1] = state
    for k in range(layers - 2, -1, -1):
        t_re, t_im = complex_times(rate_re[k][None], rate_im[k][None], *state)
        state = (t_re + f_re[k], t_im + f_im[k])
        up[k] = state

    if lax.axis_size("px") == 2 and lax.axis_size("py") == 2 and slab_count > 1:
        parts = entering_states(down[layers - 1], up[0], levels, defer_last=True)
        return finish_paired(forcing, rate_re, rate_im, *parts)
    (enter_re, enter_im), (below_re, below_im) = entering_states(down[layers - 1], up[0], levels)

    return finish(forcing, rate_re, rate_im, enter_re, enter_im, below_re, below_im)


def solution(mesh):
    in_specs = (
        P("slab", None, "px", "py"),
        P("slab", "px", "py"),
        P("slab", "px", "py"),
        P("px", "py"),
        P("px", "py", None, "slab"),
        P("px", "py", "slab", None),
        P("px", "py", "slab"),
        P("px", "py", "slab"),
    )
    out_specs = P("slab", None, "px", "py")
    return jax.shard_map(shards, mesh=mesh, in_specs=in_specs, out_specs=out_specs, check_vma=False)
```

```python
import jax
import jax.numpy as jnp
from jax import lax
from jax.sharding import PartitionSpec as P
from jax.experimental import pallas as pl
from jax.experimental.pallas import tpu as pltpu


def from_behind(array, axis, by):
    count = lax.axis_size(axis)
    pairs = [(i, i + by) for i in range(count) if 0 <= i + by < count]
    return lax.ppermute(array, axis, pairs)


def complex_times(a_re, a_im, b_re, b_im):
    return a_re * b_re - a_im * b_im, a_re * b_im + a_im * b_re


def inject_receivers(source, recv_values, recv_slab, recv_lateral, recv_layer, levels):
    layers, components, width_x, width_y = source.shape
    slab_count = lax.axis_size("slab")
    plane_size = width_x * width_y
    rows_here = recv_values.shape[3]
    capacity = rows_here // min(8, slab_count)
    values = recv_values[0, 0]
    target_slab = recv_slab[0, 0, :, 0]
    position = recv_layer[0, 0] * plane_size + recv_lateral[0, 0]
    order = jnp.arange(rows_here, dtype=jnp.int32)
    same_before = (target_slab[:, None] == target_slab[None, :]) & (order[None, :] < order[:, None])
    ranking = jnp.sum(same_before.astype(jnp.int32), axis=1)
    target_slot = target_slab * capacity + ranking
    rows = jnp.concatenate([values, position.astype(jnp.float32)[None, :]], axis=0)
    high = lax.reduce_precision(rows, exponent_bits=8, mantissa_bits=7)
    rest = rows - high
    middle = lax.reduce_precision(rest, exponent_bits=8, mantissa_bits=7)
    parts = jnp.stack([high, middle, rest - middle], axis=0).astype(jnp.bfloat16)
    spots = (
        target_slot[:, None] == jnp.arange(slab_count * capacity, dtype=jnp.int32)[None, :]
    ).astype(jnp.bfloat16)
    placed = jnp.dot(
        parts.reshape(3 * (components + 1), rows_here), spots, preferred_element_type=jnp.float32
    ).reshape(3, components + 1, slab_count * capacity)
    send_rows = (placed[0] + placed[1]) + placed[2]
    got_rows = lax.all_to_all(send_rows, "slab", split_axis=1, concat_axis=1, tiled=True)
    inject_values = got_rows[:components]
    inject_places = got_rows[components].astype(jnp.int32)
    row_of = inject_places // width_y
    col_of = inject_places % width_y
    pick_rows = (
        row_of[None, :] == jnp.arange(layers * width_x, dtype=jnp.int32)[:, None]
    ).astype(jnp.bfloat16)
    pick_cols = col_of[:, None] == jnp.arange(width_y, dtype=jnp.int32)[None, :]
    high = lax.reduce_precision(inject_values, exponent_bits=8, mantissa_bits=7)
    pieces = jnp.stack([high, inject_values - high], axis=0)
    spread = jnp.where(pick_cols[None, None, :, :], pieces[:, :, :, None], 0.0)
    spread = jnp.transpose(spread, (2, 0, 1, 3)).reshape(
        slab_count * capacity, 2 * components * width_y
    )
    added = jnp.dot(pick_rows, spread.astype(jnp.bfloat16), preferred_element_type=jnp.float32)
    added = added.reshape(layers * width_x, 2, components * width_y)
    added = added[:, 0] + added[:, 1]
    added = jnp.transpose(added.reshape(layers, width_x, components, width_y), (0, 2, 1, 3))
    return source + added, levels


def exchange(array, step):
    count = lax.axis_size("slab")
    return lax.ppermute(array, "slab", [(i, i ^ step) for i in range(count)])


def block_products(a_re, a_im):
    slab_count = lax.axis_size("slab")
    here = lax.axis_index("slab")
    one = jnp.ones_like(a_re)
    zero = jnp.zeros_like(a_re)
    total = (a_re, a_im)
    below = (one, zero)
    above = (one, zero)
    levels = []
    step = 1
    while 2 * step < slab_count:
        got = exchange(jnp.stack(total, axis=0), step)
        partner = (got[0], got[1])
        levels.append((total, partner, below, above))
        lower = (here & step) == 0
        grown_below = complex_times(*below, *partner)
        grown_above = complex_times(*above, *partner)
        below = (jnp.where(lower, below[0], grown_below[0]), jnp.where(lower, below[1], grown_below[1]))
        above = (jnp.where(lower, grown_above[0], above[0]), jnp.where(lower, grown_above[1], above[1]))
        total = complex_times(*total, *partner)
        step *= 2
    levels.append((None, None, below, above))
    return levels


def entering_states(down_b, up_b, levels, defer_last=False):
    slab_count = lax.axis_size("slab")
    here = lax.axis_index("slab")
    shots = down_b[0].shape[0]
    before = (jnp.zeros_like(down_b[0]), jnp.zeros_like(down_b[1]))
    after = (jnp.zeros_like(up_b[0]), jnp.zeros_like(up_b[1]))
    step = 1
    level = 0
    while step < slab_count:
        lower = (here & step) == 0
        total, partner, below, above = levels[level]
        if 2 * step < slab_count:
            got = exchange(jnp.concatenate([*down_b, *up_b], axis=0), step)
            pd = (got[:shots], got[shots : 2 * shots])
            pu = (got[2 * shots : 3 * shots], got[3 * shots :])
            t_re, t_im = total[0][None], total[1][None]
            q_re, q_im = partner[0][None], partner[1][None]
            first = (jnp.where(lower, q_re, t_re), jnp.where(lower, q_im, t_im))
            inner = (jnp.where(lower, down_b[0], pd[0]), jnp.where(lower, down_b[1], pd[1]))
            outer = (jnp.where(lower, pd[0], down_b[0]), jnp.where(lower, pd[1], down_b[1]))
            m_re, m_im = complex_times(*first, *inner)
            new_down = (m_re + outer[0], m_im + outer[1])
            first = (jnp.where(lower, t_re, q_re), jnp.where(lower, t_im, q_im))
            inner = (jnp.where(lower, pu[0], up_b[0]), jnp.where(lower, pu[1], up_b[1]))
            outer = (jnp.where(lower, up_b[0], pu[0]), jnp.where(lower, up_b[1], pu[1]))
            m_re, m_im = complex_times(*first, *inner)
            new_up = (m_re + outer[0], m_im + outer[1])
        else:
            send = jnp.concatenate(
                [jnp.where(lower, down_b[0], up_b[0]), jnp.where(lower, down_b[1], up_b[1])], axis=0
            )
            got = exchange(send, step)
            if defer_last:
                return before, after, got, below, above, lower
            pd = (got[:shots], got[shots:])
            pu = pd
        g_re, g_im = complex_times(below[0][None], below[1][None], *pd)
        before = (
            jnp.where(lower, before[0], g_re + before[0]),
            jnp.where(lower, before[1], g_im + before[1]),
        )
        g_re, g_im = complex_times(above[0][None], above[1][None], *pu)
        after = (
            jnp.where(lower, g_re + after[0], after[0]),
            jnp.where(lower, g_im + after[1], after[1]),
        )
        if 2 * step < slab_count:
            down_b, up_b = new_down, new_up
        step *= 2
        level += 1
    if defer_last:
        return before, after, None, None, None, None
    return before, after


def edge_pair(last, first, axis):
    count = lax.axis_size(axis)
    if count == 2:
        here = lax.axis_index(axis)
        got = lax.ppermute(jnp.where(here == 0, last, first), axis, [(0, 1), (1, 0)])
        zero = jnp.zeros_like(got)
        return jnp.where(here == 1, got, zero), jnp.where(here == 0, got, zero)
    return from_behind(last, axis, 1), from_behind(first, axis, -1)


def sweep_kernel(f_ref, rr_ref, ri_ref, er_ref, ei_ref, br_ref, bi_ref,
                 c_ref, x0_ref, x1_ref, y0_ref, y1_ref):
    layers = f_ref.shape[0]
    shots = er_ref.shape[0]
    downs = []
    for s in range(shots):
        w_re, w_im = er_ref[s], ei_ref[s]
        per_layer = []
        for k in range(layers):
            t_re, t_im = complex_times(rr_ref[k], ri_ref[k], w_re, w_im)
            w_re, w_im = t_re + f_ref[k, 2 * s], t_im + f_ref[k, 2 * s + 1]
            per_layer.append((w_re, w_im))
        downs.append(per_layer)
    for s in range(shots):
        v_re, v_im = br_ref[s], bi_ref[s]
        for k in range(layers - 1, -1, -1):
            t_re, t_im = complex_times(rr_ref[k], ri_ref[k], v_re, v_im)
            f_re, f_im = f_ref[k, 2 * s], f_ref[k, 2 * s + 1]
            v_re, v_im = t_re + f_re, t_im + f_im
            d_re, d_im = downs[s][k]
            for part, plane in ((0, d_re + v_re - f_re), (1, d_im + v_im - f_im)):
                c = 2 * s + part
                c_ref[k, c] = plane
                x0_ref[k, pl.ds(c, 1), :] = plane[0:1, :]
                x1_ref[k, pl.ds(c, 1), :] = plane[-1:, :]
                flipped = jnp.transpose(plane)
                y0_ref[k, pl.ds(c, 1), :] = flipped[0:1, :]
                y1_ref[k, pl.ds(c, 1), :] = flipped[-1:, :]


def stencil_kernel(c_ref, lx_ref, hx_ref, ly_ref, hy_ref, o_ref):
    layers, components, width_x, width_y = c_ref.shape
    rows = lax.broadcasted_iota(jnp.int32, (width_x, width_y), 0)
    cols = lax.broadcasted_iota(jnp.int32, (width_x, width_y), 1)
    for k in range(layers):
        for c in range(components):
            plane = c_ref[k, c]
            low_x = jnp.broadcast_to(lx_ref[k, pl.ds(c, 1), :], (width_x, width_y))
            high_x = jnp.broadcast_to(hx_ref[k, pl.ds(c, 1), :], (width_x, width_y))
            low_y = jnp.transpose(jnp.broadcast_to(ly_ref[k, pl.ds(c, 1), :], (width_y, width_x)))
            high_y = jnp.transpose(jnp.broadcast_to(hy_ref[k, pl.ds(c, 1), :], (width_y, width_x)))
            next_x = jnp.where(rows == width_x - 1, high_x, pltpu.roll(plane, width_x - 1, 0))
            prev_x = jnp.where(rows == 0, low_x, pltpu.roll(plane, 1, 0))
            next_y = jnp.where(cols == width_y - 1, high_y, pltpu.roll(plane, width_y - 1, 1))
            prev_y = jnp.where(cols == 0, low_y, pltpu.roll(plane, 1, 1))
            neighbours = next_x + prev_x + next_y + prev_y
            o_ref[k, c] = plane - 0.2 * (4.0 * plane - neighbours)


def finish(fields, rate_re, rate_im, enter_re, enter_im, below_re, below_im):
    layers, components, width_x, width_y = fields.shape
    edge_x = jax.ShapeDtypeStruct((layers, components, width_y), jnp.float32)
    edge_y = jax.ShapeDtypeStruct((layers, components, width_x), jnp.float32)
    combined, x0, x1, y0, y1 = pl.pallas_call(
        sweep_kernel,
        out_shape=(jax.ShapeDtypeStruct(fields.shape, jnp.float32), edge_x, edge_x, edge_y, edge_y),
    )(fields, rate_re, rate_im, enter_re, enter_im, below_re, below_im)
    from_low_x, from_high_x = edge_pair(x1, x0, "px")
    from_low_y, from_high_y = edge_pair(y1, y0, "py")
    return pl.pallas_call(
        stencil_kernel,
        out_shape=jax.ShapeDtypeStruct(fields.shape, jnp.float32),
    )(combined, from_low_x, from_high_x, from_low_y, from_high_y)


def last_sweep_kernel(flag_ref, f_ref, rr_ref, ri_ref, br_ref, bi_ref, ar_ref, ai_ref,
                      lr_ref, li_ref, hr_ref, hi_ref, got_ref, c_ref, sx_ref, sy_ref):
    layers = f_ref.shape[0]
    shots = br_ref.shape[0]
    lower = flag_ref[0] == 1
    first_x = flag_ref[1] == 0
    first_y = flag_ref[2] == 0
    for s in range(shots):
        p_re, p_im = got_ref[s], got_ref[shots + s]
        g_re, g_im = complex_times(lr_ref[...], li_ref[...], p_re, p_im)
        w_re = jnp.where(lower, br_ref[s], g_re + br_ref[s])
        w_im = jnp.where(lower, bi_ref[s], g_im + bi_ref[s])
        g_re, g_im = complex_times(hr_ref[...], hi_ref[...], p_re, p_im)
        v_re = jnp.where(lower, g_re + ar_ref[s], ar_ref[s])
        v_im = jnp.where(lower, g_im + ai_ref[s], ai_ref[s])
        downs = []
        for k in range(layers):
            t_re, t_im = complex_times(rr_ref[k], ri_ref[k], w_re, w_im)
            w_re, w_im = t_re + f_ref[k, 2 * s], t_im + f_ref[k, 2 * s + 1]
            downs.append((w_re, w_im))
        for k in range(layers - 1, -1, -1):
            t_re, t_im = complex_times(rr_ref[k], ri_ref[k], v_re, v_im)
            f_re, f_im = f_ref[k, 2 * s], f_ref[k, 2 * s + 1]
            v_re, v_im = t_re + f_re, t_im + f_im
            d_re, d_im = downs[k]
            for part, plane in ((0, d_re + v_re - f_re), (1, d_im + v_im - f_im)):
                c = 2 * s + part
                c_ref[k, c] = plane
                sx_ref[k, pl.ds(c, 1), :] = jnp.where(first_x, plane[-1:, :], plane[0:1, :])
                flipped = jnp.transpose(plane)
                sy_ref[k, pl.ds(c, 1), :] = jnp.where(first_y, flipped[-1:, :], flipped[0:1, :])


def paired_stencil_kernel(flag_ref, c_ref, gx_ref, gy_ref, o_ref):
    layers, components, width_x, width_y = c_ref.shape
    rows = lax.broadcasted_iota(jnp.int32, (width_x, width_y), 0)
    cols = lax.broadcasted_iota(jnp.int32, (width_x, width_y), 1)
    side_rows = lax.broadcasted_iota(jnp.int32, (width_y, width_x), 0)
    first_x = flag_ref[1] == 0
    first_y = flag_ref[2] == 0
    for k in range(layers):
        for c in range(components):
            plane = c_ref[k, c]
            edge_x = gx_ref[k, pl.ds(c, 1), :]
            edge_y = jnp.broadcast_to(gy_ref[k, pl.ds(c, 1), :], (width_y, width_x))
            none_x = jnp.zeros_like(edge_x)
            low_x = jnp.broadcast_to(jnp.where(first_x, none_x, edge_x), (width_x, width_y))
            high_x = jnp.broadcast_to(jnp.where(first_x, edge_x, none_x), (width_x, width_y))
            side = jnp.where(side_rows == jnp.where(first_y, width_y - 1, 0), edge_y, 0.0)
            next_x = jnp.where(rows == width_x - 1, high_x, pltpu.roll(plane, width_x - 1, 0))
            prev_x = jnp.where(rows == 0, low_x, pltpu.roll(plane, 1, 0))
            next_y = jnp.where(cols == width_y - 1, 0.0, pltpu.roll(plane, width_y - 1, 1))
            prev_y = jnp.where(cols == 0, 0.0, pltpu.roll(plane, 1, 1))
            neighbours = next_x + prev_x + next_y + prev_y + jnp.transpose(side)
            o_ref[k, c] = plane - 0.2 * (4.0 * plane - neighbours)


def finish_paired(fields, rate_re, rate_im, before, after, got, below, above, lower):
    layers, components, width_x, width_y = fields.shape
    flags = jnp.stack(
        [lower.astype(jnp.int32), lax.axis_index("px"), lax.axis_index("py")]
    ).astype(jnp.int32)
    smem = pl.BlockSpec(memory_space=pltpu.SMEM)
    vmem = pl.BlockSpec(memory_space=pltpu.VMEM)
    edge_x = jax.ShapeDtypeStruct((layers, components, width_y), jnp.float32)
    edge_y = jax.ShapeDtypeStruct((layers, components, width_x), jnp.float32)
    combined, send_x, send_y = pl.pallas_call(
        last_sweep_kernel,
        in_specs=[smem] + [vmem] * 12,
        out_specs=(vmem, vmem, vmem),
        out_shape=(jax.ShapeDtypeStruct(fields.shape, jnp.float32), edge_x, edge_y),
    )(flags, fields, rate_re, rate_im, *before, *after, *below, *above, got)
    got_x = lax.ppermute(send_x, "px", [(0, 1), (1, 0)])
    got_y = lax.ppermute(send_y, "py", [(0, 1), (1, 0)])
    plane_block = pl.BlockSpec((1, components, width_x, width_y), lambda k: (k, 0, 0, 0))
    edge_block = pl.BlockSpec((1, components, width_y), lambda k: (k, 0, 0))
    return pl.pallas_call(
        paired_stencil_kernel,
        grid=(layers,),
        in_specs=[smem, plane_block, edge_block, edge_block],
        out_specs=plane_block,
        out_shape=jax.ShapeDtypeStruct(fields.shape, jnp.float32),
    )(flags, combined, got_x, got_y)


def shards(source, phase, attenuation, pml_level, recv_values, recv_slab, recv_lateral, recv_layer):
    layers, components, width_x, width_y = source.shape
    shot_count = components // 2
    slab_count = lax.axis_size("slab")
    depth_total = layers * slab_count

    damping = attenuation + 0.5 / depth_total * pml_level.astype(jnp.float32)[None, :, :]
    amplitude = jnp.exp(-damping)
    rate_re = amplitude * jnp.cos(phase)
    rate_im = amplitude * jnp.sin(phase)

    prod_down = [(rate_re[0], rate_im[0])]
    for k in range(1, layers):
        prod_down.append(complex_times(rate_re[k], rate_im[k], *prod_down[-1]))
    levels = block_products(*prod_down[-1])

    forcing, levels = inject_receivers(
        source, recv_values, recv_slab, recv_lateral, recv_layer, levels
    )
    fields = forcing.reshape(layers, shot_count, 2, width_x, width_y)
    f_re = fields[:, :, 0]
    f_im = fields[:, :, 1]

    down = [None] * layers
    state = (f_re[0], f_im[0])
    down[0] = state
    for k in range(1, layers):
        t_re, t_im = complex_times(rate_re[k][None], rate_im[k][None], *state)
        state = (t_re + f_re[k], t_im + f_im[k])
        down[k] = state
    up = [None] * layers
    state = (f_re[layers - 1], f_im[layers - 1])
    up[layers - 1] = state
    for k in range(layers - 2, -1, -1):
        t_re, t_im = complex_times(rate_re[k][None], rate_im[k][None], *state)
        state = (t_re + f_re[k], t_im + f_im[k])
        up[k] = state

    if lax.axis_size("px") == 2 and lax.axis_size("py") == 2 and slab_count > 1:
        parts = entering_states(down[layers - 1], up[0], levels, defer_last=True)
        return finish_paired(forcing, rate_re, rate_im, *parts)
    (enter_re, enter_im), (below_re, below_im) = entering_states(down[layers - 1], up[0], levels)

    return finish(forcing, rate_re, rate_im, enter_re, enter_im, below_re, below_im)


def solution(mesh):
    in_specs = (
        P("slab", None, "px", "py"),
        P("slab", "px", "py"),
        P("slab", "px", "py"),
        P("px", "py"),
        P("px", "py", None, "slab"),
        P("px", "py", "slab", None),
        P("px", "py", "slab"),
        P("px", "py", "slab"),
    )
    out_specs = P("slab", None, "px", "py")
    return jax.shard_map(shards, mesh=mesh, in_specs=in_specs, out_specs=out_specs, check_vma=False)
```

```python
import jax
import jax.numpy as jnp
from jax import lax
from jax.sharding import PartitionSpec as P
from jax.experimental import pallas as pl
from jax.experimental.pallas import tpu as pltpu


def from_behind(array, axis, by):
    count = lax.axis_size(axis)
    pairs = [(i, i + by) for i in range(count) if 0 <= i + by < count]
    return lax.ppermute(array, axis, pairs)


def complex_times(a_re, a_im, b_re, b_im):
    return a_re * b_re - a_im * b_im, a_re * b_im + a_im * b_re


def inject_receivers(source, recv_values, recv_slab, recv_lateral, recv_layer, levels):
    layers, components, width_x, width_y = source.shape
    slab_count = lax.axis_size("slab")
    plane_size = width_x * width_y
    rows_here = recv_values.shape[3]
    capacity = rows_here // min(8, slab_count)
    values = recv_values[0, 0]
    target_slab = recv_slab[0, 0, :, 0]
    position = recv_layer[0, 0] * plane_size + recv_lateral[0, 0]
    order = jnp.arange(rows_here, dtype=jnp.int32)
    same_before = (target_slab[:, None] == target_slab[None, :]) & (order[None, :] < order[:, None])
    ranking = jnp.sum(same_before.astype(jnp.int32), axis=1)
    target_slot = target_slab * capacity + ranking
    rows = jnp.concatenate([values, position.astype(jnp.float32)[None, :]], axis=0)
    high = lax.reduce_precision(rows, exponent_bits=8, mantissa_bits=7)
    rest = rows - high
    middle = lax.reduce_precision(rest, exponent_bits=8, mantissa_bits=7)
    parts = jnp.stack([high, middle, rest - middle], axis=0).astype(jnp.bfloat16)
    spots = (
        target_slot[:, None] == jnp.arange(slab_count * capacity, dtype=jnp.int32)[None, :]
    ).astype(jnp.bfloat16)
    placed = jnp.dot(
        parts.reshape(3 * (components + 1), rows_here), spots, preferred_element_type=jnp.float32
    ).reshape(3, components + 1, slab_count * capacity)
    send_rows = (placed[0] + placed[1]) + placed[2]
    got_rows = lax.all_to_all(send_rows, "slab", split_axis=1, concat_axis=1, tiled=True)
    inject_values = got_rows[:components]
    inject_places = got_rows[components].astype(jnp.int32)
    row_of = inject_places // width_y
    col_of = inject_places % width_y
    pick_rows = (
        row_of[None, :] == jnp.arange(layers * width_x, dtype=jnp.int32)[:, None]
    ).astype(jnp.bfloat16)
    pick_cols = col_of[:, None] == jnp.arange(width_y, dtype=jnp.int32)[None, :]
    high = lax.reduce_precision(inject_values, exponent_bits=8, mantissa_bits=7)
    pieces = jnp.stack([high, inject_values - high], axis=0)
    spread = jnp.where(pick_cols[None, None, :, :], pieces[:, :, :, None], 0.0)
    spread = jnp.transpose(spread, (2, 0, 1, 3)).reshape(
        slab_count * capacity, 2 * components * width_y
    )
    added = jnp.dot(pick_rows, spread.astype(jnp.bfloat16), preferred_element_type=jnp.float32)
    added = added.reshape(layers * width_x, 2, components * width_y)
    added = added[:, 0] + added[:, 1]
    added = jnp.transpose(added.reshape(layers, width_x, components, width_y), (0, 2, 1, 3))
    return source + added, levels


def exchange(array, step):
    count = lax.axis_size("slab")
    return lax.ppermute(array, "slab", [(i, i ^ step) for i in range(count)])


def block_products(a_re, a_im):
    slab_count = lax.axis_size("slab")
    here = lax.axis_index("slab")
    one = jnp.ones_like(a_re)
    zero = jnp.zeros_like(a_re)
    total = (a_re, a_im)
    below = (one, zero)
    above = (one, zero)
    levels = []
    step = 1
    while 2 * step < slab_count:
        got = exchange(jnp.stack(total, axis=0), step)
        partner = (got[0], got[1])
        levels.append((total, partner, below, above))
        lower = (here & step) == 0
        grown_below = complex_times(*below, *partner)
        grown_above = complex_times(*above, *partner)
        below = (jnp.where(lower, below[0], grown_below[0]), jnp.where(lower, below[1], grown_below[1]))
        above = (jnp.where(lower, grown_above[0], above[0]), jnp.where(lower, grown_above[1], above[1]))
        total = complex_times(*total, *partner)
        step *= 2
    levels.append((None, None, below, above))
    return levels


def entering_states(down_b, up_b, levels, defer_last=False):
    slab_count = lax.axis_size("slab")
    here = lax.axis_index("slab")
    shots = down_b[0].shape[0]
    before = (jnp.zeros_like(down_b[0]), jnp.zeros_like(down_b[1]))
    after = (jnp.zeros_like(up_b[0]), jnp.zeros_like(up_b[1]))
    step = 1
    level = 0
    while step < slab_count:
        lower = (here & step) == 0
        total, partner, below, above = levels[level]
        if 2 * step < slab_count:
            got = exchange(jnp.concatenate([*down_b, *up_b], axis=0), step)
            pd = (got[:shots], got[shots : 2 * shots])
            pu = (got[2 * shots : 3 * shots], got[3 * shots :])
            t_re, t_im = total[0][None], total[1][None]
            q_re, q_im = partner[0][None], partner[1][None]
            first = (jnp.where(lower, q_re, t_re), jnp.where(lower, q_im, t_im))
            inner = (jnp.where(lower, down_b[0], pd[0]), jnp.where(lower, down_b[1], pd[1]))
            outer = (jnp.where(lower, pd[0], down_b[0]), jnp.where(lower, pd[1], down_b[1]))
            m_re, m_im = complex_times(*first, *inner)
            new_down = (m_re + outer[0], m_im + outer[1])
            first = (jnp.where(lower, t_re, q_re), jnp.where(lower, t_im, q_im))
            inner = (jnp.where(lower, pu[0], up_b[0]), jnp.where(lower, pu[1], up_b[1]))
            outer = (jnp.where(lower, up_b[0], pu[0]), jnp.where(lower, up_b[1], pu[1]))
            m_re, m_im = complex_times(*first, *inner)
            new_up = (m_re + outer[0], m_im + outer[1])
        else:
            send = jnp.concatenate(
                [jnp.where(lower, down_b[0], up_b[0]), jnp.where(lower, down_b[1], up_b[1])], axis=0
            )
            got = exchange(send, step)
            if defer_last:
                return before, after, got, below, above, lower
            pd = (got[:shots], got[shots:])
            pu = pd
        g_re, g_im = complex_times(below[0][None], below[1][None], *pd)
        before = (
            jnp.where(lower, before[0], g_re + before[0]),
            jnp.where(lower, before[1], g_im + before[1]),
        )
        g_re, g_im = complex_times(above[0][None], above[1][None], *pu)
        after = (
            jnp.where(lower, g_re + after[0], after[0]),
            jnp.where(lower, g_im + after[1], after[1]),
        )
        if 2 * step < slab_count:
            down_b, up_b = new_down, new_up
        step *= 2
        level += 1
    if defer_last:
        return before, after, None, None, None, None
    return before, after


def edge_pair(last, first, axis):
    count = lax.axis_size(axis)
    if count == 2:
        here = lax.axis_index(axis)
        got = lax.ppermute(jnp.where(here == 0, last, first), axis, [(0, 1), (1, 0)])
        zero = jnp.zeros_like(got)
        return jnp.where(here == 1, got, zero), jnp.where(here == 0, got, zero)
    return from_behind(last, axis, 1), from_behind(first, axis, -1)


def sweep_kernel(f_ref, rr_ref, ri_ref, er_ref, ei_ref, br_ref, bi_ref,
                 c_ref, x0_ref, x1_ref, y0_ref, y1_ref):
    layers = f_ref.shape[0]
    shots = er_ref.shape[0]
    downs = []
    for s in range(shots):
        w_re, w_im = er_ref[s], ei_ref[s]
        per_layer = []
        for k in range(layers):
            t_re, t_im = complex_times(rr_ref[k], ri_ref[k], w_re, w_im)
            w_re, w_im = t_re + f_ref[k, 2 * s], t_im + f_ref[k, 2 * s + 1]
            per_layer.append((w_re, w_im))
        downs.append(per_layer)
    for s in range(shots):
        v_re, v_im = br_ref[s], bi_ref[s]
        for k in range(layers - 1, -1, -1):
            t_re, t_im = complex_times(rr_ref[k], ri_ref[k], v_re, v_im)
            f_re, f_im = f_ref[k, 2 * s], f_ref[k, 2 * s + 1]
            v_re, v_im = t_re + f_re, t_im + f_im
            d_re, d_im = downs[s][k]
            for part, plane in ((0, d_re + v_re - f_re), (1, d_im + v_im - f_im)):
                c = 2 * s + part
                c_ref[k, c] = plane
                x0_ref[k, pl.ds(c, 1), :] = plane[0:1, :]
                x1_ref[k, pl.ds(c, 1), :] = plane[-1:, :]
                flipped = jnp.transpose(plane)
                y0_ref[k, pl.ds(c, 1), :] = flipped[0:1, :]
                y1_ref[k, pl.ds(c, 1), :] = flipped[-1:, :]


def stencil_kernel(c_ref, lx_ref, hx_ref, ly_ref, hy_ref, o_ref):
    layers, components, width_x, width_y = c_ref.shape
    rows = lax.broadcasted_iota(jnp.int32, (width_x, width_y), 0)
    cols = lax.broadcasted_iota(jnp.int32, (width_x, width_y), 1)
    for k in range(layers):
        for c in range(components):
            plane = c_ref[k, c]
            low_x = jnp.broadcast_to(lx_ref[k, pl.ds(c, 1), :], (width_x, width_y))
            high_x = jnp.broadcast_to(hx_ref[k, pl.ds(c, 1), :], (width_x, width_y))
            low_y = jnp.transpose(jnp.broadcast_to(ly_ref[k, pl.ds(c, 1), :], (width_y, width_x)))
            high_y = jnp.transpose(jnp.broadcast_to(hy_ref[k, pl.ds(c, 1), :], (width_y, width_x)))
            next_x = jnp.where(rows == width_x - 1, high_x, pltpu.roll(plane, width_x - 1, 0))
            prev_x = jnp.where(rows == 0, low_x, pltpu.roll(plane, 1, 0))
            next_y = jnp.where(cols == width_y - 1, high_y, pltpu.roll(plane, width_y - 1, 1))
            prev_y = jnp.where(cols == 0, low_y, pltpu.roll(plane, 1, 1))
            neighbours = next_x + prev_x + next_y + prev_y
            o_ref[k, c] = plane - 0.2 * (4.0 * plane - neighbours)


def finish(fields, rate_re, rate_im, enter_re, enter_im, below_re, below_im):
    layers, components, width_x, width_y = fields.shape
    edge_x = jax.ShapeDtypeStruct((layers, components, width_y), jnp.float32)
    edge_y = jax.ShapeDtypeStruct((layers, components, width_x), jnp.float32)
    combined, x0, x1, y0, y1 = pl.pallas_call(
        sweep_kernel,
        out_shape=(jax.ShapeDtypeStruct(fields.shape, jnp.float32), edge_x, edge_x, edge_y, edge_y),
    )(fields, rate_re, rate_im, enter_re, enter_im, below_re, below_im)
    from_low_x, from_high_x = edge_pair(x1, x0, "px")
    from_low_y, from_high_y = edge_pair(y1, y0, "py")
    return pl.pallas_call(
        stencil_kernel,
        out_shape=jax.ShapeDtypeStruct(fields.shape, jnp.float32),
    )(combined, from_low_x, from_high_x, from_low_y, from_high_y)


def last_sweep_kernel(flag_ref, f_ref, rr_ref, ri_ref, br_ref, bi_ref, ar_ref, ai_ref,
                      lr_ref, li_ref, hr_ref, hi_ref, got_ref, c_ref, sx_ref, sy_ref):
    layers = f_ref.shape[0]
    shots = br_ref.shape[0]
    lower = flag_ref[0] == 1
    first_x = flag_ref[1] == 0
    first_y = flag_ref[2] == 0
    components = c_ref.shape[1]
    width_x, width_y = c_ref.shape[2], c_ref.shape[3]
    lanes = lax.broadcasted_iota(jnp.int32, (width_x, width_y), 1)
    gathered = jnp.zeros((width_x, width_y), jnp.float32)
    for s in range(shots):
        p_re, p_im = got_ref[s], got_ref[shots + s]
        g_re, g_im = complex_times(lr_ref[...], li_ref[...], p_re, p_im)
        w_re = jnp.where(lower, br_ref[s], g_re + br_ref[s])
        w_im = jnp.where(lower, bi_ref[s], g_im + bi_ref[s])
        g_re, g_im = complex_times(hr_ref[...], hi_ref[...], p_re, p_im)
        v_re = jnp.where(lower, g_re + ar_ref[s], ar_ref[s])
        v_im = jnp.where(lower, g_im + ai_ref[s], ai_ref[s])
        downs = []
        for k in range(layers):
            t_re, t_im = complex_times(rr_ref[k], ri_ref[k], w_re, w_im)
            w_re, w_im = t_re + f_ref[k, 2 * s], t_im + f_ref[k, 2 * s + 1]
            downs.append((w_re, w_im))
        for k in range(layers - 1, -1, -1):
            t_re, t_im = complex_times(rr_ref[k], ri_ref[k], v_re, v_im)
            f_re, f_im = f_ref[k, 2 * s], f_ref[k, 2 * s + 1]
            v_re, v_im = t_re + f_re, t_im + f_im
            d_re, d_im = downs[k]
            for part, plane in ((0, d_re + v_re - f_re), (1, d_im + v_im - f_im)):
                c = 2 * s + part
                c_ref[k, c] = plane
                sx_ref[k, pl.ds(c, 1), :] = jnp.where(first_x, plane[-1:, :], plane[0:1, :])
                j = k * components + c
                last_col = pltpu.roll(plane, (j + 1) % width_y, 1)
                first_col = pltpu.roll(plane, j, 1) if j else plane
                gathered = jnp.where(lanes == j, jnp.where(first_y, last_col, first_col), gathered)
    flipped = jnp.transpose(gathered)
    for k in range(layers):
        for c in range(components):
            j = k * components + c
            sy_ref[k, pl.ds(c, 1), :] = flipped[j : j + 1, :]


def paired_stencil_kernel(flag_ref, c_ref, gx_ref, gy_ref, o_ref):
    layers, components, width_x, width_y = c_ref.shape
    rows = lax.broadcasted_iota(jnp.int32, (width_x, width_y), 0)
    cols = lax.broadcasted_iota(jnp.int32, (width_x, width_y), 1)
    side_rows = lax.broadcasted_iota(jnp.int32, (width_y, width_x), 0)
    first_x = flag_ref[1] == 0
    first_y = flag_ref[2] == 0
    for k in range(layers):
        for c in range(components):
            plane = c_ref[k, c]
            edge_x = gx_ref[k, pl.ds(c, 1), :]
            edge_y = jnp.broadcast_to(gy_ref[k, pl.ds(c, 1), :], (width_y, width_x))
            none_x = jnp.zeros_like(edge_x)
            low_x = jnp.broadcast_to(jnp.where(first_x, none_x, edge_x), (width_x, width_y))
            high_x = jnp.broadcast_to(jnp.where(first_x, edge_x, none_x), (width_x, width_y))
            side = jnp.where(side_rows == jnp.where(first_y, width_y - 1, 0), edge_y, 0.0)
            next_x = jnp.where(rows == width_x - 1, high_x, pltpu.roll(plane, width_x - 1, 0))
            prev_x = jnp.where(rows == 0, low_x, pltpu.roll(plane, 1, 0))
            next_y = jnp.where(cols == width_y - 1, 0.0, pltpu.roll(plane, width_y - 1, 1))
            prev_y = jnp.where(cols == 0, 0.0, pltpu.roll(plane, 1, 1))
            neighbours = next_x + prev_x + next_y + prev_y + jnp.transpose(side)
            o_ref[k, c] = plane - 0.2 * (4.0 * plane - neighbours)


def finish_paired(fields, rate_re, rate_im, before, after, got, below, above, lower):
    layers, components, width_x, width_y = fields.shape
    flags = jnp.stack(
        [lower.astype(jnp.int32), lax.axis_index("px"), lax.axis_index("py")]
    ).astype(jnp.int32)
    smem = pl.BlockSpec(memory_space=pltpu.SMEM)
    vmem = pl.BlockSpec(memory_space=pltpu.VMEM)
    edge_x = jax.ShapeDtypeStruct((layers, components, width_y), jnp.float32)
    edge_y = jax.ShapeDtypeStruct((layers, components, width_x), jnp.float32)
    combined, send_x, send_y = pl.pallas_call(
        last_sweep_kernel,
        in_specs=[smem] + [vmem] * 12,
        out_specs=(vmem, vmem, vmem),
        out_shape=(jax.ShapeDtypeStruct(fields.shape, jnp.float32), edge_x, edge_y),
    )(flags, fields, rate_re, rate_im, *before, *after, *below, *above, got)
    got_x = lax.ppermute(send_x, "px", [(0, 1), (1, 0)])
    got_y = lax.ppermute(send_y, "py", [(0, 1), (1, 0)])
    return pl.pallas_call(
        paired_stencil_kernel,
        in_specs=[smem, vmem, vmem, vmem],
        out_specs=vmem,
        out_shape=jax.ShapeDtypeStruct(fields.shape, jnp.float32),
    )(flags, combined, got_x, got_y)


def shards(source, phase, attenuation, pml_level, recv_values, recv_slab, recv_lateral, recv_layer):
    layers, components, width_x, width_y = source.shape
    shot_count = components // 2
    slab_count = lax.axis_size("slab")
    depth_total = layers * slab_count

    damping = attenuation + 0.5 / depth_total * pml_level.astype(jnp.float32)[None, :, :]
    amplitude = jnp.exp(-damping)
    rate_re = amplitude * jnp.cos(phase)
    rate_im = amplitude * jnp.sin(phase)

    prod_down = [(rate_re[0], rate_im[0])]
    for k in range(1, layers):
        prod_down.append(complex_times(rate_re[k], rate_im[k], *prod_down[-1]))
    levels = block_products(*prod_down[-1])

    forcing, levels = inject_receivers(
        source, recv_values, recv_slab, recv_lateral, recv_layer, levels
    )
    fields = forcing.reshape(layers, shot_count, 2, width_x, width_y)
    f_re = fields[:, :, 0]
    f_im = fields[:, :, 1]

    down = [None] * layers
    state = (f_re[0], f_im[0])
    down[0] = state
    for k in range(1, layers):
        t_re, t_im = complex_times(rate_re[k][None], rate_im[k][None], *state)
        state = (t_re + f_re[k], t_im + f_im[k])
        down[k] = state
    up = [None] * layers
    state = (f_re[layers - 1], f_im[layers - 1])
    up[layers - 1] = state
    for k in range(layers - 2, -1, -1):
        t_re, t_im = complex_times(rate_re[k][None], rate_im[k][None], *state)
        state = (t_re + f_re[k], t_im + f_im[k])
        up[k] = state

    if lax.axis_size("px") == 2 and lax.axis_size("py") == 2 and slab_count > 1:
        parts = entering_states(down[layers - 1], up[0], levels, defer_last=True)
        return finish_paired(forcing, rate_re, rate_im, *parts)
    (enter_re, enter_im), (below_re, below_im) = entering_states(down[layers - 1], up[0], levels)

    return finish(forcing, rate_re, rate_im, enter_re, enter_im, below_re, below_im)


def solution(mesh):
    in_specs = (
        P("slab", None, "px", "py"),
        P("slab", "px", "py"),
        P("slab", "px", "py"),
        P("px", "py"),
        P("px", "py", None, "slab"),
        P("px", "py", "slab", None),
        P("px", "py", "slab"),
        P("px", "py", "slab"),
    )
    out_specs = P("slab", None, "px", "py")
    return jax.shard_map(shards, mesh=mesh, in_specs=in_specs, out_specs=out_specs, check_vma=False)
```

```python
import jax
import jax.numpy as jnp
from jax import lax
from jax.sharding import PartitionSpec as P
from jax.experimental import pallas as pl
from jax.experimental.pallas import tpu as pltpu


def from_behind(array, axis, by):
    count = lax.axis_size(axis)
    pairs = [(i, i + by) for i in range(count) if 0 <= i + by < count]
    return lax.ppermute(array, axis, pairs)


def complex_times(a_re, a_im, b_re, b_im):
    return a_re * b_re - a_im * b_im, a_re * b_im + a_im * b_re


def inject_receivers(source, recv_values, recv_slab, recv_lateral, recv_layer, levels):
    layers, components, width_x, width_y = source.shape
    slab_count = lax.axis_size("slab")
    plane_size = width_x * width_y
    rows_here = recv_values.shape[3]
    capacity = rows_here // min(8, slab_count)
    values = recv_values[0, 0]
    target_slab = recv_slab[0, 0, :, 0]
    position = recv_layer[0, 0] * plane_size + recv_lateral[0, 0]
    order = jnp.arange(rows_here, dtype=jnp.int32)
    same_before = (target_slab[:, None] == target_slab[None, :]) & (order[None, :] < order[:, None])
    ranking = jnp.sum(same_before.astype(jnp.int32), axis=1)
    target_slot = target_slab * capacity + ranking
    rows = jnp.concatenate([values, position.astype(jnp.float32)[None, :]], axis=0)
    high = lax.reduce_precision(rows, exponent_bits=8, mantissa_bits=7)
    rest = rows - high
    middle = lax.reduce_precision(rest, exponent_bits=8, mantissa_bits=7)
    parts = jnp.stack([high, middle, rest - middle], axis=0).astype(jnp.bfloat16)
    spots = (
        target_slot[:, None] == jnp.arange(slab_count * capacity, dtype=jnp.int32)[None, :]
    ).astype(jnp.bfloat16)
    placed = jnp.dot(
        parts.reshape(3 * (components + 1), rows_here), spots, preferred_element_type=jnp.float32
    ).reshape(3, components + 1, slab_count * capacity)
    send_rows = (placed[0] + placed[1]) + placed[2]
    got_rows = lax.all_to_all(send_rows, "slab", split_axis=1, concat_axis=1, tiled=True)
    inject_values = got_rows[:components]
    inject_places = got_rows[components].astype(jnp.int32)
    row_of = inject_places // width_y
    col_of = inject_places % width_y
    pick_rows = (
        row_of[None, :] == jnp.arange(layers * width_x, dtype=jnp.int32)[:, None]
    ).astype(jnp.bfloat16)
    pick_cols = col_of[:, None] == jnp.arange(width_y, dtype=jnp.int32)[None, :]
    high = lax.reduce_precision(inject_values, exponent_bits=8, mantissa_bits=7)
    pieces = jnp.stack([high, inject_values - high], axis=0)
    spread = jnp.where(pick_cols[None, None, :, :], pieces[:, :, :, None], 0.0)
    spread = jnp.transpose(spread, (2, 0, 1, 3)).reshape(
        slab_count * capacity, 2 * components * width_y
    )
    added = jnp.dot(pick_rows, spread.astype(jnp.bfloat16), preferred_element_type=jnp.float32)
    added = added.reshape(layers * width_x, 2, components * width_y)
    added = added[:, 0] + added[:, 1]
    added = jnp.transpose(added.reshape(layers, width_x, components, width_y), (0, 2, 1, 3))
    return source + added, levels


def exchange(array, step):
    count = lax.axis_size("slab")
    return lax.ppermute(array, "slab", [(i, i ^ step) for i in range(count)])


def block_products(a_re, a_im):
    slab_count = lax.axis_size("slab")
    here = lax.axis_index("slab")
    one = jnp.ones_like(a_re)
    zero = jnp.zeros_like(a_re)
    total = (a_re, a_im)
    below = (one, zero)
    above = (one, zero)
    levels = []
    step = 1
    while 2 * step < slab_count:
        got = exchange(jnp.stack(total, axis=0), step)
        partner = (got[0], got[1])
        levels.append((total, partner, below, above))
        lower = (here & step) == 0
        grown_below = complex_times(*below, *partner)
        grown_above = complex_times(*above, *partner)
        below = (jnp.where(lower, below[0], grown_below[0]), jnp.where(lower, below[1], grown_below[1]))
        above = (jnp.where(lower, grown_above[0], above[0]), jnp.where(lower, grown_above[1], above[1]))
        total = complex_times(*total, *partner)
        step *= 2
    levels.append((None, None, below, above))
    return levels


def entering_states(down_b, up_b, levels, defer_last=False):
    slab_count = lax.axis_size("slab")
    here = lax.axis_index("slab")
    shots = down_b[0].shape[0]
    before = (jnp.zeros_like(down_b[0]), jnp.zeros_like(down_b[1]))
    after = (jnp.zeros_like(up_b[0]), jnp.zeros_like(up_b[1]))
    step = 1
    level = 0
    while step < slab_count:
        lower = (here & step) == 0
        total, partner, below, above = levels[level]
        if 2 * step < slab_count:
            got = exchange(jnp.concatenate([*down_b, *up_b], axis=0), step)
            pd = (got[:shots], got[shots : 2 * shots])
            pu = (got[2 * shots : 3 * shots], got[3 * shots :])
            t_re, t_im = total[0][None], total[1][None]
            q_re, q_im = partner[0][None], partner[1][None]
            first = (jnp.where(lower, q_re, t_re), jnp.where(lower, q_im, t_im))
            inner = (jnp.where(lower, down_b[0], pd[0]), jnp.where(lower, down_b[1], pd[1]))
            outer = (jnp.where(lower, pd[0], down_b[0]), jnp.where(lower, pd[1], down_b[1]))
            m_re, m_im = complex_times(*first, *inner)
            new_down = (m_re + outer[0], m_im + outer[1])
            first = (jnp.where(lower, t_re, q_re), jnp.where(lower, t_im, q_im))
            inner = (jnp.where(lower, pu[0], up_b[0]), jnp.where(lower, pu[1], up_b[1]))
            outer = (jnp.where(lower, up_b[0], pu[0]), jnp.where(lower, up_b[1], pu[1]))
            m_re, m_im = complex_times(*first, *inner)
            new_up = (m_re + outer[0], m_im + outer[1])
        else:
            send = jnp.concatenate(
                [jnp.where(lower, down_b[0], up_b[0]), jnp.where(lower, down_b[1], up_b[1])], axis=0
            )
            got = exchange(send, step)
            if defer_last:
                return before, after, got, below, above, lower
            pd = (got[:shots], got[shots:])
            pu = pd
        g_re, g_im = complex_times(below[0][None], below[1][None], *pd)
        before = (
            jnp.where(lower, before[0], g_re + before[0]),
            jnp.where(lower, before[1], g_im + before[1]),
        )
        g_re, g_im = complex_times(above[0][None], above[1][None], *pu)
        after = (
            jnp.where(lower, g_re + after[0], after[0]),
            jnp.where(lower, g_im + after[1], after[1]),
        )
        if 2 * step < slab_count:
            down_b, up_b = new_down, new_up
        step *= 2
        level += 1
    if defer_last:
        return before, after, None, None, None, None
    return before, after


def edge_pair(last, first, axis):
    count = lax.axis_size(axis)
    if count == 2:
        here = lax.axis_index(axis)
        got = lax.ppermute(jnp.where(here == 0, last, first), axis, [(0, 1), (1, 0)])
        zero = jnp.zeros_like(got)
        return jnp.where(here == 1, got, zero), jnp.where(here == 0, got, zero)
    return from_behind(last, axis, 1), from_behind(first, axis, -1)


def sweep_kernel(f_ref, rr_ref, ri_ref, er_ref, ei_ref, br_ref, bi_ref,
                 c_ref, x0_ref, x1_ref, y0_ref, y1_ref):
    layers = f_ref.shape[0]
    shots = er_ref.shape[0]
    downs = []
    for s in range(shots):
        w_re, w_im = er_ref[s], ei_ref[s]
        per_layer = []
        for k in range(layers):
            t_re, t_im = complex_times(rr_ref[k], ri_ref[k], w_re, w_im)
            w_re, w_im = t_re + f_ref[k, 2 * s], t_im + f_ref[k, 2 * s + 1]
            per_layer.append((w_re, w_im))
        downs.append(per_layer)
    for s in range(shots):
        v_re, v_im = br_ref[s], bi_ref[s]
        for k in range(layers - 1, -1, -1):
            t_re, t_im = complex_times(rr_ref[k], ri_ref[k], v_re, v_im)
            f_re, f_im = f_ref[k, 2 * s], f_ref[k, 2 * s + 1]
            v_re, v_im = t_re + f_re, t_im + f_im
            d_re, d_im = downs[s][k]
            for part, plane in ((0, d_re + v_re - f_re), (1, d_im + v_im - f_im)):
                c = 2 * s + part
                c_ref[k, c] = plane
                x0_ref[k, pl.ds(c, 1), :] = plane[0:1, :]
                x1_ref[k, pl.ds(c, 1), :] = plane[-1:, :]
                flipped = jnp.transpose(plane)
                y0_ref[k, pl.ds(c, 1), :] = flipped[0:1, :]
                y1_ref[k, pl.ds(c, 1), :] = flipped[-1:, :]


def stencil_kernel(c_ref, lx_ref, hx_ref, ly_ref, hy_ref, o_ref):
    layers, components, width_x, width_y = c_ref.shape
    rows = lax.broadcasted_iota(jnp.int32, (width_x, width_y), 0)
    cols = lax.broadcasted_iota(jnp.int32, (width_x, width_y), 1)
    for k in range(layers):
        for c in range(components):
            plane = c_ref[k, c]
            low_x = jnp.broadcast_to(lx_ref[k, pl.ds(c, 1), :], (width_x, width_y))
            high_x = jnp.broadcast_to(hx_ref[k, pl.ds(c, 1), :], (width_x, width_y))
            low_y = jnp.transpose(jnp.broadcast_to(ly_ref[k, pl.ds(c, 1), :], (width_y, width_x)))
            high_y = jnp.transpose(jnp.broadcast_to(hy_ref[k, pl.ds(c, 1), :], (width_y, width_x)))
            next_x = jnp.where(rows == width_x - 1, high_x, pltpu.roll(plane, width_x - 1, 0))
            prev_x = jnp.where(rows == 0, low_x, pltpu.roll(plane, 1, 0))
            next_y = jnp.where(cols == width_y - 1, high_y, pltpu.roll(plane, width_y - 1, 1))
            prev_y = jnp.where(cols == 0, low_y, pltpu.roll(plane, 1, 1))
            neighbours = next_x + prev_x + next_y + prev_y
            o_ref[k, c] = plane - 0.2 * (4.0 * plane - neighbours)


def finish(fields, rate_re, rate_im, enter_re, enter_im, below_re, below_im):
    layers, components, width_x, width_y = fields.shape
    edge_x = jax.ShapeDtypeStruct((layers, components, width_y), jnp.float32)
    edge_y = jax.ShapeDtypeStruct((layers, components, width_x), jnp.float32)
    combined, x0, x1, y0, y1 = pl.pallas_call(
        sweep_kernel,
        out_shape=(jax.ShapeDtypeStruct(fields.shape, jnp.float32), edge_x, edge_x, edge_y, edge_y),
    )(fields, rate_re, rate_im, enter_re, enter_im, below_re, below_im)
    from_low_x, from_high_x = edge_pair(x1, x0, "px")
    from_low_y, from_high_y = edge_pair(y1, y0, "py")
    return pl.pallas_call(
        stencil_kernel,
        out_shape=jax.ShapeDtypeStruct(fields.shape, jnp.float32),
    )(combined, from_low_x, from_high_x, from_low_y, from_high_y)


def last_sweep_kernel(flag_ref, f_ref, rr_ref, ri_ref, br_ref, bi_ref, ar_ref, ai_ref,
                      lr_ref, li_ref, hr_ref, hi_ref, got_ref, c_ref, sx_ref, sy_ref):
    layers = f_ref.shape[0]
    shots = br_ref.shape[0]
    lower = flag_ref[0] == 1
    first_x = flag_ref[1] == 0
    first_y = flag_ref[2] == 0
    components = c_ref.shape[1]
    width_x, width_y = c_ref.shape[2], c_ref.shape[3]
    lanes = lax.broadcasted_iota(jnp.int32, (width_x, width_y), 1)
    gathered = jnp.zeros((width_x, width_y), jnp.float32)
    for s in range(shots):
        p_re, p_im = got_ref[s], got_ref[shots + s]
        g_re, g_im = complex_times(lr_ref[...], li_ref[...], p_re, p_im)
        w_re = jnp.where(lower, br_ref[s], g_re + br_ref[s])
        w_im = jnp.where(lower, bi_ref[s], g_im + bi_ref[s])
        g_re, g_im = complex_times(hr_ref[...], hi_ref[...], p_re, p_im)
        v_re = jnp.where(lower, g_re + ar_ref[s], ar_ref[s])
        v_im = jnp.where(lower, g_im + ai_ref[s], ai_ref[s])
        downs = []
        for k in range(layers):
            t_re, t_im = complex_times(rr_ref[k], ri_ref[k], w_re, w_im)
            w_re, w_im = t_re + f_ref[k, 2 * s], t_im + f_ref[k, 2 * s + 1]
            downs.append((w_re, w_im))
        for k in range(layers - 1, -1, -1):
            t_re, t_im = complex_times(rr_ref[k], ri_ref[k], v_re, v_im)
            f_re, f_im = f_ref[k, 2 * s], f_ref[k, 2 * s + 1]
            v_re, v_im = t_re + f_re, t_im + f_im
            d_re, d_im = downs[k]
            for part, plane in ((0, d_re + v_re - f_re), (1, d_im + v_im - f_im)):
                c = 2 * s + part
                c_ref[k, c] = plane
                sx_ref[k, pl.ds(c, 1), :] = jnp.where(first_x, plane[-1:, :], plane[0:1, :])
                j = k * components + c
                last_col = pltpu.roll(plane, (j + 1) % width_y, 1)
                first_col = pltpu.roll(plane, j, 1) if j else plane
                gathered = jnp.where(lanes == j, jnp.where(first_y, last_col, first_col), gathered)
    flipped = jnp.transpose(gathered)
    for k in range(layers):
        for c in range(components):
            j = k * components + c
            sy_ref[k, pl.ds(c, 1), :] = flipped[j : j + 1, :]


def paired_stencil_kernel(flag_ref, c_ref, gx_ref, gy_ref, o_ref, pack_ref):
    layers, components, width_x, width_y = c_ref.shape
    rows = lax.broadcasted_iota(jnp.int32, (width_x, width_y), 0)
    cols = lax.broadcasted_iota(jnp.int32, (width_x, width_y), 1)
    first_x = flag_ref[1] == 0
    first_y = flag_ref[2] == 0
    pack_ref[...] = jnp.zeros_like(pack_ref)
    for k in range(layers):
        pack_ref[pl.ds(k * components, components), :] = gy_ref[k]
    columns = jnp.transpose(pack_ref[...])
    for k in range(layers):
        for c in range(components):
            j = k * components + c
            plane = c_ref[k, c]
            edge_x = gx_ref[k, pl.ds(c, 1), :]
            none_x = jnp.zeros_like(edge_x)
            low_x = jnp.broadcast_to(jnp.where(first_x, none_x, edge_x), (width_x, width_y))
            high_x = jnp.broadcast_to(jnp.where(first_x, edge_x, none_x), (width_x, width_y))
            edge_y = jnp.broadcast_to(columns[:, j : j + 1], (width_x, width_y))
            side = jnp.where(cols == jnp.where(first_y, width_y - 1, 0), edge_y, 0.0)
            next_x = jnp.where(rows == width_x - 1, high_x, pltpu.roll(plane, width_x - 1, 0))
            prev_x = jnp.where(rows == 0, low_x, pltpu.roll(plane, 1, 0))
            next_y = jnp.where(cols == width_y - 1, 0.0, pltpu.roll(plane, width_y - 1, 1))
            prev_y = jnp.where(cols == 0, 0.0, pltpu.roll(plane, 1, 1))
            neighbours = next_x + prev_x + next_y + prev_y + side
            o_ref[k, c] = plane - 0.2 * (4.0 * plane - neighbours)


def finish_paired(fields, rate_re, rate_im, before, after, got, below, above, lower):
    layers, components, width_x, width_y = fields.shape
    flags = jnp.stack(
        [lower.astype(jnp.int32), lax.axis_index("px"), lax.axis_index("py")]
    ).astype(jnp.int32)
    smem = pl.BlockSpec(memory_space=pltpu.SMEM)
    vmem = pl.BlockSpec(memory_space=pltpu.VMEM)
    edge_x = jax.ShapeDtypeStruct((layers, components, width_y), jnp.float32)
    edge_y = jax.ShapeDtypeStruct((layers, components, width_x), jnp.float32)
    combined, send_x, send_y = pl.pallas_call(
        last_sweep_kernel,
        in_specs=[smem] + [vmem] * 12,
        out_specs=(vmem, vmem, vmem),
        out_shape=(jax.ShapeDtypeStruct(fields.shape, jnp.float32), edge_x, edge_y),
    )(flags, fields, rate_re, rate_im, *before, *after, *below, *above, got)
    got_x = lax.ppermute(send_x, "px", [(0, 1), (1, 0)])
    got_y = lax.ppermute(send_y, "py", [(0, 1), (1, 0)])
    return pl.pallas_call(
        paired_stencil_kernel,
        in_specs=[smem, vmem, vmem, vmem],
        out_specs=vmem,
        out_shape=jax.ShapeDtypeStruct(fields.shape, jnp.float32),
        scratch_shapes=[pltpu.VMEM((width_y, width_x), jnp.float32)],
    )(flags, combined, got_x, got_y)


def shards(source, phase, attenuation, pml_level, recv_values, recv_slab, recv_lateral, recv_layer):
    layers, components, width_x, width_y = source.shape
    shot_count = components // 2
    slab_count = lax.axis_size("slab")
    depth_total = layers * slab_count

    damping = attenuation + 0.5 / depth_total * pml_level.astype(jnp.float32)[None, :, :]
    amplitude = jnp.exp(-damping)
    rate_re = amplitude * jnp.cos(phase)
    rate_im = amplitude * jnp.sin(phase)

    prod_down = [(rate_re[0], rate_im[0])]
    for k in range(1, layers):
        prod_down.append(complex_times(rate_re[k], rate_im[k], *prod_down[-1]))
    levels = block_products(*prod_down[-1])

    forcing, levels = inject_receivers(
        source, recv_values, recv_slab, recv_lateral, recv_layer, levels
    )
    fields = forcing.reshape(layers, shot_count, 2, width_x, width_y)
    f_re = fields[:, :, 0]
    f_im = fields[:, :, 1]

    down = [None] * layers
    state = (f_re[0], f_im[0])
    down[0] = state
    for k in range(1, layers):
        t_re, t_im = complex_times(rate_re[k][None], rate_im[k][None], *state)
        state = (t_re + f_re[k], t_im + f_im[k])
        down[k] = state
    up = [None] * layers
    state = (f_re[layers - 1], f_im[layers - 1])
    up[layers - 1] = state
    for k in range(layers - 2, -1, -1):
        t_re, t_im = complex_times(rate_re[k][None], rate_im[k][None], *state)
        state = (t_re + f_re[k], t_im + f_im[k])
        up[k] = state

    if lax.axis_size("px") == 2 and lax.axis_size("py") == 2 and slab_count > 1:
        parts = entering_states(down[layers - 1], up[0], levels, defer_last=True)
        return finish_paired(forcing, rate_re, rate_im, *parts)
    (enter_re, enter_im), (below_re, below_im) = entering_states(down[layers - 1], up[0], levels)

    return finish(forcing, rate_re, rate_im, enter_re, enter_im, below_re, below_im)


def solution(mesh):
    in_specs = (
        P("slab", None, "px", "py"),
        P("slab", "px", "py"),
        P("slab", "px", "py"),
        P("px", "py"),
        P("px", "py", None, "slab"),
        P("px", "py", "slab", None),
        P("px", "py", "slab"),
        P("px", "py", "slab"),
    )
    out_specs = P("slab", None, "px", "py")
    return jax.shard_map(shards, mesh=mesh, in_specs=in_specs, out_specs=out_specs, check_vma=False)
```

```python
import jax
import jax.numpy as jnp
from jax import lax
from jax.sharding import PartitionSpec as P
from jax.experimental import pallas as pl
from jax.experimental.pallas import tpu as pltpu


def from_behind(array, axis, by):
    count = lax.axis_size(axis)
    pairs = [(i, i + by) for i in range(count) if 0 <= i + by < count]
    return lax.ppermute(array, axis, pairs)


def complex_times(a_re, a_im, b_re, b_im):
    return a_re * b_re - a_im * b_im, a_re * b_im + a_im * b_re


def inject_receivers(source, recv_values, recv_slab, recv_lateral, recv_layer, levels):
    layers, components, width_x, width_y = source.shape
    slab_count = lax.axis_size("slab")
    plane_size = width_x * width_y
    rows_here = recv_values.shape[3]
    capacity = rows_here // min(8, slab_count)
    values = recv_values[0, 0]
    target_slab = recv_slab[0, 0, :, 0]
    position = recv_layer[0, 0] * plane_size + recv_lateral[0, 0]
    order = jnp.arange(rows_here, dtype=jnp.int32)
    same_before = (target_slab[:, None] == target_slab[None, :]) & (order[None, :] < order[:, None])
    ranking = jnp.sum(same_before.astype(jnp.int32), axis=1)
    target_slot = target_slab * capacity + ranking
    rows = jnp.concatenate([values, position.astype(jnp.float32)[None, :]], axis=0)
    high = lax.reduce_precision(rows, exponent_bits=8, mantissa_bits=7)
    rest = rows - high
    middle = lax.reduce_precision(rest, exponent_bits=8, mantissa_bits=7)
    parts = jnp.stack([high, middle, rest - middle], axis=0).astype(jnp.bfloat16)
    spots = (
        target_slot[:, None] == jnp.arange(slab_count * capacity, dtype=jnp.int32)[None, :]
    ).astype(jnp.bfloat16)
    placed = jnp.dot(
        parts.reshape(3 * (components + 1), rows_here), spots, preferred_element_type=jnp.float32
    ).reshape(3, components + 1, slab_count * capacity)
    send_rows = (placed[0] + placed[1]) + placed[2]
    got_rows = lax.all_to_all(send_rows, "slab", split_axis=1, concat_axis=1, tiled=True)
    inject_values = got_rows[:components]
    inject_places = got_rows[components].astype(jnp.int32)
    row_of = inject_places // width_y
    col_of = inject_places % width_y
    pick_rows = (
        row_of[None, :] == jnp.arange(layers * width_x, dtype=jnp.int32)[:, None]
    ).astype(jnp.bfloat16)
    pick_cols = col_of[:, None] == jnp.arange(width_y, dtype=jnp.int32)[None, :]
    high = lax.reduce_precision(inject_values, exponent_bits=8, mantissa_bits=7)
    pieces = jnp.stack([high, inject_values - high], axis=0)
    spread = jnp.where(pick_cols[None, None, :, :], pieces[:, :, :, None], 0.0)
    spread = jnp.transpose(spread, (2, 0, 1, 3)).reshape(
        slab_count * capacity, 2 * components * width_y
    )
    added = jnp.dot(pick_rows, spread.astype(jnp.bfloat16), preferred_element_type=jnp.float32)
    added = added.reshape(layers * width_x, 2, components * width_y)
    added = added[:, 0] + added[:, 1]
    added = jnp.transpose(added.reshape(layers, width_x, components, width_y), (0, 2, 1, 3))
    return source + added, levels, added


def exchange(array, step):
    count = lax.axis_size("slab")
    return lax.ppermute(array, "slab", [(i, i ^ step) for i in range(count)])


def block_products(a_re, a_im):
    slab_count = lax.axis_size("slab")
    here = lax.axis_index("slab")
    one = jnp.ones_like(a_re)
    zero = jnp.zeros_like(a_re)
    total = (a_re, a_im)
    below = (one, zero)
    above = (one, zero)
    levels = []
    step = 1
    while 2 * step < slab_count:
        got = exchange(jnp.stack(total, axis=0), step)
        partner = (got[0], got[1])
        levels.append((total, partner, below, above))
        lower = (here & step) == 0
        grown_below = complex_times(*below, *partner)
        grown_above = complex_times(*above, *partner)
        below = (jnp.where(lower, below[0], grown_below[0]), jnp.where(lower, below[1], grown_below[1]))
        above = (jnp.where(lower, grown_above[0], above[0]), jnp.where(lower, grown_above[1], above[1]))
        total = complex_times(*total, *partner)
        step *= 2
    levels.append((None, None, below, above))
    return levels


def entering_states(down_b, up_b, levels, defer_last=False):
    slab_count = lax.axis_size("slab")
    here = lax.axis_index("slab")
    shots = down_b[0].shape[0]
    before = (jnp.zeros_like(down_b[0]), jnp.zeros_like(down_b[1]))
    after = (jnp.zeros_like(up_b[0]), jnp.zeros_like(up_b[1]))
    step = 1
    level = 0
    while step < slab_count:
        lower = (here & step) == 0
        total, partner, below, above = levels[level]
        if 2 * step < slab_count:
            got = exchange(jnp.concatenate([*down_b, *up_b], axis=0), step)
            pd = (got[:shots], got[shots : 2 * shots])
            pu = (got[2 * shots : 3 * shots], got[3 * shots :])
            t_re, t_im = total[0][None], total[1][None]
            q_re, q_im = partner[0][None], partner[1][None]
            first = (jnp.where(lower, q_re, t_re), jnp.where(lower, q_im, t_im))
            inner = (jnp.where(lower, down_b[0], pd[0]), jnp.where(lower, down_b[1], pd[1]))
            outer = (jnp.where(lower, pd[0], down_b[0]), jnp.where(lower, pd[1], down_b[1]))
            m_re, m_im = complex_times(*first, *inner)
            new_down = (m_re + outer[0], m_im + outer[1])
            first = (jnp.where(lower, t_re, q_re), jnp.where(lower, t_im, q_im))
            inner = (jnp.where(lower, pu[0], up_b[0]), jnp.where(lower, pu[1], up_b[1]))
            outer = (jnp.where(lower, up_b[0], pu[0]), jnp.where(lower, up_b[1], pu[1]))
            m_re, m_im = complex_times(*first, *inner)
            new_up = (m_re + outer[0], m_im + outer[1])
        else:
            send = jnp.concatenate(
                [jnp.where(lower, down_b[0], up_b[0]), jnp.where(lower, down_b[1], up_b[1])], axis=0
            )
            got = exchange(send, step)
            if defer_last:
                return before, after, got, below, above, lower
            pd = (got[:shots], got[shots:])
            pu = pd
        g_re, g_im = complex_times(below[0][None], below[1][None], *pd)
        before = (
            jnp.where(lower, before[0], g_re + before[0]),
            jnp.where(lower, before[1], g_im + before[1]),
        )
        g_re, g_im = complex_times(above[0][None], above[1][None], *pu)
        after = (
            jnp.where(lower, g_re + after[0], after[0]),
            jnp.where(lower, g_im + after[1], after[1]),
        )
        if 2 * step < slab_count:
            down_b, up_b = new_down, new_up
        step *= 2
        level += 1
    if defer_last:
        return before, after, None, None, None, None
    return before, after


def edge_pair(last, first, axis):
    count = lax.axis_size(axis)
    if count == 2:
        here = lax.axis_index(axis)
        got = lax.ppermute(jnp.where(here == 0, last, first), axis, [(0, 1), (1, 0)])
        zero = jnp.zeros_like(got)
        return jnp.where(here == 1, got, zero), jnp.where(here == 0, got, zero)
    return from_behind(last, axis, 1), from_behind(first, axis, -1)


def sweep_kernel(f_ref, rr_ref, ri_ref, er_ref, ei_ref, br_ref, bi_ref,
                 c_ref, x0_ref, x1_ref, y0_ref, y1_ref):
    layers = f_ref.shape[0]
    shots = er_ref.shape[0]
    downs = []
    for s in range(shots):
        w_re, w_im = er_ref[s], ei_ref[s]
        per_layer = []
        for k in range(layers):
            t_re, t_im = complex_times(rr_ref[k], ri_ref[k], w_re, w_im)
            w_re, w_im = t_re + f_ref[k, 2 * s], t_im + f_ref[k, 2 * s + 1]
            per_layer.append((w_re, w_im))
        downs.append(per_layer)
    for s in range(shots):
        v_re, v_im = br_ref[s], bi_ref[s]
        for k in range(layers - 1, -1, -1):
            t_re, t_im = complex_times(rr_ref[k], ri_ref[k], v_re, v_im)
            f_re, f_im = f_ref[k, 2 * s], f_ref[k, 2 * s + 1]
            v_re, v_im = t_re + f_re, t_im + f_im
            d_re, d_im = downs[s][k]
            for part, plane in ((0, d_re + v_re - f_re), (1, d_im + v_im - f_im)):
                c = 2 * s + part
                c_ref[k, c] = plane
                x0_ref[k, pl.ds(c, 1), :] = plane[0:1, :]
                x1_ref[k, pl.ds(c, 1), :] = plane[-1:, :]
                flipped = jnp.transpose(plane)
                y0_ref[k, pl.ds(c, 1), :] = flipped[0:1, :]
                y1_ref[k, pl.ds(c, 1), :] = flipped[-1:, :]


def stencil_kernel(c_ref, lx_ref, hx_ref, ly_ref, hy_ref, o_ref):
    layers, components, width_x, width_y = c_ref.shape
    rows = lax.broadcasted_iota(jnp.int32, (width_x, width_y), 0)
    cols = lax.broadcasted_iota(jnp.int32, (width_x, width_y), 1)
    for k in range(layers):
        for c in range(components):
            plane = c_ref[k, c]
            low_x = jnp.broadcast_to(lx_ref[k, pl.ds(c, 1), :], (width_x, width_y))
            high_x = jnp.broadcast_to(hx_ref[k, pl.ds(c, 1), :], (width_x, width_y))
            low_y = jnp.transpose(jnp.broadcast_to(ly_ref[k, pl.ds(c, 1), :], (width_y, width_x)))
            high_y = jnp.transpose(jnp.broadcast_to(hy_ref[k, pl.ds(c, 1), :], (width_y, width_x)))
            next_x = jnp.where(rows == width_x - 1, high_x, pltpu.roll(plane, width_x - 1, 0))
            prev_x = jnp.where(rows == 0, low_x, pltpu.roll(plane, 1, 0))
            next_y = jnp.where(cols == width_y - 1, high_y, pltpu.roll(plane, width_y - 1, 1))
            prev_y = jnp.where(cols == 0, low_y, pltpu.roll(plane, 1, 1))
            neighbours = next_x + prev_x + next_y + prev_y
            o_ref[k, c] = plane - 0.2 * (4.0 * plane - neighbours)


def finish(fields, rate_re, rate_im, enter_re, enter_im, below_re, below_im):
    layers, components, width_x, width_y = fields.shape
    edge_x = jax.ShapeDtypeStruct((layers, components, width_y), jnp.float32)
    edge_y = jax.ShapeDtypeStruct((layers, components, width_x), jnp.float32)
    combined, x0, x1, y0, y1 = pl.pallas_call(
        sweep_kernel,
        out_shape=(jax.ShapeDtypeStruct(fields.shape, jnp.float32), edge_x, edge_x, edge_y, edge_y),
    )(fields, rate_re, rate_im, enter_re, enter_im, below_re, below_im)
    from_low_x, from_high_x = edge_pair(x1, x0, "px")
    from_low_y, from_high_y = edge_pair(y1, y0, "py")
    return pl.pallas_call(
        stencil_kernel,
        out_shape=jax.ShapeDtypeStruct(fields.shape, jnp.float32),
    )(combined, from_low_x, from_high_x, from_low_y, from_high_y)


def last_sweep_kernel(flag_ref, f_ref, rr_ref, ri_ref, br_ref, bi_ref, ar_ref, ai_ref,
                      lr_ref, li_ref, hr_ref, hi_ref, got_ref, c_ref, sx_ref, sy_ref):
    layers = f_ref.shape[0]
    shots = br_ref.shape[0]
    lower = flag_ref[0] == 1
    first_x = flag_ref[1] == 0
    first_y = flag_ref[2] == 0
    components = c_ref.shape[1]
    width_x, width_y = c_ref.shape[2], c_ref.shape[3]
    lanes = lax.broadcasted_iota(jnp.int32, (width_x, width_y), 1)
    gathered = jnp.zeros((width_x, width_y), jnp.float32)
    for s in range(shots):
        p_re, p_im = got_ref[s], got_ref[shots + s]
        g_re, g_im = complex_times(lr_ref[...], li_ref[...], p_re, p_im)
        w_re = jnp.where(lower, br_ref[s], g_re + br_ref[s])
        w_im = jnp.where(lower, bi_ref[s], g_im + bi_ref[s])
        g_re, g_im = complex_times(hr_ref[...], hi_ref[...], p_re, p_im)
        v_re = jnp.where(lower, g_re + ar_ref[s], ar_ref[s])
        v_im = jnp.where(lower, g_im + ai_ref[s], ai_ref[s])
        downs = []
        for k in range(layers):
            t_re, t_im = complex_times(rr_ref[k], ri_ref[k], w_re, w_im)
            w_re, w_im = t_re + f_ref[k, 2 * s], t_im + f_ref[k, 2 * s + 1]
            downs.append((w_re, w_im))
        for k in range(layers - 1, -1, -1):
            t_re, t_im = complex_times(rr_ref[k], ri_ref[k], v_re, v_im)
            f_re, f_im = f_ref[k, 2 * s], f_ref[k, 2 * s + 1]
            v_re, v_im = t_re + f_re, t_im + f_im
            d_re, d_im = downs[k]
            for part, plane in ((0, d_re + v_re - f_re), (1, d_im + v_im - f_im)):
                c = 2 * s + part
                c_ref[k, c] = plane
                sx_ref[k, pl.ds(c, 1), :] = jnp.where(first_x, plane[-1:, :], plane[0:1, :])
                j = k * components + c
                last_col = pltpu.roll(plane, (j + 1) % width_y, 1)
                first_col = pltpu.roll(plane, j, 1) if j else plane
                gathered = jnp.where(lanes == j, jnp.where(first_y, last_col, first_col), gathered)
    flipped = jnp.transpose(gathered)
    for k in range(layers):
        for c in range(components):
            j = k * components + c
            sy_ref[k, pl.ds(c, 1), :] = flipped[j : j + 1, :]


def paired_stencil_kernel(flag_ref, c_ref, gx_ref, gy_ref, o_ref, pack_ref):
    layers, components, width_x, width_y = c_ref.shape
    rows = lax.broadcasted_iota(jnp.int32, (width_x, width_y), 0)
    cols = lax.broadcasted_iota(jnp.int32, (width_x, width_y), 1)
    first_x = flag_ref[1] == 0
    first_y = flag_ref[2] == 0
    pack_ref[...] = jnp.zeros_like(pack_ref)
    for k in range(layers):
        pack_ref[pl.ds(k * components, components), :] = gy_ref[k]
    columns = jnp.transpose(pack_ref[...])
    for k in range(layers):
        for c in range(components):
            j = k * components + c
            plane = c_ref[k, c]
            edge_x = gx_ref[k, pl.ds(c, 1), :]
            none_x = jnp.zeros_like(edge_x)
            low_x = jnp.broadcast_to(jnp.where(first_x, none_x, edge_x), (width_x, width_y))
            high_x = jnp.broadcast_to(jnp.where(first_x, edge_x, none_x), (width_x, width_y))
            edge_y = jnp.broadcast_to(columns[:, j : j + 1], (width_x, width_y))
            side = jnp.where(cols == jnp.where(first_y, width_y - 1, 0), edge_y, 0.0)
            next_x = jnp.where(rows == width_x - 1, high_x, pltpu.roll(plane, width_x - 1, 0))
            prev_x = jnp.where(rows == 0, low_x, pltpu.roll(plane, 1, 0))
            next_y = jnp.where(cols == width_y - 1, 0.0, pltpu.roll(plane, width_y - 1, 1))
            prev_y = jnp.where(cols == 0, 0.0, pltpu.roll(plane, 1, 1))
            neighbours = next_x + prev_x + next_y + prev_y + side
            o_ref[k, c] = plane - 0.2 * (4.0 * plane - neighbours)


def finish_paired(fields, rate_re, rate_im, before, after, got, below, above, lower):
    layers, components, width_x, width_y = fields.shape
    flags = jnp.stack(
        [lower.astype(jnp.int32), lax.axis_index("px"), lax.axis_index("py")]
    ).astype(jnp.int32)
    smem = pl.BlockSpec(memory_space=pltpu.SMEM)
    vmem = pl.BlockSpec(memory_space=pltpu.VMEM)
    edge_x = jax.ShapeDtypeStruct((layers, components, width_y), jnp.float32)
    edge_y = jax.ShapeDtypeStruct((layers, components, width_x), jnp.float32)
    combined, send_x, send_y = pl.pallas_call(
        last_sweep_kernel,
        in_specs=[smem] + [vmem] * 12,
        out_specs=(vmem, vmem, vmem),
        out_shape=(jax.ShapeDtypeStruct(fields.shape, jnp.float32), edge_x, edge_y),
    )(flags, fields, rate_re, rate_im, *before, *after, *below, *above, got)
    got_x = lax.ppermute(send_x, "px", [(0, 1), (1, 0)])
    got_y = lax.ppermute(send_y, "py", [(0, 1), (1, 0)])
    return pl.pallas_call(
        paired_stencil_kernel,
        in_specs=[smem, vmem, vmem, vmem],
        out_specs=vmem,
        out_shape=jax.ShapeDtypeStruct(fields.shape, jnp.float32),
        scratch_shapes=[pltpu.VMEM((width_y, width_x), jnp.float32)],
    )(flags, combined, got_x, got_y)


def shards(source, phase, attenuation, pml_level, recv_values, recv_slab, recv_lateral, recv_layer):
    layers, components, width_x, width_y = source.shape
    shot_count = components // 2
    slab_count = lax.axis_size("slab")
    depth_total = layers * slab_count

    damping = attenuation + 0.5 / depth_total * pml_level.astype(jnp.float32)[None, :, :]
    amplitude = jnp.exp(-damping)
    rate_re = amplitude * jnp.cos(phase)
    rate_im = amplitude * jnp.sin(phase)

    prod_down = [(rate_re[0], rate_im[0])]
    for k in range(1, layers):
        prod_down.append(complex_times(rate_re[k], rate_im[k], *prod_down[-1]))
    levels = block_products(*prod_down[-1])

    forcing, levels, added = inject_receivers(
        source, recv_values, recv_slab, recv_lateral, recv_layer, levels
    )
    fields = forcing.reshape(layers, shot_count, 2, width_x, width_y)
    f_re = fields[:, :, 0]
    f_im = fields[:, :, 1]

    def local_ends(planes):
        p = planes.reshape(layers, shot_count, 2, width_x, width_y)
        p_re, p_im = p[:, :, 0], p[:, :, 1]
        state = (p_re[0], p_im[0])
        for k in range(1, layers):
            t_re, t_im = complex_times(rate_re[k][None], rate_im[k][None], *state)
            state = (t_re + p_re[k], t_im + p_im[k])
        last_down = state
        state = (p_re[layers - 1], p_im[layers - 1])
        for k in range(layers - 2, -1, -1):
            t_re, t_im = complex_times(rate_re[k][None], rate_im[k][None], *state)
            state = (t_re + p_re[k], t_im + p_im[k])
        return last_down, state

    src_down, src_up = local_ends(source)
    add_down, add_up = local_ends(added)
    down = [None] * layers
    up = [None] * layers
    down[layers - 1] = (src_down[0] + add_down[0], src_down[1] + add_down[1])
    up[0] = (src_up[0] + add_up[0], src_up[1] + add_up[1])

    if lax.axis_size("px") == 2 and lax.axis_size("py") == 2 and slab_count > 1:
        parts = entering_states(down[layers - 1], up[0], levels, defer_last=True)
        return finish_paired(forcing, rate_re, rate_im, *parts)
    (enter_re, enter_im), (below_re, below_im) = entering_states(down[layers - 1], up[0], levels)

    return finish(forcing, rate_re, rate_im, enter_re, enter_im, below_re, below_im)


def solution(mesh):
    in_specs = (
        P("slab", None, "px", "py"),
        P("slab", "px", "py"),
        P("slab", "px", "py"),
        P("px", "py"),
        P("px", "py", None, "slab"),
        P("px", "py", "slab", None),
        P("px", "py", "slab"),
        P("px", "py", "slab"),
    )
    out_specs = P("slab", None, "px", "py")
    return jax.shard_map(shards, mesh=mesh, in_specs=in_specs, out_specs=out_specs, check_vma=False)
```
